32 devices in a mesh: dp: 2 (over core), row: 4 (over y, x), col: 4 (over z).
Axes of the slice: x: 2, y: 2, z: 4, core: 2. Of those that a mesh axis runs over, the one named last changes fastest.
Arguments:
- hidden_in: bfloat16 [2, 8, 1024, 2048], P(None, ('dp', 'col'), None, 'row'), may hold values from -60 to 60
- segment_ids: int32 [2, 8, 1024], P(None, ('dp', 'row')), may hold values from 0 to 3, never falling along the last dimension, each value on 1 to 800 neighbouring positions
- w_query: bfloat16 [2048, 2048], P('row', 'col'), may hold values from -0.5 to 0.5
- w_key: bfloat16 [2048, 512], P('row', 'col'), may hold values from -0.5 to 0.5
- w_value: bfloat16 [2048, 512], P('row', 'col'), may hold values from -0.125 to 0.125
- w_out: bfloat16 [2048, 2048], P('col', 'row'), may hold values from -3 to 3
- w_gate: bfloat16 [2048, 8192], P('row', 'col'), may hold values from -0.125 to 0.125
- w_up: bfloat16 [2048, 8192], P('row', 'col'), may hold values from -0.125 to 0.125
- w_down: bfloat16 [8192, 2048], P('col', 'row'), may hold values from -0.375 to 0.375
- gain_attn: float32 [2048], P('row'), may hold values from 0.1 to 1.9
- gain_ffn: float32 [2048], P('row'), may hold values from 0.1 to 1.9
- cotangent: bfloat16 [2, 8, 1024, 2048], P(None, ('dp', 'col'), None, 'row'), may hold values from -6 to 6
Outputs:
- block_out: bfloat16 [2, 8, 1024, 2048], P(None, ('dp', 'col'), None, 'row')
- grad_input: float32 [2, 8, 1024, 2048], P(None, ('dp', 'col'), None, 'row')
- grad_query: float32 [2048, 2048], P('row', 'col')
- grad_key: float32 [2048, 512], P('row', 'col')
- grad_value: float32 [2048, 512], P('row', 'col')
- grad_out: float32 [2048, 2048], P('col', 'row')
- gate_weight_gradient: float32 [2048, 8192], P('row', 'col')
- grad_up: float32 [2048, 8192], P('row', 'col')
- grad_down: float32 [8192, 2048], P('col', 'row')
- grad_gain_attn: float32 [2048], P('row')
- grad_gain_ffn: float32 [2048], P('row')
The draws below stay inside these ranges and needn't reach their ends.
Inputs may be any that keep to these rules, and one draw needn't show every extreme that they name: `segment_ids`: segment numbers never fall along a sequence; each of the 4 documents of a sequence has 1 to 800 tokens, one of them exactly 800.
All inputs are finite; a program needn't handle non-finite values.
Results may differ from the reference program's by a relative error of at most 0.014.
The reference program's roundings to bfloat16 on the way count: a program that leaves them out, or rounds other values in their place, can miss the bound.
Values may be sent and summed in bfloat16 or wider, within the bound.
No kernel may reach another device: no remote copies, remote signals or barrier semaphores. Data moves between devices by JAX's collectives and lax.ppermute only.
A program may use at most 576 MiB of HBM per device.

```python
import math
import jax
import jax.numpy as jnp
import numpy as np
from jax import lax

D = 2048
HQ = 32
HK = 8
HD = 64
FF = 8192
LEN = 1024
MB = 2
DOCS = 4
NSEQ = 8
DOC_MOST = 800


def draw_hidden_in(key, part):
    key_parts = jax.random.split(key, 3)
    full_shape = (MB, NSEQ, LEN, D)
    columns = jnp.arange(D, dtype=jnp.float32) / D
    base_draw = jnp.clip(jax.random.normal(key_parts[0], full_shape, jnp.float32), -4.0, 4.0)
    rise_scale = jnp.exp(math.log(3.0) * columns)
    column_scale = 0.6 * rise_scale * jnp.exp(jax.random.uniform(key_parts[1], (D,), jnp.float32, -0.35, 0.35))
    row_scale = jnp.exp(jax.random.uniform(key_parts[2], (MB, NSEQ, LEN, 1), jnp.float32, math.log(0.4), math.log(4.0)))
    return (base_draw * column_scale * row_scale).astype(jnp.bfloat16)


def level_of(stream_key, dims, cuts, low, top_value):
    gain = 1.0
    for axis_at, blocks in cuts:
        heights = jax.random.uniform(jax.random.fold_in(jax.random.fold_in(stream_key, 6), axis_at), (blocks,), jnp.float32, low / len(cuts), top_value / len(cuts))
        gain = gain * jnp.repeat(jnp.exp(heights), dims[axis_at] // blocks).reshape((-1,) + (1,) * (len(dims) - 1 - axis_at))
    return gain


def split_up(number_of, total, limit, skew):
    loads = [(1 << 20) // math.isqrt(rank ** skew) + 1 for rank in range(2, number_of + 1)]
    spare, counts = total - limit - (number_of - 1), [1] * (number_of - 1)
    while spare > 0:
        candidates = [i for i in range(number_of - 1) if counts[i] < limit]
        whole, left = sum([loads[i] for i in candidates]), spare
        for i in candidates:
            extra = min(limit - counts[i], max(1, left * loads[i] // whole), spare)
            counts[i] = counts[i] + extra
            spare = spare - extra
    return np.array([limit] + counts)


def ragged_sizes(rng, number_of, total, bound, slope):
    if number_of == 2:
        one = jax.random.randint(rng, (), max(1, total - bound), min(bound, total - 1) + 1)
        return jnp.stack([one, total - one])
    lengths = jnp.asarray(split_up(number_of, total, bound, slope), jnp.int32)
    couples = (number_of - 1) // 2
    donor, sink = lengths[1:1 + 2 * couples:2], lengths[2:2 + 2 * couples:2]
    room = jnp.minimum(donor - 1, bound - sink)
    shifted = jax.random.randint(jax.random.fold_in(rng, 1), (couples,), 0, 1 << 20) % (room + 1)
    lengths = lengths.at[1:1 + 2 * couples:2].set(donor - shifted).at[2:2 + 2 * couples:2].set(sink + shifted)
    return lengths[jax.random.permutation(jax.random.fold_in(rng, 2), number_of)]


def bell_draw(rng, dims, spread, most, cuts=(), kind=jnp.bfloat16):
    values = spread * jax.random.normal(rng, dims, jnp.float32)
    if cuts:
        values = values * level_of(rng, dims, cuts, -0.22, 0.18)
    return jnp.clip(values, -most, most).astype(kind)


def setup_inputs(seed: int = 0) -> dict:
    seeds = jax.random.split(jax.random.key(seed), 13)
    hidden_in = draw_hidden_in(jax.random.fold_in(seeds[12], 71), 0)
    segment_ids = jax.vmap(lambda own: jnp.searchsorted(jnp.cumsum(ragged_sizes(own, DOCS, LEN, DOC_MOST, 1)), jnp.arange(LEN), side="right"))(jax.random.split(seeds[1], MB * NSEQ)).reshape((MB, NSEQ, LEN)).astype(jnp.int32)
    w_query = bell_draw(seeds[2], (D, HQ * HD), (D // 16) ** -0.5, 0.5, ((0, 4), (1, 4)))
    w_key = bell_draw(seeds[3], (D, HK * HD), (D // 16) ** -0.5, 0.5, ((0, 4), (1, 4)))
    w_value = bell_draw(seeds[4], (D, HK * HD), D ** -0.5, 0.125, ((0, 4), (1, 4)))
    w_out = bell_draw(seeds[5], (HQ * HD, D), 4 ** -0.5, 3.0, ((0, 4), (1, 4)))
    w_gate = bell_draw(seeds[6], (D, FF), D ** -0.5, 0.125, ((0, 4), (1, 4)))
    w_up = bell_draw(seeds[7], (D, FF), D ** -0.5, 0.125, ((0, 4), (1, 4)))
    w_down = bell_draw(seeds[8], (FF, D), (FF // 32) ** -0.5, 0.375, ((0, 4), (1, 4)))
    gain_attn = jnp.clip(1.0 + 0.18 * jax.random.normal(seeds[9], (D,), jnp.float32), 0.1, 1.9)
    gain_ffn = jnp.clip(1.0 + 0.18 * jax.random.normal(seeds[10], (D,), jnp.float32), 0.1, 1.9)
    cotangent = bell_draw(seeds[11], (MB, NSEQ, LEN, D), 1.0, 6.0, ((1, 8), (3, 4)))
    return {"hidden_in": hidden_in, "segment_ids": segment_ids, "w_query": w_query, "w_key": w_key, "w_value": w_value, "w_out": w_out, "w_gate": w_gate, "w_up": w_up, "w_down": w_down, "gain_attn": gain_attn, "gain_ffn": gain_ffn, "cotangent": cotangent}


EPSILON = 1e-05
RESIDUAL_SCALE = 0.22
SCORE_SCALE = 0.015625
ROPE_BASE = 10000000.0
MASKED_SCORE = -1e+30

@jax.custom_vjp
def low(v):
    return lax.optimization_barrier(v.astype(jnp.bfloat16)).astype(jnp.float32)

@jax.custom_vjp
def low_back(v):
    return v

def low_keep(v):
    return (low(v), None)

def low_pass(kept, grad):
    return (grad,)

def back_keep(v):
    return (v, None)

def back_low(kept, grad):
    return (low(grad),)
low.defvjp(low_keep, low_pass)
low_back.defvjp(back_keep, back_low)

def matmul_rows(left_operand_half, right_operand_half):
    return jnp.einsum('tgf,fm->tgm', left_operand_half, right_operand_half, precision=lax.Precision.HIGHEST)

def positions(segment_row):
    places = jnp.arange(segment_row.shape[0], dtype=jnp.int32)
    starts = jnp.concatenate([jnp.ones((1,), jnp.bool_), segment_row[1:] != segment_row[:-1]])
    first_place = lax.cummax(jnp.where(starts, places, jnp.zeros_like(places)), axis=0)
    return places - first_place

def rotary(segment_row):
    half_dim = HD // 2
    frequency = jnp.exp(jnp.arange(half_dim, dtype=jnp.float32) * (-2.0 * math.log(ROPE_BASE) / HD))
    angles = positions(segment_row).astype(jnp.float32)[:, None] * frequency[None, :]
    return (jnp.cos(angles)[:, None, :], jnp.sin(angles)[:, None, :])

def rotate(head_rows, cosine, sine_part):
    half_dim = head_rows.shape[-1] // 2
    first_half = head_rows[..., :half_dim]
    second_half = head_rows[..., half_dim:]
    return jnp.concatenate([first_half * cosine - second_half * sine_part, second_half * cosine + first_half * sine_part], axis=-1)

def attend(pieces):
    query_in, key_in, value_in, segment_row = pieces
    seq_len = segment_row.shape[0]
    cosine, sine_part = rotary(segment_row)
    query_rot = low(rotate(query_in.reshape(seq_len, HQ, HD), cosine, sine_part)).reshape(seq_len, HK, HQ // HK, HD)
    key_rot = low(rotate(key_in.reshape(seq_len, HK, HD), cosine, sine_part))
    value_grp = value_in.reshape(seq_len, HK, HD)
    places = jnp.arange(seq_len)
    allowed = (segment_row[:, None] == segment_row[None, :]) & (places[:, None] >= places[None, :])
    attention_scores = jnp.einsum('qkgd,pkd->kgqp', query_rot, key_rot, precision=lax.Precision.HIGHEST) * SCORE_SCALE
    attention_scores = low_back(jnp.where(allowed, attention_scores, MASKED_SCORE))
    weights_low = low(jax.nn.softmax(attention_scores, axis=-1))
    mixed = jnp.einsum('kgqp,pkd->qkgd', weights_low, value_grp, precision=lax.Precision.HIGHEST)
    return mixed.reshape(seq_len, HQ * HD)

def rms_scale(rows_in):
    return lax.rsqrt(lax.optimization_barrier(jnp.mean(rows_in * rows_in, axis=-1, keepdims=True)) + EPSILON)

def layer(block_in, segment_block, w_query, w_key, w_value, w_out, w_gate, w_up, w_down, gain_attn, gain_ffn):
    normed_attn = low(block_in * rms_scale(block_in) * gain_attn)
    query_all = low_back(matmul_rows(normed_attn, w_query))
    key_all = low_back(matmul_rows(normed_attn, w_key))
    value_all = low(low_back(matmul_rows(normed_attn, w_value)))
    mixed = lax.map(jax.checkpoint(attend), (query_all, key_all, value_all, segment_block))
    mixed = low(low_back(mixed))
    attn_branch = low_back(matmul_rows(mixed, w_out))
    resid_mid = block_in + RESIDUAL_SCALE * attn_branch
    normed_ffn = low(resid_mid * rms_scale(resid_mid) * gain_ffn)
    gate_rows = low_back(matmul_rows(normed_ffn, w_gate))
    up_projection_rows = low_back(matmul_rows(normed_ffn, w_up))
    act_rows = low(jax.nn.silu(gate_rows) * up_projection_rows)
    ffn_branch = low_back(matmul_rows(act_rows, w_down))
    return resid_mid + RESIDUAL_SCALE * ffn_branch

def reference(hidden_in, segment_ids, w_query, w_key, w_value, w_out, w_gate, w_up, w_down, gain_attn, gain_ffn, cotangent):
    params = tuple((weight.astype(jnp.float32) for weight in (w_query, w_key, w_value, w_out, w_gate, w_up, w_down, gain_attn, gain_ffn)))
    group_size = 4 if NSEQ % 4 == 0 else 1
    blocks_count = NSEQ // group_size

    def scan_step(totals, carried):
        block_in, segment_block, block_cot = carried

        def forward(block_f, *weights_f):
            return layer(block_f, segment_block, *weights_f)
        block_result, pullback = jax.vjp(forward, block_in.astype(jnp.float32), *params)
        pieces = pullback(block_cot.astype(jnp.float32))
        totals = tuple((total_now + piece for total_now, piece in zip(totals, pieces[1:])))
        return (totals, (block_result.astype(jnp.bfloat16), pieces[0]))
    totals = tuple((jnp.zeros(weight.shape, jnp.float32) for weight in params))
    outs_all = []
    grads_all = []
    block_shape = (blocks_count, group_size, LEN, D)
    for batch_index in range(MB):
        carried = (hidden_in[batch_index].reshape(block_shape), segment_ids[batch_index].reshape(blocks_count, group_size, LEN), cotangent[batch_index].reshape(block_shape))
        totals, results = lax.scan(scan_step, totals, carried)
        outs_all.append(results[0].reshape(NSEQ, LEN, D))
        grads_all.append(results[1].reshape(NSEQ, LEN, D))
    return (jnp.stack(outs_all), jnp.stack(grads_all), totals[0], totals[1], totals[2], totals[3], totals[4], totals[5], totals[6], totals[7], totals[8])
```

```python
import math

import jax
import jax.numpy as jnp
from jax import lax
from jax.sharding import PartitionSpec as P

HD = 64

EPSILON = 1e-05
RESIDUAL_SCALE = 0.22
SCORE_SCALE = 0.015625
ROPE_BASE = 10000000.0
MASKED_SCORE = -1e30


def positions(segment_rows):
    seq_len = segment_rows.shape[-1]
    places = jnp.arange(seq_len, dtype=jnp.int32)
    starts = jnp.concatenate(
        [
            jnp.ones(segment_rows.shape[:-1] + (1,), jnp.bool_),
            segment_rows[..., 1:] != segment_rows[..., :-1],
        ],
        axis=-1,
    )
    first_place = lax.cummax(
        jnp.where(starts, places, jnp.zeros_like(places)), axis=segment_rows.ndim - 1
    )
    return places - first_place


def rotary(place_rows):
    half_dim = HD // 2
    frequency = jnp.exp(jnp.arange(half_dim, dtype=jnp.float32) * (-2.0 * math.log(ROPE_BASE) / HD))
    angles = place_rows.astype(jnp.float32)[..., None] * frequency
    return (jnp.cos(angles)[..., None, :], jnp.sin(angles)[..., None, :])


def rotate(head_rows, cosine, sine_part):
    half_dim = head_rows.shape[-1] // 2
    first_half = head_rows[..., :half_dim]
    second_half = head_rows[..., half_dim:]
    return jnp.concatenate(
        [
            first_half * cosine - second_half * sine_part,
            second_half * cosine + first_half * sine_part,
        ],
        axis=-1,
    )


def masked_scores(query_rot, key_rot, query_segment, key_segment, query_place):
    key_place = jnp.arange(key_segment.shape[0])
    allowed = (query_segment[:, None] == key_segment[None, :]) & (
        query_place[:, None] >= key_place[None, :]
    )
    raw_scores = (
        jnp.einsum("qkgd,pkd->kgqp", query_rot, key_rot, preferred_element_type=jnp.float32)
        * SCORE_SCALE
    )
    return jnp.where(allowed, raw_scores, MASKED_SCORE)


def attend_forward(pieces):
    query_rot, key_all, value_all, query_segment, key_segment, query_place = pieces
    chunk, heads_k, group_count, head_dim = query_rot.shape
    attention_scores = masked_scores(query_rot, key_all, query_segment, key_segment, query_place)
    row_peak = jnp.max(attention_scores, axis=-1, keepdims=True)
    log_total = row_peak + jnp.log(
        jnp.sum(jnp.exp(attention_scores - row_peak), axis=-1, keepdims=True)
    )
    attn_probs = jnp.exp(attention_scores - log_total).astype(jnp.bfloat16)
    mixed = jnp.einsum("kgqp,pkd->qkgd", attn_probs, value_all, preferred_element_type=jnp.float32)
    return mixed.reshape(chunk, -1).astype(jnp.bfloat16), log_total


def attend_backward(pieces):
    grad_mixed, query_rot, key_all, value_all, log_total, query_segment, key_segment, query_place = pieces
    chunk, heads_k, group_count, head_dim = query_rot.shape
    grad_grouped = grad_mixed.reshape(chunk, heads_k, group_count, head_dim)
    attn_probs = jnp.exp(
        masked_scores(query_rot, key_all, query_segment, key_segment, query_place) - log_total
    )
    grad_probs = jnp.einsum(
        "qkgd,pkd->kgqp", grad_grouped, value_all, preferred_element_type=jnp.float32
    )
    grad_value = jnp.einsum(
        "kgqp,qkgd->pkd",
        attn_probs.astype(jnp.bfloat16),
        grad_grouped,
        preferred_element_type=jnp.float32,
    )
    grad_scores = (
        attn_probs * (grad_probs - jnp.sum(attn_probs * grad_probs, axis=-1, keepdims=True))
    ).astype(jnp.bfloat16)
    grad_query = (
        jnp.einsum("kgqp,pkd->qkgd", grad_scores, key_all, preferred_element_type=jnp.float32)
        * SCORE_SCALE
    )
    grad_key = (
        jnp.einsum("kgqp,qkgd->pkd", grad_scores, query_rot, preferred_element_type=jnp.float32)
        * SCORE_SCALE
    )
    return grad_query, jnp.concatenate([grad_key, grad_value], axis=-1)


def make_shards(n_dp, n_row, n_col):
    def gather_features(block, axis):
        half = block.shape[axis] // n_dp
        mine = lax.dynamic_slice_in_dim(block, lax.axis_index("dp") * half, half, axis=axis)
        gathered = lax.all_gather(mine, "row", axis=axis)
        gathered = lax.all_gather(gathered, "dp", axis=axis)
        gathered = jnp.swapaxes(gathered, axis, axis + 1)
        shape = list(block.shape)
        shape[axis] = block.shape[axis] * n_row
        return gathered.reshape(shape)

    def reduce_features(partial, axis):
        half = partial.shape[axis] // (n_row * n_dp)
        shape = list(partial.shape)
        shape[axis : axis + 1] = [n_row, n_dp, half]
        split = jnp.swapaxes(partial.reshape(shape), axis, axis + 1)
        split = lax.psum_scatter(split, "dp", scatter_dimension=axis)
        split = lax.psum_scatter(split, "row", scatter_dimension=axis)
        return lax.all_gather(split, "dp", axis=axis, tiled=True)

    def to_tokens(rows):
        batches, local, seq_len, width = rows.shape
        rows = rows.reshape(batches, local, n_row, seq_len // n_row, width)
        rows = lax.all_to_all(rows, "row", 2, 3)
        return rows.reshape(batches, local, seq_len // n_row, n_row * width)

    def to_features(rows):
        batches, local, chunk, width = rows.shape
        rows = rows.reshape(batches, local, chunk, n_row, width // n_row)
        rows = lax.all_to_all(rows, "row", 3, 2)
        return rows.reshape(batches, local, n_row * chunk, width // n_row)

    def shards(
        hidden_in,
        segment_ids,
        w_query,
        w_key,
        w_value,
        w_out,
        w_gate,
        w_up,
        w_down,
        gain_attn,
        gain_ffn,
        cotangent,
    ):
        batches, local, seq_len, width_r = hidden_in.shape
        chunk = seq_len // n_row
        row_index = lax.axis_index("row")
        query_cols = w_query.shape[1]
        key_cols = w_key.shape[1]
        heads_q = query_cols // HD
        heads_k = key_cols // HD
        group_count = heads_q // heads_k
        ffn_cols = w_gate.shape[1]

        w_qkv = gather_features(jnp.concatenate([w_query, w_key, w_value], axis=1), 0)
        w_pair = gather_features(jnp.concatenate([w_gate, w_up], axis=1), 0)
        w_out_all = gather_features(w_out, 1)
        w_down_all = gather_features(w_down, 1)
        gain_attn_all = lax.all_gather(gain_attn, "row", tiled=True)
        gain_ffn_all = lax.all_gather(gain_ffn, "row", tiled=True)

        segments = lax.all_gather(segment_ids, "row", axis=1, tiled=True)
        places = positions(segments)
        query_segments = lax.dynamic_slice_in_dim(segments, row_index * chunk, chunk, axis=2)
        query_places_seq = lax.dynamic_slice_in_dim(places, row_index * chunk, chunk, axis=2)
        query_index = row_index * chunk + jnp.arange(chunk)
        seq_all = segments.shape[1]

        hidden_t = to_tokens(hidden_in)
        cotangent_t = to_tokens(cotangent)

        grad_qkv_w = None
        grad_out_w = None
        grad_pair_w = None
        grad_down_w = None
        gain_attn_total = jnp.zeros(gain_attn_all.shape, jnp.float32)
        gain_ffn_total = jnp.zeros(gain_ffn_all.shape, jnp.float32)
        outs_list = []
        inputs_grad = []
        for batch_index in range(batches):
            rows_f = hidden_t[batch_index].astype(jnp.float32)
            inv_attn = lax.rsqrt(jnp.mean(rows_f * rows_f, axis=-1, keepdims=True) + EPSILON)
            norm_attn = rows_f * inv_attn
            normed_attn = (norm_attn * gain_attn_all).astype(jnp.bfloat16)
            spread_attn = lax.all_gather(normed_attn, "col", axis=0, tiled=True)
            qkv = jnp.einsum(
                "std,dm->stm", spread_attn, w_qkv, preferred_element_type=jnp.float32
            )
            cosine, sine_part = rotary(query_places_seq[batch_index])
            query_rot = rotate(
                qkv[..., :query_cols].reshape(seq_all, chunk, heads_q, HD), cosine, sine_part
            ).astype(jnp.bfloat16)
            key_rot = rotate(
                qkv[..., query_cols : query_cols + key_cols].reshape(seq_all, chunk, heads_k, HD),
                cosine,
                sine_part,
            ).astype(jnp.bfloat16)
            value_low = (
                qkv[..., query_cols + key_cols :]
                .reshape(seq_all, chunk, heads_k, HD)
                .astype(jnp.bfloat16)
            )
            key_value = lax.all_gather(
                jnp.concatenate([key_rot, value_low], axis=-1), "row", axis=1, tiled=True
            )
            key_all = key_value[..., :HD]
            value_all = key_value[..., HD:]
            query_grouped = query_rot.reshape(seq_all, chunk, heads_k, group_count, HD)
            query_place = jnp.broadcast_to(query_index, (seq_all, chunk))
            mixed, log_total = lax.map(
                attend_forward,
                (
                    query_grouped,
                    key_all,
                    value_all,
                    query_segments[batch_index],
                    segments[batch_index],
                    query_place,
                ),
            )
            attn_part = jnp.einsum(
                "stm,md->std", mixed, w_out_all, preferred_element_type=jnp.float32
            )
            attn_branch = lax.psum_scatter(attn_part, "col", scatter_dimension=0, tiled=True)
            resid_mid = rows_f + RESIDUAL_SCALE * attn_branch
            inv_ffn = lax.rsqrt(jnp.mean(resid_mid * resid_mid, axis=-1, keepdims=True) + EPSILON)
            norm_ffn = resid_mid * inv_ffn
            normed_ffn = (norm_ffn * gain_ffn_all).astype(jnp.bfloat16)
            spread_ffn = lax.all_gather(normed_ffn, "col", axis=0, tiled=True)
            pair = jnp.einsum(
                "std,df->stf", spread_ffn, w_pair, preferred_element_type=jnp.float32
            )
            gate_rows = pair[..., :ffn_cols]
            up_rows = pair[..., ffn_cols:]
            sigmoid_gate = jax.nn.sigmoid(gate_rows)
            act_low = (gate_rows * sigmoid_gate * up_rows).astype(jnp.bfloat16)
            ffn_part = jnp.einsum(
                "stf,fd->std", act_low, w_down_all, preferred_element_type=jnp.float32
            )
            ffn_branch = lax.psum_scatter(ffn_part, "col", scatter_dimension=0, tiled=True)
            outs_list.append((resid_mid + RESIDUAL_SCALE * ffn_branch).astype(jnp.bfloat16))

            grad_rows = cotangent_t[batch_index].astype(jnp.float32)
            grad_ffn = (RESIDUAL_SCALE * grad_rows).astype(jnp.bfloat16)
            spread_grad_ffn = lax.all_gather(grad_ffn, "col", axis=0, tiled=True)
            fresh_down = jnp.einsum(
                "stf,std->fd", act_low, spread_grad_ffn, preferred_element_type=jnp.float32
            )
            grad_act = jnp.einsum(
                "std,fd->stf", spread_grad_ffn, w_down_all, preferred_element_type=jnp.float32
            )
            grad_gate_rows = (
                grad_act * up_rows * sigmoid_gate * (1.0 + gate_rows * (1.0 - sigmoid_gate))
            )
            grad_up_rows = grad_act * gate_rows * sigmoid_gate
            paired_gradient = jnp.concatenate([grad_gate_rows, grad_up_rows], axis=-1).astype(
                jnp.bfloat16
            )
            fresh_pair = jnp.einsum(
                "std,stf->df", spread_ffn, paired_gradient, preferred_element_type=jnp.float32
            )
            grad_normed_part = jnp.einsum(
                "stf,df->std", paired_gradient, w_pair, preferred_element_type=jnp.float32
            )
            grad_normed_ffn = lax.psum_scatter(
                grad_normed_part, "col", scatter_dimension=0, tiled=True
            )
            scaled_ffn = grad_normed_ffn * gain_ffn_all
            gain_ffn_total = gain_ffn_total + jnp.sum(grad_normed_ffn * norm_ffn, axis=(0, 1))
            inner_ffn = jnp.mean(scaled_ffn * norm_ffn, axis=-1, keepdims=True)
            grad_mid = grad_rows + inv_ffn * (scaled_ffn - norm_ffn * inner_ffn)
            grad_attn = (RESIDUAL_SCALE * grad_mid).astype(jnp.bfloat16)
            spread_grad_attn = lax.all_gather(grad_attn, "col", axis=0, tiled=True)
            fresh_out = jnp.einsum(
                "stm,std->md", mixed, spread_grad_attn, preferred_element_type=jnp.float32
            )
            grad_mixed = jnp.einsum(
                "std,md->stm", spread_grad_attn, w_out_all, preferred_element_type=jnp.float32
            ).astype(jnp.bfloat16)
            grad_query_rot, grad_kv_part = lax.map(
                attend_backward,
                (
                    grad_mixed,
                    query_grouped,
                    key_all,
                    value_all,
                    log_total,
                    query_segments[batch_index],
                    segments[batch_index],
                    query_place,
                ),
            )
            grad_kv = lax.psum_scatter(grad_kv_part, "row", scatter_dimension=1, tiled=True)
            grad_query = rotate(
                grad_query_rot.reshape(seq_all, chunk, heads_q, HD), cosine, -sine_part
            )
            grad_key = rotate(grad_kv[..., :HD], cosine, -sine_part)
            grad_qkv = jnp.concatenate(
                [
                    grad_query.reshape(seq_all, chunk, -1),
                    grad_key.reshape(seq_all, chunk, -1),
                    grad_kv[..., HD:].reshape(seq_all, chunk, -1),
                ],
                axis=-1,
            ).astype(jnp.bfloat16)
            fresh_qkv = jnp.einsum(
                "std,stm->dm", spread_attn, grad_qkv, preferred_element_type=jnp.float32
            )
            grad_normed_attn_part = jnp.einsum(
                "stm,dm->std", grad_qkv, w_qkv, preferred_element_type=jnp.float32
            )
            grad_normed_attn = lax.psum_scatter(
                grad_normed_attn_part, "col", scatter_dimension=0, tiled=True
            )
            scaled_attn = grad_normed_attn * gain_attn_all
            gain_attn_total = gain_attn_total + jnp.sum(grad_normed_attn * norm_attn, axis=(0, 1))
            inner_attn = jnp.mean(scaled_attn * norm_attn, axis=-1, keepdims=True)
            inputs_grad.append(grad_mid + inv_attn * (scaled_attn - norm_attn * inner_attn))
            if grad_qkv_w is None:
                grad_qkv_w, grad_out_w = fresh_qkv, fresh_out
                grad_pair_w, grad_down_w = fresh_pair, fresh_down
            else:
                grad_qkv_w = grad_qkv_w + fresh_qkv
                grad_out_w = grad_out_w + fresh_out
                grad_pair_w = grad_pair_w + fresh_pair
                grad_down_w = grad_down_w + fresh_down

        total_pair = reduce_features(grad_pair_w, 0)
        total_down = reduce_features(grad_down_w, 1)
        total_qkv = reduce_features(grad_qkv_w, 0)
        total_out = reduce_features(grad_out_w, 1)
        gain_totals = lax.psum(
            jnp.stack([gain_attn_total, gain_ffn_total]), ("dp", "row", "col")
        )
        gain_totals = lax.dynamic_slice_in_dim(gain_totals, row_index * width_r, width_r, axis=1)
        key_end = query_cols + key_cols
        return (
            to_features(jnp.stack(outs_list)),
            to_features(jnp.stack(inputs_grad)),
            total_qkv[:, :query_cols],
            total_qkv[:, query_cols:key_end],
            total_qkv[:, key_end:],
            total_out,
            total_pair[:, :ffn_cols],
            total_pair[:, ffn_cols:],
            total_down,
            gain_totals[0],
            gain_totals[1],
        )

    return shards


def solution(mesh):
    activation = P(None, ("dp", "col"), None, "row")
    return jax.shard_map(
        make_shards(mesh.shape["dp"], mesh.shape["row"], mesh.shape["col"]),
        mesh=mesh,
        in_specs=(
            activation,
            P(None, ("dp", "row"), None),
            P("row", "col"),
            P("row", "col"),
            P("row", "col"),
            P("col", "row"),
            P("row", "col"),
            P("row", "col"),
            P("col", "row"),
            P("row"),
            P("row"),
            activation,
        ),
        out_specs=(
            activation,
            activation,
            P("row", "col"),
            P("row", "col"),
            P("row", "col"),
            P("col", "row"),
            P("row", "col"),
            P("row", "col"),
            P("col", "row"),
            P("row"),
            P("row"),
        ),
        check_vma=False,
    )
```

```python
import math

import jax
import jax.numpy as jnp
from jax import lax
from jax.sharding import PartitionSpec as P

HD = 64

EPSILON = 1e-05
RESIDUAL_SCALE = 0.22
SCORE_SCALE = 0.015625
ROPE_BASE = 10000000.0
MASKED_SCORE = -1e30


def positions(segment_rows):
    seq_len = segment_rows.shape[-1]
    places = jnp.arange(seq_len, dtype=jnp.int32)
    starts = jnp.concatenate(
        [
            jnp.ones(segment_rows.shape[:-1] + (1,), jnp.bool_),
            segment_rows[..., 1:] != segment_rows[..., :-1],
        ],
        axis=-1,
    )
    first_place = lax.cummax(
        jnp.where(starts, places, jnp.zeros_like(places)), axis=segment_rows.ndim - 1
    )
    return places - first_place


def rotary(place_rows):
    half_dim = HD // 2
    frequency = jnp.exp(jnp.arange(half_dim, dtype=jnp.float32) * (-2.0 * math.log(ROPE_BASE) / HD))
    angles = place_rows.astype(jnp.float32)[..., None] * frequency
    return (jnp.cos(angles)[..., None, :], jnp.sin(angles)[..., None, :])


def rotate(head_rows, cosine, sine_part):
    half_dim = head_rows.shape[-1] // 2
    first_half = head_rows[..., :half_dim]
    second_half = head_rows[..., half_dim:]
    return jnp.concatenate(
        [
            first_half * cosine - second_half * sine_part,
            second_half * cosine + first_half * sine_part,
        ],
        axis=-1,
    )


def masked_scores(query_rot, key_rot, query_segment, key_segment, query_place):
    key_place = jnp.arange(key_segment.shape[0])
    allowed = (query_segment[:, None] == key_segment[None, :]) & (
        query_place[:, None] >= key_place[None, :]
    )
    raw_scores = (
        jnp.einsum("qkgd,pkd->kgqp", query_rot, key_rot, preferred_element_type=jnp.float32)
        * SCORE_SCALE
    )
    return jnp.where(allowed, raw_scores, MASKED_SCORE)


def attend_forward(pieces):
    query_rot, key_all, value_all, query_segment, key_segment, query_place = pieces
    chunk, heads_k, group_count, head_dim = query_rot.shape
    attention_scores = masked_scores(query_rot, key_all, query_segment, key_segment, query_place)
    row_peak = jnp.max(attention_scores, axis=-1, keepdims=True)
    log_total = row_peak + jnp.log(
        jnp.sum(jnp.exp(attention_scores - row_peak), axis=-1, keepdims=True)
    )
    attn_probs = jnp.exp(attention_scores - log_total).astype(jnp.bfloat16)
    mixed = jnp.einsum("kgqp,pkd->qkgd", attn_probs, value_all, preferred_element_type=jnp.float32)
    return mixed.reshape(chunk, -1).astype(jnp.bfloat16), log_total


def attend_backward(pieces):
    grad_mixed, query_rot, key_all, value_all, log_total, query_segment, key_segment, query_place = pieces
    chunk, heads_k, group_count, head_dim = query_rot.shape
    grad_grouped = grad_mixed.reshape(chunk, heads_k, group_count, head_dim)
    attn_probs = jnp.exp(
        masked_scores(query_rot, key_all, query_segment, key_segment, query_place) - log_total
    )
    grad_probs = jnp.einsum(
        "qkgd,pkd->kgqp", grad_grouped, value_all, preferred_element_type=jnp.float32
    )
    grad_value = jnp.einsum(
        "kgqp,qkgd->pkd",
        attn_probs.astype(jnp.bfloat16),
        grad_grouped,
        preferred_element_type=jnp.float32,
    )
    grad_scores = (
        attn_probs * (grad_probs - jnp.sum(attn_probs * grad_probs, axis=-1, keepdims=True))
    ).astype(jnp.bfloat16)
    grad_query = (
        jnp.einsum("kgqp,pkd->qkgd", grad_scores, key_all, preferred_element_type=jnp.float32)
        * SCORE_SCALE
    )
    grad_key = (
        jnp.einsum("kgqp,qkgd->pkd", grad_scores, query_rot, preferred_element_type=jnp.float32)
        * SCORE_SCALE
    )
    return grad_query, jnp.concatenate([grad_key, grad_value], axis=-1)


def scatter_low(partial, axis_name, axis):
    return lax.psum_scatter(
        partial.astype(jnp.bfloat16), axis_name, scatter_dimension=axis, tiled=True
    ).astype(jnp.float32)


def make_shards(n_dp, n_row, n_col):
    def gather_features(block, axis):
        half = block.shape[axis] // n_dp
        mine = lax.dynamic_slice_in_dim(block, lax.axis_index("dp") * half, half, axis=axis)
        gathered = lax.all_gather(mine, "row", axis=axis)
        gathered = lax.all_gather(gathered, "dp", axis=axis)
        gathered = jnp.swapaxes(gathered, axis, axis + 1)
        shape = list(block.shape)
        shape[axis] = block.shape[axis] * n_row
        return gathered.reshape(shape)

    def reduce_features(partial, axis):
        half = partial.shape[axis] // (n_row * n_dp)
        shape = list(partial.shape)
        shape[axis : axis + 1] = [n_row, n_dp, half]
        split = jnp.swapaxes(partial.reshape(shape), axis, axis + 1)
        split = lax.psum_scatter(split, "dp", scatter_dimension=axis)
        split = lax.psum_scatter(split, "row", scatter_dimension=axis)
        return lax.all_gather(split, "dp", axis=axis, tiled=True)

    def to_tokens(rows):
        batches, local, seq_len, width = rows.shape
        rows = rows.reshape(batches, local, n_row, seq_len // n_row, width)
        rows = lax.all_to_all(rows, "row", 2, 3)
        return rows.reshape(batches, local, seq_len // n_row, n_row * width)

    def to_features(rows):
        batches, local, chunk, width = rows.shape
        rows = rows.reshape(batches, local, chunk, n_row, width // n_row)
        rows = lax.all_to_all(rows, "row", 3, 2)
        return rows.reshape(batches, local, n_row * chunk, width // n_row)

    def shards(
        hidden_in,
        segment_ids,
        w_query,
        w_key,
        w_value,
        w_out,
        w_gate,
        w_up,
        w_down,
        gain_attn,
        gain_ffn,
        cotangent,
    ):
        batches, local, seq_len, width_r = hidden_in.shape
        chunk = seq_len // n_row
        row_index = lax.axis_index("row")
        query_cols = w_query.shape[1]
        key_cols = w_key.shape[1]
        heads_q = query_cols // HD
        heads_k = key_cols // HD
        group_count = heads_q // heads_k
        ffn_cols = w_gate.shape[1]

        w_qkv = gather_features(jnp.concatenate([w_query, w_key, w_value], axis=1), 0)
        w_pair = gather_features(jnp.concatenate([w_gate, w_up], axis=1), 0)
        w_out_all = gather_features(w_out, 1)
        w_down_all = gather_features(w_down, 1)
        gain_attn_all = lax.all_gather(gain_attn, "row", tiled=True)
        gain_ffn_all = lax.all_gather(gain_ffn, "row", tiled=True)

        segments = lax.all_gather(segment_ids, "row", axis=1, tiled=True)
        places = positions(segments)
        query_segments = lax.dynamic_slice_in_dim(segments, row_index * chunk, chunk, axis=2)
        query_places_seq = lax.dynamic_slice_in_dim(places, row_index * chunk, chunk, axis=2)
        query_index = row_index * chunk + jnp.arange(chunk)
        seq_all = segments.shape[1]

        hidden_t = to_tokens(hidden_in)
        cotangent_t = to_tokens(cotangent)

        grad_qkv_w = None
        grad_out_w = None
        grad_pair_w = None
        grad_down_w = None
        gain_attn_total = jnp.zeros(gain_attn_all.shape, jnp.float32)
        gain_ffn_total = jnp.zeros(gain_ffn_all.shape, jnp.float32)
        outs_list = []
        inputs_grad = []
        for batch_index in range(batches):
            rows_f = hidden_t[batch_index].astype(jnp.float32)
            inv_attn = lax.rsqrt(jnp.mean(rows_f * rows_f, axis=-1, keepdims=True) + EPSILON)
            norm_attn = rows_f * inv_attn
            normed_attn = (norm_attn * gain_attn_all).astype(jnp.bfloat16)
            spread_attn = lax.all_gather(normed_attn, "col", axis=0, tiled=True)
            qkv = jnp.einsum(
                "std,dm->stm", spread_attn, w_qkv, preferred_element_type=jnp.float32
            )
            cosine, sine_part = rotary(query_places_seq[batch_index])
            query_rot = rotate(
                qkv[..., :query_cols].reshape(seq_all, chunk, heads_q, HD), cosine, sine_part
            ).astype(jnp.bfloat16)
            key_rot = rotate(
                qkv[..., query_cols : query_cols + key_cols].reshape(seq_all, chunk, heads_k, HD),
                cosine,
                sine_part,
            ).astype(jnp.bfloat16)
            value_low = (
                qkv[..., query_cols + key_cols :]
                .reshape(seq_all, chunk, heads_k, HD)
                .astype(jnp.bfloat16)
            )
            key_value = lax.all_gather(
                jnp.concatenate([key_rot, value_low], axis=-1), "row", axis=1, tiled=True
            )
            key_all = key_value[..., :HD]
            value_all = key_value[..., HD:]
            query_grouped = query_rot.reshape(seq_all, chunk, heads_k, group_count, HD)
            query_place = jnp.broadcast_to(query_index, (seq_all, chunk))
            mixed, log_total = lax.map(
                attend_forward,
                (
                    query_grouped,
                    key_all,
                    value_all,
                    query_segments[batch_index],
                    segments[batch_index],
                    query_place,
                ),
            )
            attn_part = jnp.einsum(
                "stm,md->std", mixed, w_out_all, preferred_element_type=jnp.float32
            )
            attn_branch = scatter_low(attn_part, "col", 0)
            resid_mid = rows_f + RESIDUAL_SCALE * attn_branch
            inv_ffn = lax.rsqrt(jnp.mean(resid_mid * resid_mid, axis=-1, keepdims=True) + EPSILON)
            norm_ffn = resid_mid * inv_ffn
            normed_ffn = (norm_ffn * gain_ffn_all).astype(jnp.bfloat16)
            spread_ffn = lax.all_gather(normed_ffn, "col", axis=0, tiled=True)
            pair = jnp.einsum(
                "std,df->stf", spread_ffn, w_pair, preferred_element_type=jnp.float32
            )
            gate_rows = pair[..., :ffn_cols]
            up_rows = pair[..., ffn_cols:]
            sigmoid_gate = jax.nn.sigmoid(gate_rows)
            act_low = (gate_rows * sigmoid_gate * up_rows).astype(jnp.bfloat16)
            ffn_part = jnp.einsum(
                "stf,fd->std", act_low, w_down_all, preferred_element_type=jnp.float32
            )
            ffn_branch = scatter_low(ffn_part, "col", 0)
            outs_list.append((resid_mid + RESIDUAL_SCALE * ffn_branch).astype(jnp.bfloat16))

            grad_rows = cotangent_t[batch_index].astype(jnp.float32)
            grad_ffn = (RESIDUAL_SCALE * grad_rows).astype(jnp.bfloat16)
            spread_grad_ffn = lax.all_gather(grad_ffn, "col", axis=0, tiled=True)
            fresh_down = jnp.einsum(
                "stf,std->fd", act_low, spread_grad_ffn, preferred_element_type=jnp.float32
            )
            grad_act = jnp.einsum(
                "std,fd->stf", spread_grad_ffn, w_down_all, preferred_element_type=jnp.float32
            )
            grad_gate_rows = (
                grad_act * up_rows * sigmoid_gate * (1.0 + gate_rows * (1.0 - sigmoid_gate))
            )
            grad_up_rows = grad_act * gate_rows * sigmoid_gate
            paired_gradient = jnp.concatenate([grad_gate_rows, grad_up_rows], axis=-1).astype(
                jnp.bfloat16
            )
            fresh_pair = jnp.einsum(
                "std,stf->df", spread_ffn, paired_gradient, preferred_element_type=jnp.float32
            )
            grad_normed_part = jnp.einsum(
                "stf,df->std", paired_gradient, w_pair, preferred_element_type=jnp.float32
            )
            grad_normed_ffn = scatter_low(grad_normed_part, "col", 0)
            scaled_ffn = grad_normed_ffn * gain_ffn_all
            gain_ffn_total = gain_ffn_total + jnp.sum(grad_normed_ffn * norm_ffn, axis=(0, 1))
            inner_ffn = jnp.mean(scaled_ffn * norm_ffn, axis=-1, keepdims=True)
            grad_mid = grad_rows + inv_ffn * (scaled_ffn - norm_ffn * inner_ffn)
            grad_attn = (RESIDUAL_SCALE * grad_mid).astype(jnp.bfloat16)
            spread_grad_attn = lax.all_gather(grad_attn, "col", axis=0, tiled=True)
            fresh_out = jnp.einsum(
                "stm,std->md", mixed, spread_grad_attn, preferred_element_type=jnp.float32
            )
            grad_mixed = jnp.einsum(
                "std,md->stm", spread_grad_attn, w_out_all, preferred_element_type=jnp.float32
            ).astype(jnp.bfloat16)
            grad_query_rot, grad_kv_part = lax.map(
                attend_backward,
                (
                    grad_mixed,
                    query_grouped,
                    key_all,
                    value_all,
                    log_total,
                    query_segments[batch_index],
                    segments[batch_index],
                    query_place,
                ),
            )
            grad_kv = lax.psum_scatter(grad_kv_part, "row", scatter_dimension=1, tiled=True)
            grad_query = rotate(
                grad_query_rot.reshape(seq_all, chunk, heads_q, HD), cosine, -sine_part
            )
            grad_key = rotate(grad_kv[..., :HD], cosine, -sine_part)
            grad_qkv = jnp.concatenate(
                [
                    grad_query.reshape(seq_all, chunk, -1),
                    grad_key.reshape(seq_all, chunk, -1),
                    grad_kv[..., HD:].reshape(seq_all, chunk, -1),
                ],
                axis=-1,
            ).astype(jnp.bfloat16)
            fresh_qkv = jnp.einsum(
                "std,stm->dm", spread_attn, grad_qkv, preferred_element_type=jnp.float32
            )
            grad_normed_attn_part = jnp.einsum(
                "stm,dm->std", grad_qkv, w_qkv, preferred_element_type=jnp.float32
            )
            grad_normed_attn = scatter_low(grad_normed_attn_part, "col", 0)
            scaled_attn = grad_normed_attn * gain_attn_all
            gain_attn_total = gain_attn_total + jnp.sum(grad_normed_attn * norm_attn, axis=(0, 1))
            inner_attn = jnp.mean(scaled_attn * norm_attn, axis=-1, keepdims=True)
            inputs_grad.append(grad_mid + inv_attn * (scaled_attn - norm_attn * inner_attn))
            if grad_qkv_w is None:
                grad_qkv_w, grad_out_w = fresh_qkv, fresh_out
                grad_pair_w, grad_down_w = fresh_pair, fresh_down
            else:
                grad_qkv_w = grad_qkv_w + fresh_qkv
                grad_out_w = grad_out_w + fresh_out
                grad_pair_w = grad_pair_w + fresh_pair
                grad_down_w = grad_down_w + fresh_down

        total_pair = reduce_features(grad_pair_w, 0)
        total_down = reduce_features(grad_down_w, 1)
        total_qkv = reduce_features(grad_qkv_w, 0)
        total_out = reduce_features(grad_out_w, 1)
        gain_totals = lax.psum(
            jnp.stack([gain_attn_total, gain_ffn_total]), ("dp", "row", "col")
        )
        gain_totals = lax.dynamic_slice_in_dim(gain_totals, row_index * width_r, width_r, axis=1)
        key_end = query_cols + key_cols
        return (
            to_features(jnp.stack(outs_list)),
            to_features(jnp.stack(inputs_grad)),
            total_qkv[:, :query_cols],
            total_qkv[:, query_cols:key_end],
            total_qkv[:, key_end:],
            total_out,
            total_pair[:, :ffn_cols],
            total_pair[:, ffn_cols:],
            total_down,
            gain_totals[0],
            gain_totals[1],
        )

    return shards


def solution(mesh):
    activation = P(None, ("dp", "col"), None, "row")
    return jax.shard_map(
        make_shards(mesh.shape["dp"], mesh.shape["row"], mesh.shape["col"]),
        mesh=mesh,
        in_specs=(
            activation,
            P(None, ("dp", "row"), None),
            P("row", "col"),
            P("row", "col"),
            P("row", "col"),
            P("col", "row"),
            P("row", "col"),
            P("row", "col"),
            P("col", "row"),
            P("row"),
            P("row"),
            activation,
        ),
        out_specs=(
            activation,
            activation,
            P("row", "col"),
            P("row", "col"),
            P("row", "col"),
            P("col", "row"),
            P("row", "col"),
            P("row", "col"),
            P("col", "row"),
            P("row"),
            P("row"),
        ),
        check_vma=False,
    )
```

```python
import math

import jax
import jax.numpy as jnp
from jax import lax
from jax.sharding import PartitionSpec as P

HD = 64

EPSILON = 1e-05
RESIDUAL_SCALE = 0.22
SCORE_SCALE = 0.015625
ROPE_BASE = 10000000.0
MASKED_SCORE = -1e30


def positions(segment_rows):
    seq_len = segment_rows.shape[-1]
    places = jnp.arange(seq_len, dtype=jnp.int32)
    starts = jnp.concatenate(
        [
            jnp.ones(segment_rows.shape[:-1] + (1,), jnp.bool_),
            segment_rows[..., 1:] != segment_rows[..., :-1],
        ],
        axis=-1,
    )
    first_place = lax.cummax(
        jnp.where(starts, places, jnp.zeros_like(places)), axis=segment_rows.ndim - 1
    )
    return places - first_place


def rotary(place_rows):
    half_dim = HD // 2
    frequency = jnp.exp(jnp.arange(half_dim, dtype=jnp.float32) * (-2.0 * math.log(ROPE_BASE) / HD))
    angles = place_rows.astype(jnp.float32)[..., None] * frequency
    return (jnp.cos(angles)[..., None, :], jnp.sin(angles)[..., None, :])


def rotate(head_rows, cosine, sine_part):
    half_dim = head_rows.shape[-1] // 2
    first_half = head_rows[..., :half_dim]
    second_half = head_rows[..., half_dim:]
    return jnp.concatenate(
        [
            first_half * cosine - second_half * sine_part,
            second_half * cosine + first_half * sine_part,
        ],
        axis=-1,
    )


def masked_scores(query_rot, key_rot, query_segment, key_segment, query_place):
    key_place = jnp.arange(key_segment.shape[0])
    allowed = (query_segment[:, None] == key_segment[None, :]) & (
        query_place[:, None] >= key_place[None, :]
    )
    raw_scores = (
        jnp.einsum("qkgd,pkd->kgqp", query_rot, key_rot, preferred_element_type=jnp.float32)
        * SCORE_SCALE
    )
    return jnp.where(allowed, raw_scores, MASKED_SCORE)


def attend_forward(pieces):
    query_rot, key_all, value_all, query_segment, key_segment, query_place = pieces
    chunk, heads_k, group_count, head_dim = query_rot.shape
    attention_scores = masked_scores(query_rot, key_all, query_segment, key_segment, query_place)
    row_peak = jnp.max(attention_scores, axis=-1, keepdims=True)
    log_total = row_peak + jnp.log(
        jnp.sum(jnp.exp(attention_scores - row_peak), axis=-1, keepdims=True)
    )
    attn_probs = jnp.exp(attention_scores - log_total).astype(jnp.bfloat16)
    mixed = jnp.einsum("kgqp,pkd->qkgd", attn_probs, value_all, preferred_element_type=jnp.float32)
    return mixed.reshape(chunk, -1).astype(jnp.bfloat16), log_total


def attend_backward(pieces):
    grad_mixed, query_rot, key_all, value_all, log_total, query_segment, key_segment, query_place = pieces
    chunk, heads_k, group_count, head_dim = query_rot.shape
    grad_grouped = grad_mixed.reshape(chunk, heads_k, group_count, head_dim)
    attn_probs = jnp.exp(
        masked_scores(query_rot, key_all, query_segment, key_segment, query_place) - log_total
    )
    grad_probs = jnp.einsum(
        "qkgd,pkd->kgqp", grad_grouped, value_all, preferred_element_type=jnp.float32
    )
    grad_value = jnp.einsum(
        "kgqp,qkgd->pkd",
        attn_probs.astype(jnp.bfloat16),
        grad_grouped,
        preferred_element_type=jnp.float32,
    )
    grad_scores = (
        attn_probs * (grad_probs - jnp.sum(attn_probs * grad_probs, axis=-1, keepdims=True))
    ).astype(jnp.bfloat16)
    grad_query = (
        jnp.einsum("kgqp,pkd->qkgd", grad_scores, key_all, preferred_element_type=jnp.float32)
        * SCORE_SCALE
    )
    grad_key = (
        jnp.einsum("kgqp,qkgd->pkd", grad_scores, query_rot, preferred_element_type=jnp.float32)
        * SCORE_SCALE
    )
    return grad_query, jnp.concatenate([grad_key, grad_value], axis=-1)


def scatter_low(partial, axis_name, axis):
    return lax.psum_scatter(
        partial.astype(jnp.bfloat16), axis_name, scatter_dimension=axis, tiled=True
    ).astype(jnp.float32)


def make_shards(n_dp, n_row, n_col):
    assert n_row == n_col
    transpose_pairs = [
        (a * n_col + b, b * n_col + a) for a in range(n_row) for b in range(n_col)
    ]

    def gather_features(block, axis, axis_name):
        count = n_row if axis_name == "row" else n_col
        half = block.shape[axis] // n_dp
        mine = lax.dynamic_slice_in_dim(block, lax.axis_index("dp") * half, half, axis=axis)
        gathered = lax.all_gather(mine, axis_name, axis=axis)
        gathered = lax.all_gather(gathered, "dp", axis=axis)
        gathered = jnp.swapaxes(gathered, axis, axis + 1)
        shape = list(block.shape)
        shape[axis] = block.shape[axis] * count
        return gathered.reshape(shape)

    def reduce_features(partial, axis, axis_name):
        count = n_row if axis_name == "row" else n_col
        half = partial.shape[axis] // (count * n_dp)
        shape = list(partial.shape)
        shape[axis : axis + 1] = [count, n_dp, half]
        split = jnp.swapaxes(partial.reshape(shape), axis, axis + 1)
        split = lax.psum_scatter(split, "dp", scatter_dimension=axis)
        split = lax.psum_scatter(split, axis_name, scatter_dimension=axis)
        return lax.all_gather(split, "dp", axis=axis, tiled=True)

    def transpose_grid(block):
        return lax.ppermute(block, ("row", "col"), transpose_pairs)

    def to_tokens(rows):
        batches, local, seq_len, width = rows.shape
        rows = rows.reshape(batches, local, n_row, seq_len // n_row, width)
        rows = lax.all_to_all(rows, "row", 2, 3)
        return rows.reshape(batches, local, seq_len // n_row, n_row * width)

    def to_features(rows):
        batches, local, chunk, width = rows.shape
        rows = rows.reshape(batches, local, chunk, n_row, width // n_row)
        rows = lax.all_to_all(rows, "row", 3, 2)
        return rows.reshape(batches, local, n_row * chunk, width // n_row)

    def shards(
        hidden_in,
        segment_ids,
        w_query,
        w_key,
        w_value,
        w_out,
        w_gate,
        w_up,
        w_down,
        gain_attn,
        gain_ffn,
        cotangent,
    ):
        batches, local, seq_len, width_r = hidden_in.shape
        chunk = seq_len // n_row
        row_index = lax.axis_index("row")
        col_index = lax.axis_index("col")
        query_cols = w_query.shape[1]
        key_cols = w_key.shape[1]
        key_end = query_cols + key_cols
        qkv_cols = key_end + w_value.shape[1]
        heads_q = query_cols // HD
        heads_k = key_cols // HD
        group_count = heads_q // heads_k
        ffn_cols = w_gate.shape[1]

        w_attn = gather_features(
            transpose_grid(jnp.concatenate([w_query, w_key, w_value, w_out.T], axis=1)), 0, "col"
        )
        w_qkv = w_attn[:, :qkv_cols]
        w_out_heads = w_attn[:, qkv_cols:].T
        w_pair = gather_features(jnp.concatenate([w_gate, w_up], axis=1), 0, "row")
        w_down_all = gather_features(w_down, 1, "row")
        gain_attn_all = lax.all_gather(gain_attn, "row", tiled=True)
        gain_ffn_all = lax.all_gather(gain_ffn, "row", tiled=True)

        segments = lax.all_gather(segment_ids, "row", axis=1, tiled=True)
        segments = lax.dynamic_slice_in_dim(segments, col_index * local, local, axis=1)
        places = positions(segments)
        token_place = jnp.broadcast_to(jnp.arange(seq_len), (local, seq_len))

        hidden_t = to_tokens(hidden_in)
        cotangent_t = to_tokens(cotangent)

        grad_attn_w = None
        grad_pair_w = None
        grad_down_w = None
        gain_attn_total = jnp.zeros(gain_attn_all.shape, jnp.float32)
        gain_ffn_total = jnp.zeros(gain_ffn_all.shape, jnp.float32)
        outs_list = []
        inputs_grad = []
        for batch_index in range(batches):
            rows_f = hidden_t[batch_index].astype(jnp.float32)
            inv_attn = lax.rsqrt(jnp.mean(rows_f * rows_f, axis=-1, keepdims=True) + EPSILON)
            norm_attn = rows_f * inv_attn
            normed_attn = (norm_attn * gain_attn_all).astype(jnp.bfloat16)
            spread_attn = lax.all_gather(normed_attn, "row", axis=1, tiled=True)
            qkv = jnp.einsum(
                "std,dm->stm", spread_attn, w_qkv, preferred_element_type=jnp.float32
            )
            cosine, sine_part = rotary(places[batch_index])
            query_rot = rotate(
                qkv[..., :query_cols].reshape(local, seq_len, heads_q, HD), cosine, sine_part
            ).astype(jnp.bfloat16)
            key_all = rotate(
                qkv[..., query_cols:key_end].reshape(local, seq_len, heads_k, HD),
                cosine,
                sine_part,
            ).astype(jnp.bfloat16)
            value_all = (
                qkv[..., key_end:].reshape(local, seq_len, heads_k, HD).astype(jnp.bfloat16)
            )
            query_grouped = query_rot.reshape(local, seq_len, heads_k, group_count, HD)
            mixed, log_total = lax.map(
                attend_forward,
                (
                    query_grouped,
                    key_all,
                    value_all,
                    segments[batch_index],
                    segments[batch_index],
                    token_place,
                ),
            )
            attn_part = jnp.einsum(
                "stm,md->std", mixed, w_out_heads, preferred_element_type=jnp.float32
            )
            attn_branch = scatter_low(attn_part, "row", 1)
            resid_mid = rows_f + RESIDUAL_SCALE * attn_branch
            inv_ffn = lax.rsqrt(jnp.mean(resid_mid * resid_mid, axis=-1, keepdims=True) + EPSILON)
            norm_ffn = resid_mid * inv_ffn
            normed_ffn = (norm_ffn * gain_ffn_all).astype(jnp.bfloat16)
            spread_ffn = lax.all_gather(normed_ffn, "col", axis=0, tiled=True)
            pair = jnp.einsum(
                "std,df->stf", spread_ffn, w_pair, preferred_element_type=jnp.float32
            )
            gate_rows = pair[..., :ffn_cols]
            up_rows = pair[..., ffn_cols:]
            sigmoid_gate = jax.nn.sigmoid(gate_rows)
            act_low = (gate_rows * sigmoid_gate * up_rows).astype(jnp.bfloat16)
            ffn_part = jnp.einsum(
                "stf,fd->std", act_low, w_down_all, preferred_element_type=jnp.float32
            )
            ffn_branch = scatter_low(ffn_part, "col", 0)
            outs_list.append((resid_mid + RESIDUAL_SCALE * ffn_branch).astype(jnp.bfloat16))

            grad_rows = cotangent_t[batch_index].astype(jnp.float32)
            grad_ffn = (RESIDUAL_SCALE * grad_rows).astype(jnp.bfloat16)
            spread_grad_ffn = lax.all_gather(grad_ffn, "col", axis=0, tiled=True)
            fresh_down = jnp.einsum(
                "stf,std->fd", act_low, spread_grad_ffn, preferred_element_type=jnp.float32
            )
            grad_act = jnp.einsum(
                "std,fd->stf", spread_grad_ffn, w_down_all, preferred_element_type=jnp.float32
            )
            grad_gate_rows = (
                grad_act * up_rows * sigmoid_gate * (1.0 + gate_rows * (1.0 - sigmoid_gate))
            )
            grad_up_rows = grad_act * gate_rows * sigmoid_gate
            paired_gradient = jnp.concatenate([grad_gate_rows, grad_up_rows], axis=-1).astype(
                jnp.bfloat16
            )
            fresh_pair = jnp.einsum(
                "std,stf->df", spread_ffn, paired_gradient, preferred_element_type=jnp.float32
            )
            grad_normed_part = jnp.einsum(
                "stf,df->std", paired_gradient, w_pair, preferred_element_type=jnp.float32
            )
            grad_normed_ffn = scatter_low(grad_normed_part, "col", 0)
            scaled_ffn = grad_normed_ffn * gain_ffn_all
            gain_ffn_total = gain_ffn_total + jnp.sum(grad_normed_ffn * norm_ffn, axis=(0, 1))
            inner_ffn = jnp.mean(scaled_ffn * norm_ffn, axis=-1, keepdims=True)
            grad_mid = grad_rows + inv_ffn * (scaled_ffn - norm_ffn * inner_ffn)
            grad_attn = (RESIDUAL_SCALE * grad_mid).astype(jnp.bfloat16)
            spread_grad_attn = lax.all_gather(grad_attn, "row", axis=1, tiled=True)
            fresh_out = jnp.einsum(
                "std,stm->dm", spread_grad_attn, mixed, preferred_element_type=jnp.float32
            )
            grad_mixed = jnp.einsum(
                "std,md->stm", spread_grad_attn, w_out_heads, preferred_element_type=jnp.float32
            ).astype(jnp.bfloat16)
            grad_query_rot, grad_kv = lax.map(
                attend_backward,
                (
                    grad_mixed,
                    query_grouped,
                    key_all,
                    value_all,
                    log_total,
                    segments[batch_index],
                    segments[batch_index],
                    token_place,
                ),
            )
            grad_query = rotate(
                grad_query_rot.reshape(local, seq_len, heads_q, HD), cosine, -sine_part
            )
            grad_key = rotate(grad_kv[..., :HD], cosine, -sine_part)
            grad_qkv = jnp.concatenate(
                [
                    grad_query.reshape(local, seq_len, -1),
                    grad_key.reshape(local, seq_len, -1),
                    grad_kv[..., HD:].reshape(local, seq_len, -1),
                ],
                axis=-1,
            ).astype(jnp.bfloat16)
            fresh_qkv = jnp.einsum(
                "std,stm->dm", spread_attn, grad_qkv, preferred_element_type=jnp.float32
            )
            grad_normed_attn_part = jnp.einsum(
                "stm,dm->std", grad_qkv, w_qkv, preferred_element_type=jnp.float32
            )
            grad_normed_attn = scatter_low(grad_normed_attn_part, "row", 1)
            scaled_attn = grad_normed_attn * gain_attn_all
            gain_attn_total = gain_attn_total + jnp.sum(grad_normed_attn * norm_attn, axis=(0, 1))
            inner_attn = jnp.mean(scaled_attn * norm_attn, axis=-1, keepdims=True)
            inputs_grad.append(grad_mid + inv_attn * (scaled_attn - norm_attn * inner_attn))
            fresh_attn = jnp.concatenate([fresh_qkv, fresh_out], axis=1)
            if grad_attn_w is None:
                grad_attn_w = fresh_attn
                grad_pair_w, grad_down_w = fresh_pair, fresh_down
            else:
                grad_attn_w = grad_attn_w + fresh_attn
                grad_pair_w = grad_pair_w + fresh_pair
                grad_down_w = grad_down_w + fresh_down

        total_pair = reduce_features(grad_pair_w, 0, "row")
        total_down = reduce_features(grad_down_w, 1, "row")
        total_attn = transpose_grid(reduce_features(grad_attn_w, 0, "col"))
        gain_totals = lax.psum(
            jnp.stack([gain_attn_total, gain_ffn_total]), ("dp", "row", "col")
        )
        gain_totals = lax.dynamic_slice_in_dim(gain_totals, row_index * width_r, width_r, axis=1)
        return (
            to_features(jnp.stack(outs_list)),
            to_features(jnp.stack(inputs_grad)),
            total_attn[:, :query_cols],
            total_attn[:, query_cols:key_end],
            total_attn[:, key_end:qkv_cols],
            total_attn[:, qkv_cols:].T,
            total_pair[:, :ffn_cols],
            total_pair[:, ffn_cols:],
            total_down,
            gain_totals[0],
            gain_totals[1],
        )

    return shards


def solution(mesh):
    activation = P(None, ("dp", "col"), None, "row")
    return jax.shard_map(
        make_shards(mesh.shape["dp"], mesh.shape["row"], mesh.shape["col"]),
        mesh=mesh,
        in_specs=(
            activation,
            P(None, ("dp", "row"), None),
            P("row", "col"),
            P("row", "col"),
            P("row", "col"),
            P("col", "row"),
            P("row", "col"),
            P("row", "col"),
            P("col", "row"),
            P("row"),
            P("row"),
            activation,
        ),
        out_specs=(
            activation,
            activation,
            P("row", "col"),
            P("row", "col"),
            P("row", "col"),
            P("col", "row"),
            P("row", "col"),
            P("row", "col"),
            P("col", "row"),
            P("row"),
            P("row"),
        ),
        check_vma=False,
    )
```

```python
import math

import jax
import jax.numpy as jnp
from jax import lax
from jax.sharding import PartitionSpec as P

HD = 64

EPSILON = 1e-05
RESIDUAL_SCALE = 0.22
SCORE_SCALE = 0.015625
ROPE_BASE = 10000000.0
MASKED_SCORE = -1e30


def positions(segment_rows):
    seq_len = segment_rows.shape[-1]
    places = jnp.arange(seq_len, dtype=jnp.int32)
    starts = jnp.concatenate(
        [
            jnp.ones(segment_rows.shape[:-1] + (1,), jnp.bool_),
            segment_rows[..., 1:] != segment_rows[..., :-1],
        ],
        axis=-1,
    )
    first_place = lax.cummax(
        jnp.where(starts, places, jnp.zeros_like(places)), axis=segment_rows.ndim - 1
    )
    return places - first_place


def rotary(place_rows):
    half_dim = HD // 2
    frequency = jnp.exp(jnp.arange(half_dim, dtype=jnp.float32) * (-2.0 * math.log(ROPE_BASE) / HD))
    angles = place_rows.astype(jnp.float32)[..., None] * frequency
    return (jnp.cos(angles)[..., None, :], jnp.sin(angles)[..., None, :])


def rotate(head_rows, cosine, sine_part):
    half_dim = head_rows.shape[-1] // 2
    first_half = head_rows[..., :half_dim]
    second_half = head_rows[..., half_dim:]
    return jnp.concatenate(
        [
            first_half * cosine - second_half * sine_part,
            second_half * cosine + first_half * sine_part,
        ],
        axis=-1,
    )


def masked_scores(query_rot, key_rot, query_segment, key_segment, query_place):
    key_place = jnp.arange(key_segment.shape[0])
    allowed = (query_segment[:, None] == key_segment[None, :]) & (
        query_place[:, None] >= key_place[None, :]
    )
    raw_scores = (
        jnp.einsum("qkgd,pkd->kgqp", query_rot, key_rot, preferred_element_type=jnp.float32)
        * SCORE_SCALE
    )
    return jnp.where(allowed, raw_scores, MASKED_SCORE)


def attend_forward(pieces):
    query_rot, key_all, value_all, query_segment, key_segment, query_place = pieces
    chunk, heads_k, group_count, head_dim = query_rot.shape
    attention_scores = masked_scores(query_rot, key_all, query_segment, key_segment, query_place)
    row_peak = jnp.max(attention_scores, axis=-1, keepdims=True)
    log_total = row_peak + jnp.log(
        jnp.sum(jnp.exp(attention_scores - row_peak), axis=-1, keepdims=True)
    )
    attn_probs = jnp.exp(attention_scores - log_total).astype(jnp.bfloat16)
    mixed = jnp.einsum("kgqp,pkd->qkgd", attn_probs, value_all, preferred_element_type=jnp.float32)
    return mixed.reshape(chunk, -1).astype(jnp.bfloat16), log_total


def attend_backward(pieces):
    grad_mixed, query_rot, key_all, value_all, log_total, query_segment, key_segment, query_place = pieces
    chunk, heads_k, group_count, head_dim = query_rot.shape
    grad_grouped = grad_mixed.reshape(chunk, heads_k, group_count, head_dim)
    attn_probs = jnp.exp(
        masked_scores(query_rot, key_all, query_segment, key_segment, query_place) - log_total
    )
    grad_probs = jnp.einsum(
        "qkgd,pkd->kgqp", grad_grouped, value_all, preferred_element_type=jnp.float32
    )
    grad_value = jnp.einsum(
        "kgqp,qkgd->pkd",
        attn_probs.astype(jnp.bfloat16),
        grad_grouped,
        preferred_element_type=jnp.float32,
    )
    grad_scores = (
        attn_probs * (grad_probs - jnp.sum(attn_probs * grad_probs, axis=-1, keepdims=True))
    ).astype(jnp.bfloat16)
    grad_query = (
        jnp.einsum("kgqp,pkd->qkgd", grad_scores, key_all, preferred_element_type=jnp.float32)
        * SCORE_SCALE
    )
    grad_key = (
        jnp.einsum("kgqp,qkgd->pkd", grad_scores, query_rot, preferred_element_type=jnp.float32)
        * SCORE_SCALE
    )
    return grad_query, jnp.concatenate([grad_key, grad_value], axis=-1)


def scatter_low(partial, axis_name, axis):
    return lax.psum_scatter(
        partial.astype(jnp.bfloat16), axis_name, scatter_dimension=axis, tiled=True
    ).astype(jnp.float32)


def make_shards(n_dp, n_row, n_col):
    assert n_row == n_col
    transpose_pairs = [
        (a * n_col + b, b * n_col + a) for a in range(n_row) for b in range(n_col)
    ]

    def gather_half(mine, axis, axis_name):
        count = n_row if axis_name == "row" else n_col
        gathered = lax.all_gather(mine, axis_name, axis=axis)
        gathered = lax.all_gather(gathered, "dp", axis=axis)
        gathered = jnp.swapaxes(gathered, axis, axis + 1)
        shape = list(mine.shape)
        shape[axis] = mine.shape[axis] * count * n_dp
        return gathered.reshape(shape)

    def own_half(block, axis):
        half = block.shape[axis] // n_dp
        return lax.dynamic_slice_in_dim(block, lax.axis_index("dp") * half, half, axis=axis)

    def gather_features(block, axis, axis_name):
        return gather_half(own_half(block, axis), axis, axis_name)

    def reduce_half(partial, axis, axis_name):
        count = n_row if axis_name == "row" else n_col
        half = partial.shape[axis] // (count * n_dp)
        shape = list(partial.shape)
        shape[axis : axis + 1] = [count, n_dp, half]
        split = jnp.swapaxes(partial.reshape(shape), axis, axis + 1)
        split = lax.psum_scatter(split, "dp", scatter_dimension=axis)
        return lax.psum_scatter(split, axis_name, scatter_dimension=axis)

    def reduce_features(partial, axis, axis_name):
        return lax.all_gather(reduce_half(partial, axis, axis_name), "dp", axis=axis, tiled=True)

    def transpose_grid(block):
        return lax.ppermute(block, ("row", "col"), transpose_pairs)

    def to_tokens(rows):
        batches, local, seq_len, width = rows.shape
        rows = rows.reshape(batches, local, n_row, seq_len // n_row, width)
        rows = lax.all_to_all(rows, "row", 2, 3)
        return rows.reshape(batches, local, seq_len // n_row, n_row * width)

    def to_features(rows):
        batches, local, chunk, width = rows.shape
        rows = rows.reshape(batches, local, chunk, n_row, width // n_row)
        rows = lax.all_to_all(rows, "row", 3, 2)
        return rows.reshape(batches, local, n_row * chunk, width // n_row)

    def shards(
        hidden_in,
        segment_ids,
        w_query,
        w_key,
        w_value,
        w_out,
        w_gate,
        w_up,
        w_down,
        gain_attn,
        gain_ffn,
        cotangent,
    ):
        batches, local, seq_len, width_r = hidden_in.shape
        chunk = seq_len // n_row
        row_index = lax.axis_index("row")
        col_index = lax.axis_index("col")
        query_cols = w_query.shape[1]
        key_cols = w_key.shape[1]
        key_end = query_cols + key_cols
        qkv_cols = key_end + w_value.shape[1]
        heads_q = query_cols // HD
        heads_k = key_cols // HD
        group_count = heads_q // heads_k
        ffn_cols = w_gate.shape[1]

        w_attn = gather_half(
            transpose_grid(own_half(jnp.concatenate([w_query, w_key, w_value, w_out.T], axis=1), 0)),
            0,
            "col",
        )
        w_qkv = w_attn[:, :qkv_cols]
        w_out_heads = w_attn[:, qkv_cols:].T
        w_pair = gather_features(jnp.concatenate([w_gate, w_up], axis=1), 0, "row")
        w_down_all = gather_features(w_down, 1, "row")
        gain_attn_all = lax.all_gather(gain_attn, "row", tiled=True)
        gain_ffn_all = lax.all_gather(gain_ffn, "row", tiled=True)

        segments = lax.all_gather(segment_ids, "row", axis=1, tiled=True)
        segments = lax.dynamic_slice_in_dim(segments, col_index * local, local, axis=1)
        places = positions(segments)
        token_place = jnp.broadcast_to(jnp.arange(seq_len), (local, seq_len))

        hidden_t = to_tokens(hidden_in)
        cotangent_t = to_tokens(cotangent)

        grad_attn_w = None
        grad_pair_w = None
        grad_down_w = None
        gain_attn_total = jnp.zeros(gain_attn_all.shape, jnp.float32)
        gain_ffn_total = jnp.zeros(gain_ffn_all.shape, jnp.float32)
        outs_list = []
        inputs_grad = []
        for batch_index in range(batches):
            rows_f = hidden_t[batch_index].astype(jnp.float32)
            inv_attn = lax.rsqrt(jnp.mean(rows_f * rows_f, axis=-1, keepdims=True) + EPSILON)
            norm_attn = rows_f * inv_attn
            normed_attn = (norm_attn * gain_attn_all).astype(jnp.bfloat16)
            spread_attn = lax.all_gather(normed_attn, "row", axis=1, tiled=True)
            qkv = jnp.einsum(
                "std,dm->stm", spread_attn, w_qkv, preferred_element_type=jnp.float32
            )
            cosine, sine_part = rotary(places[batch_index])
            query_rot = rotate(
                qkv[..., :query_cols].reshape(local, seq_len, heads_q, HD), cosine, sine_part
            ).astype(jnp.bfloat16)
            key_all = rotate(
                qkv[..., query_cols:key_end].reshape(local, seq_len, heads_k, HD),
                cosine,
                sine_part,
            ).astype(jnp.bfloat16)
            value_all = (
                qkv[..., key_end:].reshape(local, seq_len, heads_k, HD).astype(jnp.bfloat16)
            )
            query_grouped = query_rot.reshape(local, seq_len, heads_k, group_count, HD)
            mixed, log_total = lax.map(
                attend_forward,
                (
                    query_grouped,
                    key_all,
                    value_all,
                    segments[batch_index],
                    segments[batch_index],
                    token_place,
                ),
            )
            attn_part = jnp.einsum(
                "stm,md->std", mixed, w_out_heads, preferred_element_type=jnp.float32
            )
            attn_branch = scatter_low(attn_part, "row", 1)
            resid_mid = rows_f + RESIDUAL_SCALE * attn_branch
            inv_ffn = lax.rsqrt(jnp.mean(resid_mid * resid_mid, axis=-1, keepdims=True) + EPSILON)
            norm_ffn = resid_mid * inv_ffn
            normed_ffn = (norm_ffn * gain_ffn_all).astype(jnp.bfloat16)
            spread_ffn = lax.all_gather(normed_ffn, "col", axis=0, tiled=True)
            pair = jnp.einsum(
                "std,df->stf", spread_ffn, w_pair, preferred_element_type=jnp.float32
            )
            gate_rows = pair[..., :ffn_cols]
            up_rows = pair[..., ffn_cols:]
            sigmoid_gate = jax.nn.sigmoid(gate_rows)
            act_low = (gate_rows * sigmoid_gate * up_rows).astype(jnp.bfloat16)
            ffn_part = jnp.einsum(
                "stf,fd->std", act_low, w_down_all, preferred_element_type=jnp.float32
            )
            ffn_branch = scatter_low(ffn_part, "col", 0)
            outs_list.append(
                to_features((resid_mid + RESIDUAL_SCALE * ffn_branch).astype(jnp.bfloat16)[None])
            )

            grad_rows = cotangent_t[batch_index].astype(jnp.float32)
            grad_ffn = (RESIDUAL_SCALE * grad_rows).astype(jnp.bfloat16)
            spread_grad_ffn = lax.all_gather(grad_ffn, "col", axis=0, tiled=True)
            fresh_down = jnp.einsum(
                "stf,std->fd", act_low, spread_grad_ffn, preferred_element_type=jnp.float32
            )
            grad_act = jnp.einsum(
                "std,fd->stf", spread_grad_ffn, w_down_all, preferred_element_type=jnp.float32
            )
            grad_gate_rows = (
                grad_act * up_rows * sigmoid_gate * (1.0 + gate_rows * (1.0 - sigmoid_gate))
            )
            grad_up_rows = grad_act * gate_rows * sigmoid_gate
            paired_gradient = jnp.concatenate([grad_gate_rows, grad_up_rows], axis=-1).astype(
                jnp.bfloat16
            )
            fresh_pair = jnp.einsum(
                "std,stf->df", spread_ffn, paired_gradient, preferred_element_type=jnp.float32
            )
            grad_normed_part = jnp.einsum(
                "stf,df->std", paired_gradient, w_pair, preferred_element_type=jnp.float32
            )
            grad_normed_ffn = scatter_low(grad_normed_part, "col", 0)
            scaled_ffn = grad_normed_ffn * gain_ffn_all
            gain_ffn_total = gain_ffn_total + jnp.sum(grad_normed_ffn * norm_ffn, axis=(0, 1))
            inner_ffn = jnp.mean(scaled_ffn * norm_ffn, axis=-1, keepdims=True)
            grad_mid = grad_rows + inv_ffn * (scaled_ffn - norm_ffn * inner_ffn)
            grad_attn = (RESIDUAL_SCALE * grad_mid).astype(jnp.bfloat16)
            spread_grad_attn = lax.all_gather(grad_attn, "row", axis=1, tiled=True)
            fresh_out = jnp.einsum(
                "std,stm->dm", spread_grad_attn, mixed, preferred_element_type=jnp.float32
            )
            grad_mixed = jnp.einsum(
                "std,md->stm", spread_grad_attn, w_out_heads, preferred_element_type=jnp.float32
            ).astype(jnp.bfloat16)
            grad_query_rot, grad_kv = lax.map(
                attend_backward,
                (
                    grad_mixed,
                    query_grouped,
                    key_all,
                    value_all,
                    log_total,
                    segments[batch_index],
                    segments[batch_index],
                    token_place,
                ),
            )
            grad_query = rotate(
                grad_query_rot.reshape(local, seq_len, heads_q, HD), cosine, -sine_part
            )
            grad_key = rotate(grad_kv[..., :HD], cosine, -sine_part)
            grad_qkv = jnp.concatenate(
                [
                    grad_query.reshape(local, seq_len, -1),
                    grad_key.reshape(local, seq_len, -1),
                    grad_kv[..., HD:].reshape(local, seq_len, -1),
                ],
                axis=-1,
            ).astype(jnp.bfloat16)
            fresh_qkv = jnp.einsum(
                "std,stm->dm", spread_attn, grad_qkv, preferred_element_type=jnp.float32
            )
            grad_normed_attn_part = jnp.einsum(
                "stm,dm->std", grad_qkv, w_qkv, preferred_element_type=jnp.float32
            )
            grad_normed_attn = scatter_low(grad_normed_attn_part, "row", 1)
            scaled_attn = grad_normed_attn * gain_attn_all
            gain_attn_total = gain_attn_total + jnp.sum(grad_normed_attn * norm_attn, axis=(0, 1))
            inner_attn = jnp.mean(scaled_attn * norm_attn, axis=-1, keepdims=True)
            inputs_grad.append(
                to_features((grad_mid + inv_attn * (scaled_attn - norm_attn * inner_attn))[None])
            )
            fresh_attn = jnp.concatenate([fresh_qkv, fresh_out], axis=1)
            if grad_attn_w is None:
                grad_attn_w = fresh_attn
                grad_pair_w, grad_down_w = fresh_pair, fresh_down
            else:
                grad_attn_w = grad_attn_w + fresh_attn
                grad_pair_w = grad_pair_w + fresh_pair
                grad_down_w = grad_down_w + fresh_down

        total_pair = reduce_features(grad_pair_w, 0, "row")
        total_down = reduce_features(grad_down_w, 1, "row")
        gain_rows = lax.psum(jnp.stack([gain_attn_total, gain_ffn_total], axis=1), "row")
        gain_cols = jnp.pad(gain_rows, ((0, 0), (0, 126)))
        total_attn = lax.all_gather(
            transpose_grid(
                reduce_half(jnp.concatenate([grad_attn_w, gain_cols], axis=1), 0, "col")
            ),
            "dp",
            axis=0,
            tiled=True,
        )
        attn_cols = qkv_cols + w_out.shape[0]
        return (
            jnp.concatenate(outs_list),
            jnp.concatenate(inputs_grad),
            total_attn[:, :query_cols],
            total_attn[:, query_cols:key_end],
            total_attn[:, key_end:qkv_cols],
            total_attn[:, qkv_cols:attn_cols].T,
            total_pair[:, :ffn_cols],
            total_pair[:, ffn_cols:],
            total_down,
            total_attn[:, attn_cols],
            total_attn[:, attn_cols + 1],
        )

    return shards


def solution(mesh):
    activation = P(None, ("dp", "col"), None, "row")
    return jax.shard_map(
        make_shards(mesh.shape["dp"], mesh.shape["row"], mesh.shape["col"]),
        mesh=mesh,
        in_specs=(
            activation,
            P(None, ("dp", "row"), None),
            P("row", "col"),
            P("row", "col"),
            P("row", "col"),
            P("col", "row"),
            P("row", "col"),
            P("row", "col"),
            P("col", "row"),
            P("row"),
            P("row"),
            activation,
        ),
        out_specs=(
            activation,
            activation,
            P("row", "col"),
            P("row", "col"),
            P("row", "col"),
            P("col", "row"),
            P("row", "col"),
            P("row", "col"),
            P("col", "row"),
            P("row"),
            P("row"),
        ),
        check_vma=False,
    )
```

```python
import math

import jax
import jax.numpy as jnp
from jax import lax
from jax.sharding import PartitionSpec as P

HD = 64

EPSILON = 1e-05
RESIDUAL_SCALE = 0.22
SCORE_SCALE = 0.015625
ROPE_BASE = 10000000.0
MASKED_SCORE = -1e30


def positions(segment_rows):
    seq_len = segment_rows.shape[-1]
    places = jnp.arange(seq_len, dtype=jnp.int32)
    starts = jnp.concatenate(
        [
            jnp.ones(segment_rows.shape[:-1] + (1,), jnp.bool_),
            segment_rows[..., 1:] != segment_rows[..., :-1],
        ],
        axis=-1,
    )
    first_place = lax.cummax(
        jnp.where(starts, places, jnp.zeros_like(places)), axis=segment_rows.ndim - 1
    )
    return places - first_place


def rotary(place_rows):
    half_dim = HD // 2
    frequency = jnp.exp(jnp.arange(half_dim, dtype=jnp.float32) * (-2.0 * math.log(ROPE_BASE) / HD))
    angles = place_rows.astype(jnp.float32)[..., None] * frequency
    return (jnp.cos(angles)[..., None, :], jnp.sin(angles)[..., None, :])


def rotate(head_rows, cosine, sine_part):
    half_dim = head_rows.shape[-1] // 2
    first_half = head_rows[..., :half_dim]
    second_half = head_rows[..., half_dim:]
    return jnp.concatenate(
        [
            first_half * cosine - second_half * sine_part,
            second_half * cosine + first_half * sine_part,
        ],
        axis=-1,
    )


def masked_scores(query_rot, key_rot, query_segment, key_segment, query_place):
    key_place = jnp.arange(key_segment.shape[0])
    allowed = (query_segment[:, None] == key_segment[None, :]) & (
        query_place[:, None] >= key_place[None, :]
    )
    raw_scores = (
        jnp.einsum("qkgd,pkd->kgqp", query_rot, key_rot, preferred_element_type=jnp.float32)
        * SCORE_SCALE
    )
    return jnp.where(allowed, raw_scores, MASKED_SCORE)


def attend_forward(pieces):
    query_rot, key_all, value_all, query_segment, key_segment, query_place = pieces
    chunk, heads_k, group_count, head_dim = query_rot.shape
    attention_scores = masked_scores(query_rot, key_all, query_segment, key_segment, query_place)
    row_peak = jnp.max(attention_scores, axis=-1, keepdims=True)
    log_total = row_peak + jnp.log(
        jnp.sum(jnp.exp(attention_scores - row_peak), axis=-1, keepdims=True)
    )
    attn_probs = jnp.exp(attention_scores - log_total).astype(jnp.bfloat16)
    mixed = jnp.einsum("kgqp,pkd->qkgd", attn_probs, value_all, preferred_element_type=jnp.float32)
    return mixed.reshape(chunk, -1).astype(jnp.bfloat16), log_total


def attend_backward(pieces):
    grad_mixed, query_rot, key_all, value_all, log_total, query_segment, key_segment, query_place = pieces
    chunk, heads_k, group_count, head_dim = query_rot.shape
    grad_grouped = grad_mixed.reshape(chunk, heads_k, group_count, head_dim)
    attn_probs = jnp.exp(
        masked_scores(query_rot, key_all, query_segment, key_segment, query_place) - log_total
    )
    grad_probs = jnp.einsum(
        "qkgd,pkd->kgqp", grad_grouped, value_all, preferred_element_type=jnp.float32
    )
    grad_value = jnp.einsum(
        "kgqp,qkgd->pkd",
        attn_probs.astype(jnp.bfloat16),
        grad_grouped,
        preferred_element_type=jnp.float32,
    )
    grad_scores = (
        attn_probs * (grad_probs - jnp.sum(attn_probs * grad_probs, axis=-1, keepdims=True))
    ).astype(jnp.bfloat16)
    grad_query = (
        jnp.einsum("kgqp,pkd->qkgd", grad_scores, key_all, preferred_element_type=jnp.float32)
        * SCORE_SCALE
    )
    grad_key = (
        jnp.einsum("kgqp,qkgd->pkd", grad_scores, query_rot, preferred_element_type=jnp.float32)
        * SCORE_SCALE
    )
    return grad_query, jnp.concatenate([grad_key, grad_value], axis=-1)


def scatter_low(partial, axis_name, axis):
    return lax.psum_scatter(
        partial.astype(jnp.bfloat16), axis_name, scatter_dimension=axis, tiled=True
    ).astype(jnp.float32)


def make_shards(n_dp, n_row, n_col):
    assert n_row == n_col
    transpose_pairs = [
        (a * n_col + b, b * n_col + a) for a in range(n_row) for b in range(n_col)
    ]

    def gather_half(mine, axis, axis_name):
        count = n_row if axis_name == "row" else n_col
        gathered = lax.all_gather(mine, axis_name, axis=axis)
        gathered = lax.all_gather(gathered, "dp", axis=axis)
        gathered = jnp.swapaxes(gathered, axis, axis + 1)
        shape = list(mine.shape)
        shape[axis] = mine.shape[axis] * count * n_dp
        return gathered.reshape(shape)

    def own_half(block, axis):
        half = block.shape[axis] // n_dp
        return lax.dynamic_slice_in_dim(block, lax.axis_index("dp") * half, half, axis=axis)

    def gather_features(block, axis, axis_name):
        return gather_half(own_half(block, axis), axis, axis_name)

    def reduce_half(partial, axis, axis_name):
        count = n_row if axis_name == "row" else n_col
        half = partial.shape[axis] // (count * n_dp)
        shape = list(partial.shape)
        shape[axis : axis + 1] = [count, n_dp, half]
        split = jnp.swapaxes(partial.reshape(shape), axis, axis + 1)
        split = lax.psum_scatter(split, "dp", scatter_dimension=axis)
        return lax.psum_scatter(
            split.astype(jnp.bfloat16), axis_name, scatter_dimension=axis
        ).astype(jnp.float32)

    def reduce_features(partial, axis, axis_name):
        return lax.all_gather(reduce_half(partial, axis, axis_name), "dp", axis=axis, tiled=True)

    def transpose_grid(block):
        return lax.ppermute(block, ("row", "col"), transpose_pairs)

    def to_tokens(rows):
        batches, local, seq_len, width = rows.shape
        rows = rows.reshape(batches, local, n_row, seq_len // n_row, width)
        rows = lax.all_to_all(rows, "row", 2, 3)
        return rows.reshape(batches, local, seq_len // n_row, n_row * width)

    def to_features(rows):
        batches, local, chunk, width = rows.shape
        rows = rows.reshape(batches, local, chunk, n_row, width // n_row)
        rows = lax.all_to_all(rows, "row", 3, 2)
        return rows.reshape(batches, local, n_row * chunk, width // n_row)

    def shards(
        hidden_in,
        segment_ids,
        w_query,
        w_key,
        w_value,
        w_out,
        w_gate,
        w_up,
        w_down,
        gain_attn,
        gain_ffn,
        cotangent,
    ):
        batches, local, seq_len, width_r = hidden_in.shape
        chunk = seq_len // n_row
        row_index = lax.axis_index("row")
        col_index = lax.axis_index("col")
        query_cols = w_query.shape[1]
        key_cols = w_key.shape[1]
        key_end = query_cols + key_cols
        qkv_cols = key_end + w_value.shape[1]
        heads_q = query_cols // HD
        heads_k = key_cols // HD
        group_count = heads_q // heads_k
        ffn_cols = w_gate.shape[1]

        w_attn = gather_half(
            transpose_grid(own_half(jnp.concatenate([w_query, w_key, w_value, w_out.T], axis=1), 0)),
            0,
            "col",
        )
        w_qkv = w_attn[:, :qkv_cols]
        w_out_heads = w_attn[:, qkv_cols:].T
        w_pair = gather_features(jnp.concatenate([w_gate, w_up], axis=1), 0, "row")
        w_down_all = gather_features(w_down, 1, "row")
        gain_attn_all = lax.all_gather(gain_attn, "row", tiled=True)
        gain_ffn_all = lax.all_gather(gain_ffn, "row", tiled=True)

        segments = lax.all_gather(segment_ids, "row", axis=1, tiled=True)
        segments = lax.dynamic_slice_in_dim(segments, col_index * local, local, axis=1)
        places = positions(segments)
        token_place = jnp.broadcast_to(jnp.arange(seq_len), (local, seq_len))

        hidden_t = to_tokens(hidden_in)
        cotangent_t = to_tokens(cotangent)

        grad_attn_w = None
        grad_pair_w = None
        grad_down_w = None
        gain_attn_total = jnp.zeros(gain_attn_all.shape, jnp.float32)
        gain_ffn_total = jnp.zeros(gain_ffn_all.shape, jnp.float32)
        outs_list = []
        inputs_grad = []
        for batch_index in range(batches):
            rows_f = hidden_t[batch_index].astype(jnp.float32)
            inv_attn = lax.rsqrt(jnp.mean(rows_f * rows_f, axis=-1, keepdims=True) + EPSILON)
            norm_attn = rows_f * inv_attn
            normed_attn = (norm_attn * gain_attn_all).astype(jnp.bfloat16)
            spread_attn = lax.all_gather(normed_attn, "row", axis=1, tiled=True)
            qkv = jnp.einsum(
                "std,dm->stm", spread_attn, w_qkv, preferred_element_type=jnp.float32
            )
            cosine, sine_part = rotary(places[batch_index])
            query_rot = rotate(
                qkv[..., :query_cols].reshape(local, seq_len, heads_q, HD), cosine, sine_part
            ).astype(jnp.bfloat16)
            key_all = rotate(
                qkv[..., query_cols:key_end].reshape(local, seq_len, heads_k, HD),
                cosine,
                sine_part,
            ).astype(jnp.bfloat16)
            value_all = (
                qkv[..., key_end:].reshape(local, seq_len, heads_k, HD).astype(jnp.bfloat16)
            )
            query_grouped = query_rot.reshape(local, seq_len, heads_k, group_count, HD)
            mixed, log_total = lax.map(
                attend_forward,
                (
                    query_grouped,
                    key_all,
                    value_all,
                    segments[batch_index],
                    segments[batch_index],
                    token_place,
                ),
            )
            attn_part = jnp.einsum(
                "stm,md->std", mixed, w_out_heads, preferred_element_type=jnp.float32
            )
            attn_branch = scatter_low(attn_part, "row", 1)
            resid_mid = rows_f + RESIDUAL_SCALE * attn_branch
            inv_ffn = lax.rsqrt(jnp.mean(resid_mid * resid_mid, axis=-1, keepdims=True) + EPSILON)
            norm_ffn = resid_mid * inv_ffn
            normed_ffn = (norm_ffn * gain_ffn_all).astype(jnp.bfloat16)
            spread_ffn = lax.all_gather(normed_ffn, "col", axis=0, tiled=True)
            pair = jnp.einsum(
                "std,df->stf", spread_ffn, w_pair, preferred_element_type=jnp.float32
            )
            gate_rows = pair[..., :ffn_cols]
            up_rows = pair[..., ffn_cols:]
            sigmoid_gate = jax.nn.sigmoid(gate_rows)
            act_low = (gate_rows * sigmoid_gate * up_rows).astype(jnp.bfloat16)
            ffn_part = jnp.einsum(
                "stf,fd->std", act_low, w_down_all, preferred_element_type=jnp.float32
            )
            ffn_branch = scatter_low(ffn_part, "col", 0)
            block_out = (resid_mid + RESIDUAL_SCALE * ffn_branch).astype(jnp.bfloat16)
            block_out, cotangent_here = lax.optimization_barrier(
                (block_out, cotangent_t[batch_index])
            )
            outs_list.append(to_features(block_out[None]))

            grad_rows = cotangent_here.astype(jnp.float32)
            grad_ffn = (RESIDUAL_SCALE * grad_rows).astype(jnp.bfloat16)
            spread_grad_ffn = lax.all_gather(grad_ffn, "col", axis=0, tiled=True)
            fresh_down = jnp.einsum(
                "stf,std->fd", act_low, spread_grad_ffn, preferred_element_type=jnp.float32
            )
            grad_act = jnp.einsum(
                "std,fd->stf", spread_grad_ffn, w_down_all, preferred_element_type=jnp.float32
            )
            grad_gate_rows = (
                grad_act * up_rows * sigmoid_gate * (1.0 + gate_rows * (1.0 - sigmoid_gate))
            )
            grad_up_rows = grad_act * gate_rows * sigmoid_gate
            paired_gradient = jnp.concatenate([grad_gate_rows, grad_up_rows], axis=-1).astype(
                jnp.bfloat16
            )
            fresh_pair = jnp.einsum(
                "std,stf->df", spread_ffn, paired_gradient, preferred_element_type=jnp.float32
            )
            grad_normed_part = jnp.einsum(
                "stf,df->std", paired_gradient, w_pair, preferred_element_type=jnp.float32
            )
            grad_normed_ffn = scatter_low(grad_normed_part, "col", 0)
            scaled_ffn = grad_normed_ffn * gain_ffn_all
            gain_ffn_total = gain_ffn_total + jnp.sum(grad_normed_ffn * norm_ffn, axis=(0, 1))
            inner_ffn = jnp.mean(scaled_ffn * norm_ffn, axis=-1, keepdims=True)
            grad_mid = grad_rows + inv_ffn * (scaled_ffn - norm_ffn * inner_ffn)
            grad_attn = (RESIDUAL_SCALE * grad_mid).astype(jnp.bfloat16)
            spread_grad_attn = lax.all_gather(grad_attn, "row", axis=1, tiled=True)
            fresh_out = jnp.einsum(
                "std,stm->dm", spread_grad_attn, mixed, preferred_element_type=jnp.float32
            )
            grad_mixed = jnp.einsum(
                "std,md->stm", spread_grad_attn, w_out_heads, preferred_element_type=jnp.float32
            ).astype(jnp.bfloat16)
            grad_query_rot, grad_kv = lax.map(
                attend_backward,
                (
                    grad_mixed,
                    query_grouped,
                    key_all,
                    value_all,
                    log_total,
                    segments[batch_index],
                    segments[batch_index],
                    token_place,
                ),
            )
            grad_query = rotate(
                grad_query_rot.reshape(local, seq_len, heads_q, HD), cosine, -sine_part
            )
            grad_key = rotate(grad_kv[..., :HD], cosine, -sine_part)
            grad_qkv = jnp.concatenate(
                [
                    grad_query.reshape(local, seq_len, -1),
                    grad_key.reshape(local, seq_len, -1),
                    grad_kv[..., HD:].reshape(local, seq_len, -1),
                ],
                axis=-1,
            ).astype(jnp.bfloat16)
            fresh_qkv = jnp.einsum(
                "std,stm->dm", spread_attn, grad_qkv, preferred_element_type=jnp.float32
            )
            grad_normed_attn_part = jnp.einsum(
                "stm,dm->std", grad_qkv, w_qkv, preferred_element_type=jnp.float32
            )
            grad_normed_attn = scatter_low(grad_normed_attn_part, "row", 1)
            scaled_attn = grad_normed_attn * gain_attn_all
            gain_attn_total = gain_attn_total + jnp.sum(grad_normed_attn * norm_attn, axis=(0, 1))
            inner_attn = jnp.mean(scaled_attn * norm_attn, axis=-1, keepdims=True)
            inputs_grad.append(
                to_features((grad_mid + inv_attn * (scaled_attn - norm_attn * inner_attn))[None])
            )
            fresh_attn = jnp.concatenate([fresh_qkv, fresh_out], axis=1)
            if grad_attn_w is None:
                grad_attn_w = fresh_attn
                grad_pair_w, grad_down_w = fresh_pair, fresh_down
            else:
                grad_attn_w = grad_attn_w + fresh_attn
                grad_pair_w = grad_pair_w + fresh_pair
                grad_down_w = grad_down_w + fresh_down

        total_pair = reduce_features(grad_pair_w, 0, "row")
        total_down = reduce_features(grad_down_w, 1, "row")
        gain_rows = lax.psum(jnp.stack([gain_attn_total, gain_ffn_total], axis=1), "row")
        gain_cols = jnp.pad(gain_rows, ((0, 0), (0, 126)))
        total_attn = lax.all_gather(
            transpose_grid(
                reduce_half(jnp.concatenate([grad_attn_w, gain_cols], axis=1), 0, "col")
            ),
            "dp",
            axis=0,
            tiled=True,
        )
        attn_cols = qkv_cols + w_out.shape[0]
        return (
            jnp.concatenate(outs_list),
            jnp.concatenate(inputs_grad),
            total_attn[:, :query_cols],
            total_attn[:, query_cols:key_end],
            total_attn[:, key_end:qkv_cols],
            total_attn[:, qkv_cols:attn_cols].T,
            total_pair[:, :ffn_cols],
            total_pair[:, ffn_cols:],
            total_down,
            total_attn[:, attn_cols],
            total_attn[:, attn_cols + 1],
        )

    return shards


def solution(mesh):
    activation = P(None, ("dp", "col"), None, "row")
    return jax.shard_map(
        make_shards(mesh.shape["dp"], mesh.shape["row"], mesh.shape["col"]),
        mesh=mesh,
        in_specs=(
            activation,
            P(None, ("dp", "row"), None),
            P("row", "col"),
            P("row", "col"),
            P("row", "col"),
            P("col", "row"),
            P("row", "col"),
            P("row", "col"),
            P("col", "row"),
            P("row"),
            P("row"),
            activation,
        ),
        out_specs=(
            activation,
            activation,
            P("row", "col"),
            P("row", "col"),
            P("row", "col"),
            P("col", "row"),
            P("row", "col"),
            P("row", "col"),
            P("col", "row"),
            P("row"),
            P("row"),
        ),
        check_vma=False,
    )
```

```python
import math

import jax
import jax.numpy as jnp
from jax import lax
from jax.sharding import PartitionSpec as P

HD = 64

EPSILON = 1e-05
RESIDUAL_SCALE = 0.22
SCORE_SCALE = 0.015625
ROPE_BASE = 10000000.0
MASKED_SCORE = -1e30


def positions(segment_rows):
    seq_len = segment_rows.shape[-1]
    places = jnp.arange(seq_len, dtype=jnp.int32)
    starts = jnp.concatenate(
        [
            jnp.ones(segment_rows.shape[:-1] + (1,), jnp.bool_),
            segment_rows[..., 1:] != segment_rows[..., :-1],
        ],
        axis=-1,
    )
    first_place = lax.cummax(
        jnp.where(starts, places, jnp.zeros_like(places)), axis=segment_rows.ndim - 1
    )
    return places - first_place


def rotary(place_rows):
    half_dim = HD // 2
    frequency = jnp.exp(jnp.arange(half_dim, dtype=jnp.float32) * (-2.0 * math.log(ROPE_BASE) / HD))
    angles = place_rows.astype(jnp.float32)[..., None] * frequency
    return (jnp.cos(angles)[..., None, :], jnp.sin(angles)[..., None, :])


def rotate(head_rows, cosine, sine_part):
    half_dim = head_rows.shape[-1] // 2
    first_half = head_rows[..., :half_dim]
    second_half = head_rows[..., half_dim:]
    return jnp.concatenate(
        [
            first_half * cosine - second_half * sine_part,
            second_half * cosine + first_half * sine_part,
        ],
        axis=-1,
    )


def masked_scores(query_rot, key_rot, query_segment, key_segment, query_place):
    key_place = jnp.arange(key_segment.shape[0])
    allowed = (query_segment[:, None] == key_segment[None, :]) & (
        query_place[:, None] >= key_place[None, :]
    )
    raw_scores = (
        jnp.einsum("qkgd,pkd->kgqp", query_rot, key_rot, preferred_element_type=jnp.float32)
        * SCORE_SCALE
    )
    return jnp.where(allowed, raw_scores, MASKED_SCORE)


def attend_forward(pieces):
    query_rot, key_all, value_all, query_segment, key_segment, query_place = pieces
    chunk, heads_k, group_count, head_dim = query_rot.shape
    attention_scores = masked_scores(query_rot, key_all, query_segment, key_segment, query_place)
    row_peak = jnp.max(attention_scores, axis=-1, keepdims=True)
    log_total = row_peak + jnp.log(
        jnp.sum(jnp.exp(attention_scores - row_peak), axis=-1, keepdims=True)
    )
    attn_probs = jnp.exp(attention_scores - log_total).astype(jnp.bfloat16)
    mixed = jnp.einsum("kgqp,pkd->qkgd", attn_probs, value_all, preferred_element_type=jnp.float32)
    return mixed.reshape(chunk, -1).astype(jnp.bfloat16), log_total


def attend_backward(pieces):
    grad_mixed, query_rot, key_all, value_all, log_total, query_segment, key_segment, query_place = pieces
    chunk, heads_k, group_count, head_dim = query_rot.shape
    grad_grouped = grad_mixed.reshape(chunk, heads_k, group_count, head_dim)
    attn_probs = jnp.exp(
        masked_scores(query_rot, key_all, query_segment, key_segment, query_place) - log_total
    )
    grad_probs = jnp.einsum(
        "qkgd,pkd->kgqp", grad_grouped, value_all, preferred_element_type=jnp.float32
    )
    grad_value = jnp.einsum(
        "kgqp,qkgd->pkd",
        attn_probs.astype(jnp.bfloat16),
        grad_grouped,
        preferred_element_type=jnp.float32,
    )
    grad_scores = (
        attn_probs * (grad_probs - jnp.sum(attn_probs * grad_probs, axis=-1, keepdims=True))
    ).astype(jnp.bfloat16)
    grad_query = (
        jnp.einsum("kgqp,pkd->qkgd", grad_scores, key_all, preferred_element_type=jnp.float32)
        * SCORE_SCALE
    )
    grad_key = (
        jnp.einsum("kgqp,qkgd->pkd", grad_scores, query_rot, preferred_element_type=jnp.float32)
        * SCORE_SCALE
    )
    return grad_query, jnp.concatenate([grad_key, grad_value], axis=-1)


def scatter_low(partial, axis_name, axis):
    return lax.psum_scatter(
        partial.astype(jnp.bfloat16), axis_name, scatter_dimension=axis, tiled=True
    ).astype(jnp.float32)


def run_interleaved(streams):
    pending = {}
    finished = {}

    def feed(index, value):
        try:
            pending[index] = streams[index].send(value)
        except StopIteration as stop:
            finished[index] = stop.value

    for index in range(len(streams)):
        feed(index, None)
    previous = None
    while len(finished) < len(streams):
        for index in range(len(streams)):
            if index in finished:
                continue
            if previous is not None and previous[0] == index:
                feed(index, previous[1])
                previous = None
                if index in finished:
                    continue
            collective, operand = pending[index]
            if previous is not None:
                owner, result = previous
                result, operand = lax.optimization_barrier((result, operand))
                feed(owner, result)
            previous = (index, collective(operand))
    return [finished[index] for index in range(len(streams))]


def make_shards(n_dp, n_row, n_col):
    assert n_row == n_col
    transpose_pairs = [
        (a * n_col + b, b * n_col + a) for a in range(n_row) for b in range(n_col)
    ]

    def gather_half(mine, axis, axis_name):
        count = n_row if axis_name == "row" else n_col
        gathered = lax.all_gather(mine, axis_name, axis=axis)
        gathered = lax.all_gather(gathered, "dp", axis=axis)
        gathered = jnp.swapaxes(gathered, axis, axis + 1)
        shape = list(mine.shape)
        shape[axis] = mine.shape[axis] * count * n_dp
        return gathered.reshape(shape)

    def own_half(block, axis):
        half = block.shape[axis] // n_dp
        return lax.dynamic_slice_in_dim(block, lax.axis_index("dp") * half, half, axis=axis)

    def gather_features(block, axis, axis_name):
        return gather_half(own_half(block, axis), axis, axis_name)

    def reduce_half(partial, axis, axis_name):
        count = n_row if axis_name == "row" else n_col
        half = partial.shape[axis] // (count * n_dp)
        shape = list(partial.shape)
        shape[axis : axis + 1] = [count, n_dp, half]
        split = jnp.swapaxes(partial.reshape(shape), axis, axis + 1)
        split = lax.psum_scatter(split, "dp", scatter_dimension=axis)
        return lax.psum_scatter(
            split.astype(jnp.bfloat16), axis_name, scatter_dimension=axis
        ).astype(jnp.float32)

    def reduce_features(partial, axis, axis_name):
        return lax.all_gather(reduce_half(partial, axis, axis_name), "dp", axis=axis, tiled=True)

    def transpose_grid(block):
        return lax.ppermute(block, ("row", "col"), transpose_pairs)

    def gather_tokens(rows):
        return lax.all_gather(rows, "row", axis=1, tiled=True)

    def scatter_tokens(rows):
        return lax.psum_scatter(rows, "row", scatter_dimension=1, tiled=True)

    def gather_seqs(rows):
        return lax.all_gather(rows, "col", axis=0, tiled=True)

    def scatter_seqs(rows):
        return lax.psum_scatter(rows, "col", scatter_dimension=0, tiled=True)

    def to_tokens(rows):
        batches, local, seq_len, width = rows.shape
        rows = rows.reshape(batches, local, n_row, seq_len // n_row, width)
        rows = lax.all_to_all(rows, "row", 2, 3)
        return rows.reshape(batches, local, seq_len // n_row, n_row * width)

    def to_features(rows):
        batches, local, chunk, width = rows.shape
        rows = rows.reshape(batches, local, chunk, n_row, width // n_row)
        rows = lax.all_to_all(rows, "row", 3, 2)
        return rows.reshape(batches, local, n_row * chunk, width // n_row)

    def shards(
        hidden_in,
        segment_ids,
        w_query,
        w_key,
        w_value,
        w_out,
        w_gate,
        w_up,
        w_down,
        gain_attn,
        gain_ffn,
        cotangent,
    ):
        batches, local, seq_len, width_r = hidden_in.shape
        chunk = seq_len // n_row
        row_index = lax.axis_index("row")
        col_index = lax.axis_index("col")
        query_cols = w_query.shape[1]
        key_cols = w_key.shape[1]
        key_end = query_cols + key_cols
        qkv_cols = key_end + w_value.shape[1]
        heads_q = query_cols // HD
        heads_k = key_cols // HD
        group_count = heads_q // heads_k
        ffn_cols = w_gate.shape[1]

        w_attn = gather_half(
            transpose_grid(own_half(jnp.concatenate([w_query, w_key, w_value, w_out.T], axis=1), 0)),
            0,
            "col",
        )
        w_qkv = w_attn[:, :qkv_cols]
        w_out_heads = w_attn[:, qkv_cols:].T
        w_pair = gather_features(jnp.concatenate([w_gate, w_up], axis=1), 0, "row")
        w_down_all = gather_features(w_down, 1, "row")
        gain_attn_all = lax.all_gather(gain_attn, "row", tiled=True)
        gain_ffn_all = lax.all_gather(gain_ffn, "row", tiled=True)

        segments = lax.all_gather(segment_ids, "row", axis=1, tiled=True)
        segments = lax.dynamic_slice_in_dim(segments, col_index * local, local, axis=1)
        places = positions(segments)
        token_place = jnp.broadcast_to(jnp.arange(seq_len), (local, seq_len))

        hidden_t = to_tokens(hidden_in)
        cotangent_t = to_tokens(cotangent)

        def micro_batch(batch_index):
            rows_f = hidden_t[batch_index].astype(jnp.float32)
            inv_attn = lax.rsqrt(jnp.mean(rows_f * rows_f, axis=-1, keepdims=True) + EPSILON)
            norm_attn = rows_f * inv_attn
            normed_attn = (norm_attn * gain_attn_all).astype(jnp.bfloat16)
            spread_attn = yield (gather_tokens, normed_attn)
            qkv = jnp.einsum(
                "std,dm->stm", spread_attn, w_qkv, preferred_element_type=jnp.float32
            )
            cosine, sine_part = rotary(places[batch_index])
            query_rot = rotate(
                qkv[..., :query_cols].reshape(local, seq_len, heads_q, HD), cosine, sine_part
            ).astype(jnp.bfloat16)
            key_all = rotate(
                qkv[..., query_cols:key_end].reshape(local, seq_len, heads_k, HD),
                cosine,
                sine_part,
            ).astype(jnp.bfloat16)
            value_all = (
                qkv[..., key_end:].reshape(local, seq_len, heads_k, HD).astype(jnp.bfloat16)
            )
            query_grouped = query_rot.reshape(local, seq_len, heads_k, group_count, HD)
            mixed, log_total = lax.map(
                attend_forward,
                (
                    query_grouped,
                    key_all,
                    value_all,
                    segments[batch_index],
                    segments[batch_index],
                    token_place,
                ),
            )
            attn_part = jnp.einsum(
                "stm,md->std", mixed, w_out_heads, preferred_element_type=jnp.float32
            )
            attn_branch = yield (scatter_tokens, attn_part.astype(jnp.bfloat16))
            attn_branch = attn_branch.astype(jnp.float32)
            resid_mid = rows_f + RESIDUAL_SCALE * attn_branch
            inv_ffn = lax.rsqrt(jnp.mean(resid_mid * resid_mid, axis=-1, keepdims=True) + EPSILON)
            norm_ffn = resid_mid * inv_ffn
            normed_ffn = (norm_ffn * gain_ffn_all).astype(jnp.bfloat16)
            spread_ffn = yield (gather_seqs, normed_ffn)
            pair = jnp.einsum(
                "std,df->stf", spread_ffn, w_pair, preferred_element_type=jnp.float32
            )
            gate_rows = pair[..., :ffn_cols]
            up_rows = pair[..., ffn_cols:]
            sigmoid_gate = jax.nn.sigmoid(gate_rows)
            act_low = (gate_rows * sigmoid_gate * up_rows).astype(jnp.bfloat16)
            ffn_part = jnp.einsum(
                "stf,fd->std", act_low, w_down_all, preferred_element_type=jnp.float32
            )
            ffn_branch = yield (scatter_seqs, ffn_part.astype(jnp.bfloat16))
            ffn_branch = ffn_branch.astype(jnp.float32)
            block_out = (resid_mid + RESIDUAL_SCALE * ffn_branch).astype(jnp.bfloat16)
            block_features = to_features(block_out[None])

            grad_rows = cotangent_t[batch_index].astype(jnp.float32)
            grad_ffn = (RESIDUAL_SCALE * grad_rows).astype(jnp.bfloat16)
            spread_grad_ffn = yield (gather_seqs, grad_ffn)
            fresh_down = jnp.einsum(
                "stf,std->fd", act_low, spread_grad_ffn, preferred_element_type=jnp.float32
            )
            grad_act = jnp.einsum(
                "std,fd->stf", spread_grad_ffn, w_down_all, preferred_element_type=jnp.float32
            )
            grad_gate_rows = (
                grad_act * up_rows * sigmoid_gate * (1.0 + gate_rows * (1.0 - sigmoid_gate))
            )
            grad_up_rows = grad_act * gate_rows * sigmoid_gate
            paired_gradient = jnp.concatenate([grad_gate_rows, grad_up_rows], axis=-1).astype(
                jnp.bfloat16
            )
            fresh_pair = jnp.einsum(
                "std,stf->df", spread_ffn, paired_gradient, preferred_element_type=jnp.float32
            )
            grad_normed_part = jnp.einsum(
                "stf,df->std", paired_gradient, w_pair, preferred_element_type=jnp.float32
            )
            grad_normed_ffn = yield (scatter_seqs, grad_normed_part.astype(jnp.bfloat16))
            grad_normed_ffn = grad_normed_ffn.astype(jnp.float32)
            scaled_ffn = grad_normed_ffn * gain_ffn_all
            gain_ffn_part = jnp.sum(grad_normed_ffn * norm_ffn, axis=(0, 1))
            inner_ffn = jnp.mean(scaled_ffn * norm_ffn, axis=-1, keepdims=True)
            grad_mid = grad_rows + inv_ffn * (scaled_ffn - norm_ffn * inner_ffn)
            grad_attn = (RESIDUAL_SCALE * grad_mid).astype(jnp.bfloat16)
            spread_grad_attn = yield (gather_tokens, grad_attn)
            fresh_out = jnp.einsum(
                "std,stm->dm", spread_grad_attn, mixed, preferred_element_type=jnp.float32
            )
            grad_mixed = jnp.einsum(
                "std,md->stm", spread_grad_attn, w_out_heads, preferred_element_type=jnp.float32
            ).astype(jnp.bfloat16)
            grad_query_rot, grad_kv = lax.map(
                attend_backward,
                (
                    grad_mixed,
                    query_grouped,
                    key_all,
                    value_all,
                    log_total,
                    segments[batch_index],
                    segments[batch_index],
                    token_place,
                ),
            )
            grad_query = rotate(
                grad_query_rot.reshape(local, seq_len, heads_q, HD), cosine, -sine_part
            )
            grad_key = rotate(grad_kv[..., :HD], cosine, -sine_part)
            grad_qkv = jnp.concatenate(
                [
                    grad_query.reshape(local, seq_len, -1),
                    grad_key.reshape(local, seq_len, -1),
                    grad_kv[..., HD:].reshape(local, seq_len, -1),
                ],
                axis=-1,
            ).astype(jnp.bfloat16)
            fresh_qkv = jnp.einsum(
                "std,stm->dm", spread_attn, grad_qkv, preferred_element_type=jnp.float32
            )
            grad_normed_attn_part = jnp.einsum(
                "stm,dm->std", grad_qkv, w_qkv, preferred_element_type=jnp.float32
            )
            grad_normed_attn = yield (
                scatter_tokens, grad_normed_attn_part.astype(jnp.bfloat16)
            )
            grad_normed_attn = grad_normed_attn.astype(jnp.float32)
            scaled_attn = grad_normed_attn * gain_attn_all
            gain_attn_part = jnp.sum(grad_normed_attn * norm_attn, axis=(0, 1))
            inner_attn = jnp.mean(scaled_attn * norm_attn, axis=-1, keepdims=True)
            input_features = to_features(
                (grad_mid + inv_attn * (scaled_attn - norm_attn * inner_attn))[None]
            )
            fresh_attn = jnp.concatenate([fresh_qkv, fresh_out], axis=1)
            return (
                block_features,
                input_features,
                fresh_attn,
                fresh_pair,
                fresh_down,
                gain_attn_part,
                gain_ffn_part,
            )

        results = run_interleaved([micro_batch(b) for b in range(batches)])
        sums = [sum(parts[1:], parts[0]) for parts in zip(*[r[2:] for r in results])]
        grad_attn_w, grad_pair_w, grad_down_w, gain_attn_total, gain_ffn_total = sums
        outs_list = [r[0] for r in results]
        inputs_grad = [r[1] for r in results]

        total_pair = reduce_features(grad_pair_w, 0, "row")
        total_down = reduce_features(grad_down_w, 1, "row")
        gain_rows = lax.psum(jnp.stack([gain_attn_total, gain_ffn_total], axis=1), "row")
        gain_cols = jnp.pad(gain_rows, ((0, 0), (0, 126)))
        total_attn = lax.all_gather(
            transpose_grid(
                reduce_half(jnp.concatenate([grad_attn_w, gain_cols], axis=1), 0, "col")
            ),
            "dp",
            axis=0,
            tiled=True,
        )
        attn_cols = qkv_cols + w_out.shape[0]
        return (
            jnp.concatenate(outs_list),
            jnp.concatenate(inputs_grad),
            total_attn[:, :query_cols],
            total_attn[:, query_cols:key_end],
            total_attn[:, key_end:qkv_cols],
            total_attn[:, qkv_cols:attn_cols].T,
            total_pair[:, :ffn_cols],
            total_pair[:, ffn_cols:],
            total_down,
            total_attn[:, attn_cols],
            total_attn[:, attn_cols + 1],
        )

    return shards


def solution(mesh):
    activation = P(None, ("dp", "col"), None, "row")
    return jax.shard_map(
        make_shards(mesh.shape["dp"], mesh.shape["row"], mesh.shape["col"]),
        mesh=mesh,
        in_specs=(
            activation,
            P(None, ("dp", "row"), None),
            P("row", "col"),
            P("row", "col"),
            P("row", "col"),
            P("col", "row"),
            P("row", "col"),
            P("row", "col"),
            P("col", "row"),
            P("row"),
            P("row"),
            activation,
        ),
        out_specs=(
            activation,
            activation,
            P("row", "col"),
            P("row", "col"),
            P("row", "col"),
            P("col", "row"),
            P("row", "col"),
            P("row", "col"),
            P("col", "row"),
            P("row"),
            P("row"),
        ),
        check_vma=False,
    )
```

```python
import math

import jax
import jax.numpy as jnp
from jax import lax
from jax.sharding import PartitionSpec as P

HD = 64

EPSILON = 1e-05
RESIDUAL_SCALE = 0.22
SCORE_SCALE = 0.015625
ROPE_BASE = 10000000.0
MASKED_SCORE = -1e30


def positions(segment_rows):
    seq_len = segment_rows.shape[-1]
    places = jnp.arange(seq_len, dtype=jnp.int32)
    starts = jnp.concatenate(
        [
            jnp.ones(segment_rows.shape[:-1] + (1,), jnp.bool_),
            segment_rows[..., 1:] != segment_rows[..., :-1],
        ],
        axis=-1,
    )
    first_place = lax.cummax(
        jnp.where(starts, places, jnp.zeros_like(places)), axis=segment_rows.ndim - 1
    )
    return places - first_place


def rotary(place_rows):
    half_dim = HD // 2
    frequency = jnp.exp(jnp.arange(half_dim, dtype=jnp.float32) * (-2.0 * math.log(ROPE_BASE) / HD))
    angles = place_rows.astype(jnp.float32)[..., None] * frequency
    return (jnp.cos(angles)[..., None, :], jnp.sin(angles)[..., None, :])


def rotate(head_rows, cosine, sine_part):
    half_dim = head_rows.shape[-1] // 2
    first_half = head_rows[..., :half_dim]
    second_half = head_rows[..., half_dim:]
    return jnp.concatenate(
        [
            first_half * cosine - second_half * sine_part,
            second_half * cosine + first_half * sine_part,
        ],
        axis=-1,
    )


def masked_scores(query_rot, key_rot, query_segment, key_segment, query_place):
    key_place = jnp.arange(key_segment.shape[0])
    allowed = (query_segment[:, None] == key_segment[None, :]) & (
        query_place[:, None] >= key_place[None, :]
    )
    raw_scores = (
        jnp.einsum("qkgd,pkd->kgqp", query_rot, key_rot, preferred_element_type=jnp.float32)
        * SCORE_SCALE
    )
    return jnp.where(allowed, raw_scores, MASKED_SCORE)


def attend_forward(pieces):
    query_rot, key_all, value_all, query_segment, key_segment, query_place = pieces
    chunk, heads_k, group_count, head_dim = query_rot.shape
    attention_scores = masked_scores(query_rot, key_all, query_segment, key_segment, query_place)
    row_peak = jnp.max(attention_scores, axis=-1, keepdims=True)
    log_total = row_peak + jnp.log(
        jnp.sum(jnp.exp(attention_scores - row_peak), axis=-1, keepdims=True)
    )
    attn_probs = jnp.exp(attention_scores - log_total).astype(jnp.bfloat16)
    mixed = jnp.einsum("kgqp,pkd->qkgd", attn_probs, value_all, preferred_element_type=jnp.float32)
    return mixed.reshape(chunk, -1).astype(jnp.bfloat16), log_total


def attend_backward(pieces):
    grad_mixed, query_rot, key_all, value_all, log_total, query_segment, key_segment, query_place = pieces
    chunk, heads_k, group_count, head_dim = query_rot.shape
    grad_grouped = grad_mixed.reshape(chunk, heads_k, group_count, head_dim)
    attn_probs = jnp.exp(
        masked_scores(query_rot, key_all, query_segment, key_segment, query_place) - log_total
    )
    grad_probs = jnp.einsum(
        "qkgd,pkd->kgqp", grad_grouped, value_all, preferred_element_type=jnp.float32
    )
    grad_value = jnp.einsum(
        "kgqp,qkgd->pkd",
        attn_probs.astype(jnp.bfloat16),
        grad_grouped,
        preferred_element_type=jnp.float32,
    )
    grad_scores = (
        attn_probs * (grad_probs - jnp.sum(attn_probs * grad_probs, axis=-1, keepdims=True))
    ).astype(jnp.bfloat16)
    grad_query = (
        jnp.einsum("kgqp,pkd->qkgd", grad_scores, key_all, preferred_element_type=jnp.float32)
        * SCORE_SCALE
    )
    grad_key = (
        jnp.einsum("kgqp,qkgd->pkd", grad_scores, query_rot, preferred_element_type=jnp.float32)
        * SCORE_SCALE
    )
    return grad_query, jnp.concatenate([grad_key, grad_value], axis=-1)


def scatter_low(partial, axis_name, axis):
    return lax.psum_scatter(
        partial.astype(jnp.bfloat16), axis_name, scatter_dimension=axis, tiled=True
    ).astype(jnp.float32)


def run_interleaved(streams, first, keep_first):
    pending = {}
    finished = {}

    def feed(index, value):
        try:
            pending[index] = streams[index].send(value)
        except StopIteration as stop:
            finished[index] = stop.value

    for index in range(len(streams)):
        feed(index, None)
    previous = (-1, first)
    while len(finished) < len(streams):
        for index in range(len(streams)):
            if index in finished:
                continue
            if previous is not None and previous[0] == index:
                feed(index, previous[1])
                previous = None
                if index in finished:
                    continue
            collective, operand = pending[index]
            if previous is not None:
                owner, result = previous
                result, operand = lax.optimization_barrier((result, operand))
                if owner >= 0:
                    feed(owner, result)
                else:
                    keep_first(result)
            previous = (index, collective(operand))
    return [finished[index] for index in range(len(streams))]


def make_shards(n_dp, n_row, n_col):
    assert n_row == n_col
    transpose_pairs = [
        (a * n_col + b, b * n_col + a) for a in range(n_row) for b in range(n_col)
    ]

    def gather_half(mine, axis, axis_name):
        count = n_row if axis_name == "row" else n_col
        gathered = lax.all_gather(mine, axis_name, axis=axis)
        gathered = lax.all_gather(gathered, "dp", axis=axis)
        gathered = jnp.swapaxes(gathered, axis, axis + 1)
        shape = list(mine.shape)
        shape[axis] = mine.shape[axis] * count * n_dp
        return gathered.reshape(shape)

    def own_half(block, axis):
        half = block.shape[axis] // n_dp
        return lax.dynamic_slice_in_dim(block, lax.axis_index("dp") * half, half, axis=axis)

    def gather_features(block, axis, axis_name):
        return gather_half(own_half(block, axis), axis, axis_name)

    def reduce_half(partial, axis, axis_name):
        count = n_row if axis_name == "row" else n_col
        half = partial.shape[axis] // (count * n_dp)
        shape = list(partial.shape)
        shape[axis : axis + 1] = [count, n_dp, half]
        split = jnp.swapaxes(partial.reshape(shape), axis, axis + 1)
        split = lax.psum_scatter(split, "dp", scatter_dimension=axis)
        return lax.psum_scatter(
            split.astype(jnp.bfloat16), axis_name, scatter_dimension=axis
        ).astype(jnp.float32)

    def reduce_features(partial, axis, axis_name):
        return lax.all_gather(reduce_half(partial, axis, axis_name), "dp", axis=axis, tiled=True)

    def transpose_grid(block):
        return lax.ppermute(block, ("row", "col"), transpose_pairs)

    def gather_tokens(rows):
        return lax.all_gather(rows, "row", axis=1, tiled=True)

    def scatter_tokens(rows):
        return lax.psum_scatter(rows, "row", scatter_dimension=1, tiled=True)

    def gather_seqs(rows):
        return lax.all_gather(rows, "col", axis=0, tiled=True)

    def scatter_seqs(rows):
        return lax.psum_scatter(rows, "col", scatter_dimension=0, tiled=True)

    def to_tokens(rows):
        batches, local, seq_len, width = rows.shape
        rows = rows.reshape(batches, local, n_row, seq_len // n_row, width)
        rows = lax.all_to_all(rows, "row", 2, 3)
        return rows.reshape(batches, local, seq_len // n_row, n_row * width)

    def to_features(rows):
        batches, local, chunk, width = rows.shape
        rows = rows.reshape(batches, local, chunk, n_row, width // n_row)
        rows = lax.all_to_all(rows, "row", 3, 2)
        return rows.reshape(batches, local, n_row * chunk, width // n_row)

    def shards(
        hidden_in,
        segment_ids,
        w_query,
        w_key,
        w_value,
        w_out,
        w_gate,
        w_up,
        w_down,
        gain_attn,
        gain_ffn,
        cotangent,
    ):
        batches, local, seq_len, width_r = hidden_in.shape
        chunk = seq_len // n_row
        row_index = lax.axis_index("row")
        col_index = lax.axis_index("col")
        query_cols = w_query.shape[1]
        key_cols = w_key.shape[1]
        key_end = query_cols + key_cols
        qkv_cols = key_end + w_value.shape[1]
        heads_q = query_cols // HD
        heads_k = key_cols // HD
        group_count = heads_q // heads_k
        ffn_cols = w_gate.shape[1]

        w_attn = gather_half(
            transpose_grid(own_half(jnp.concatenate([w_query, w_key, w_value, w_out.T], axis=1), 0)),
            0,
            "col",
        )
        shared = {}
        gain_attn_all, gain_ffn_all = lax.all_gather(
            jnp.stack([gain_attn, gain_ffn]), "row", axis=1, tiled=True
        )

        segments = lax.all_gather(segment_ids, "row", axis=1, tiled=True)
        segments = lax.dynamic_slice_in_dim(segments, col_index * local, local, axis=1)
        places = positions(segments)
        token_place = jnp.broadcast_to(jnp.arange(seq_len), (local, seq_len))

        hidden_t = to_tokens(hidden_in)
        cotangent_t = to_tokens(cotangent)

        def micro_batch(batch_index):
            rows_f = hidden_t[batch_index].astype(jnp.float32)
            inv_attn = lax.rsqrt(jnp.mean(rows_f * rows_f, axis=-1, keepdims=True) + EPSILON)
            norm_attn = rows_f * inv_attn
            normed_attn = (norm_attn * gain_attn_all).astype(jnp.bfloat16)
            spread_attn = yield (gather_tokens, normed_attn)
            w_qkv = shared["attn"][:, :qkv_cols]
            w_out_heads = shared["attn"][:, qkv_cols:].T
            qkv = jnp.einsum(
                "std,dm->stm", spread_attn, w_qkv, preferred_element_type=jnp.float32
            )
            cosine, sine_part = rotary(places[batch_index])
            query_rot = rotate(
                qkv[..., :query_cols].reshape(local, seq_len, heads_q, HD), cosine, sine_part
            ).astype(jnp.bfloat16)
            key_all = rotate(
                qkv[..., query_cols:key_end].reshape(local, seq_len, heads_k, HD),
                cosine,
                sine_part,
            ).astype(jnp.bfloat16)
            value_all = (
                qkv[..., key_end:].reshape(local, seq_len, heads_k, HD).astype(jnp.bfloat16)
            )
            query_grouped = query_rot.reshape(local, seq_len, heads_k, group_count, HD)
            mixed, log_total = lax.map(
                attend_forward,
                (
                    query_grouped,
                    key_all,
                    value_all,
                    segments[batch_index],
                    segments[batch_index],
                    token_place,
                ),
            )
            attn_part = jnp.einsum(
                "stm,md->std", mixed, w_out_heads, preferred_element_type=jnp.float32
            )
            attn_branch = yield (scatter_tokens, attn_part.astype(jnp.bfloat16))
            attn_branch = attn_branch.astype(jnp.float32)
            resid_mid = rows_f + RESIDUAL_SCALE * attn_branch
            inv_ffn = lax.rsqrt(jnp.mean(resid_mid * resid_mid, axis=-1, keepdims=True) + EPSILON)
            norm_ffn = resid_mid * inv_ffn
            normed_ffn = (norm_ffn * gain_ffn_all).astype(jnp.bfloat16)
            spread_ffn = yield (gather_seqs, normed_ffn)
            w_pair_all = shared["pair"]
            pair = jnp.einsum(
                "std,df->stf", spread_ffn, w_pair_all, preferred_element_type=jnp.float32
            )
            gate_rows = pair[..., :ffn_cols]
            up_rows = pair[..., ffn_cols:]
            sigmoid_gate = jax.nn.sigmoid(gate_rows)
            act_low = (gate_rows * sigmoid_gate * up_rows).astype(jnp.bfloat16)
            w_down_all = shared["down"]
            ffn_part = jnp.einsum(
                "stf,fd->std", act_low, w_down_all, preferred_element_type=jnp.float32
            )
            ffn_branch = yield (scatter_seqs, ffn_part.astype(jnp.bfloat16))
            ffn_branch = ffn_branch.astype(jnp.float32)
            block_out = (resid_mid + RESIDUAL_SCALE * ffn_branch).astype(jnp.bfloat16)
            block_features = yield (to_features, block_out[None])

            grad_rows = cotangent_t[batch_index].astype(jnp.float32)
            grad_ffn = (RESIDUAL_SCALE * grad_rows).astype(jnp.bfloat16)
            spread_grad_ffn = yield (gather_seqs, grad_ffn)
            fresh_down = jnp.einsum(
                "stf,std->fd", act_low, spread_grad_ffn, preferred_element_type=jnp.float32
            )
            grad_act = jnp.einsum(
                "std,fd->stf", spread_grad_ffn, w_down_all, preferred_element_type=jnp.float32
            )
            grad_gate_rows = (
                grad_act * up_rows * sigmoid_gate * (1.0 + gate_rows * (1.0 - sigmoid_gate))
            )
            grad_up_rows = grad_act * gate_rows * sigmoid_gate
            paired_gradient = jnp.concatenate([grad_gate_rows, grad_up_rows], axis=-1).astype(
                jnp.bfloat16
            )
            fresh_pair = jnp.einsum(
                "std,stf->df", spread_ffn, paired_gradient, preferred_element_type=jnp.float32
            )
            grad_normed_part = jnp.einsum(
                "stf,df->std", paired_gradient, w_pair_all, preferred_element_type=jnp.float32
            )
            grad_normed_ffn = yield (scatter_seqs, grad_normed_part.astype(jnp.bfloat16))
            grad_normed_ffn = grad_normed_ffn.astype(jnp.float32)
            scaled_ffn = grad_normed_ffn * gain_ffn_all
            gain_ffn_part = jnp.sum(grad_normed_ffn * norm_ffn, axis=(0, 1))
            inner_ffn = jnp.mean(scaled_ffn * norm_ffn, axis=-1, keepdims=True)
            grad_mid = grad_rows + inv_ffn * (scaled_ffn - norm_ffn * inner_ffn)
            grad_attn = (RESIDUAL_SCALE * grad_mid).astype(jnp.bfloat16)
            spread_grad_attn = yield (gather_tokens, grad_attn)
            fresh_out = jnp.einsum(
                "std,stm->dm", spread_grad_attn, mixed, preferred_element_type=jnp.float32
            )
            grad_mixed = jnp.einsum(
                "std,md->stm", spread_grad_attn, w_out_heads, preferred_element_type=jnp.float32
            ).astype(jnp.bfloat16)
            grad_query_rot, grad_kv = lax.map(
                attend_backward,
                (
                    grad_mixed,
                    query_grouped,
                    key_all,
                    value_all,
                    log_total,
                    segments[batch_index],
                    segments[batch_index],
                    token_place,
                ),
            )
            grad_query = rotate(
                grad_query_rot.reshape(local, seq_len, heads_q, HD), cosine, -sine_part
            )
            grad_key = rotate(grad_kv[..., :HD], cosine, -sine_part)
            grad_qkv = jnp.concatenate(
                [
                    grad_query.reshape(local, seq_len, -1),
                    grad_key.reshape(local, seq_len, -1),
                    grad_kv[..., HD:].reshape(local, seq_len, -1),
                ],
                axis=-1,
            ).astype(jnp.bfloat16)
            fresh_qkv = jnp.einsum(
                "std,stm->dm", spread_attn, grad_qkv, preferred_element_type=jnp.float32
            )
            grad_normed_attn_part = jnp.einsum(
                "stm,dm->std", grad_qkv, w_qkv, preferred_element_type=jnp.float32
            )
            grad_normed_attn = yield (
                scatter_tokens, grad_normed_attn_part.astype(jnp.bfloat16)
            )
            grad_normed_attn = grad_normed_attn.astype(jnp.float32)
            scaled_attn = grad_normed_attn * gain_attn_all
            gain_attn_part = jnp.sum(grad_normed_attn * norm_attn, axis=(0, 1))
            inner_attn = jnp.mean(scaled_attn * norm_attn, axis=-1, keepdims=True)
            input_features = yield (
                to_features, (grad_mid + inv_attn * (scaled_attn - norm_attn * inner_attn))[None]
            )
            fresh_attn = jnp.concatenate([fresh_qkv, fresh_out], axis=1)
            return (
                block_features,
                input_features,
                fresh_attn,
                fresh_pair,
                fresh_down,
                gain_attn_part,
                gain_ffn_part,
            )

        def weight_stream():
            shared["pair"] = yield (
                lambda rows: gather_features(rows, 0, "row"),
                jnp.concatenate([w_gate, w_up], axis=1),
            )
            shared["down"] = yield (lambda rows: gather_features(rows, 1, "row"), w_down)
            return None

        streams = [micro_batch(b) for b in range(batches)]
        streams.insert(1, weight_stream())
        results = run_interleaved(streams, w_attn, lambda kept: shared.update(attn=kept))
        results = [r for r in results if r is not None]
        sums = [sum(parts[1:], parts[0]) for parts in zip(*[r[2:] for r in results])]
        grad_attn_w, grad_pair_w, grad_down_w, gain_attn_total, gain_ffn_total = sums
        outs_list = [r[0] for r in results]
        inputs_grad = [r[1] for r in results]

        total_pair = reduce_features(grad_pair_w, 0, "row")
        total_down = reduce_features(grad_down_w, 1, "row")
        gain_rows = lax.psum(jnp.stack([gain_attn_total, gain_ffn_total], axis=1), "row")
        gain_cols = jnp.pad(gain_rows, ((0, 0), (0, 126)))
        total_attn = lax.all_gather(
            transpose_grid(
                reduce_half(jnp.concatenate([grad_attn_w, gain_cols], axis=1), 0, "col")
            ),
            "dp",
            axis=0,
            tiled=True,
        )
        attn_cols = qkv_cols + w_out.shape[0]
        return (
            jnp.concatenate(outs_list),
            jnp.concatenate(inputs_grad),
            total_attn[:, :query_cols],
            total_attn[:, query_cols:key_end],
            total_attn[:, key_end:qkv_cols],
            total_attn[:, qkv_cols:attn_cols].T,
            total_pair[:, :ffn_cols],
            total_pair[:, ffn_cols:],
            total_down,
            total_attn[:, attn_cols],
            total_attn[:, attn_cols + 1],
        )

    return shards


def solution(mesh):
    activation = P(None, ("dp", "col"), None, "row")
    return jax.shard_map(
        make_shards(mesh.shape["dp"], mesh.shape["row"], mesh.shape["col"]),
        mesh=mesh,
        in_specs=(
            activation,
            P(None, ("dp", "row"), None),
            P("row", "col"),
            P("row", "col"),
            P("row", "col"),
            P("col", "row"),
            P("row", "col"),
            P("row", "col"),
            P("col", "row"),
            P("row"),
            P("row"),
            activation,
        ),
        out_specs=(
            activation,
            activation,
            P("row", "col"),
            P("row", "col"),
            P("row", "col"),
            P("col", "row"),
            P("row", "col"),
            P("row", "col"),
            P("col", "row"),
            P("row"),
            P("row"),
        ),
        check_vma=False,
    )
```

```python
import math

import jax
import jax.numpy as jnp
from jax import lax
from jax.sharding import PartitionSpec as P

HD = 64

EPSILON = 1e-05
RESIDUAL_SCALE = 0.22
SCORE_SCALE = 0.015625
ROPE_BASE = 10000000.0
MASKED_SCORE = -1e30


def positions(segment_rows):
    seq_len = segment_rows.shape[-1]
    places = jnp.arange(seq_len, dtype=jnp.int32)
    starts = jnp.concatenate(
        [
            jnp.ones(segment_rows.shape[:-1] + (1,), jnp.bool_),
            segment_rows[..., 1:] != segment_rows[..., :-1],
        ],
        axis=-1,
    )
    first_place = lax.cummax(
        jnp.where(starts, places, jnp.zeros_like(places)), axis=segment_rows.ndim - 1
    )
    return places - first_place


def rotary(place_rows):
    half_dim = HD // 2
    frequency = jnp.exp(jnp.arange(half_dim, dtype=jnp.float32) * (-2.0 * math.log(ROPE_BASE) / HD))
    angles = place_rows.astype(jnp.float32)[..., None] * frequency
    return (jnp.cos(angles)[..., None, :], jnp.sin(angles)[..., None, :])


def rotate(head_rows, cosine, sine_part):
    half_dim = head_rows.shape[-1] // 2
    first_half = head_rows[..., :half_dim]
    second_half = head_rows[..., half_dim:]
    return jnp.concatenate(
        [
            first_half * cosine - second_half * sine_part,
            second_half * cosine + first_half * sine_part,
        ],
        axis=-1,
    )


def masked_scores(query_rot, key_rot, query_segment, key_segment, query_place):
    key_place = jnp.arange(key_segment.shape[0])
    allowed = (query_segment[:, None] == key_segment[None, :]) & (
        query_place[:, None] >= key_place[None, :]
    )
    raw_scores = (
        jnp.einsum("qkgd,pkd->kgqp", query_rot, key_rot, preferred_element_type=jnp.float32)
        * SCORE_SCALE
    )
    return jnp.where(allowed, raw_scores, MASKED_SCORE)


def attend_forward(pieces):
    query_rot, key_all, value_all, query_segment, key_segment, query_place = pieces
    chunk, heads_k, group_count, head_dim = query_rot.shape
    attention_scores = masked_scores(query_rot, key_all, query_segment, key_segment, query_place)
    row_peak = jnp.max(attention_scores, axis=-1, keepdims=True)
    log_total = row_peak + jnp.log(
        jnp.sum(jnp.exp(attention_scores - row_peak), axis=-1, keepdims=True)
    )
    attn_probs = jnp.exp(attention_scores - log_total).astype(jnp.bfloat16)
    mixed = jnp.einsum("kgqp,pkd->qkgd", attn_probs, value_all, preferred_element_type=jnp.float32)
    return mixed.reshape(chunk, -1).astype(jnp.bfloat16), log_total


def attend_backward(pieces):
    grad_mixed, query_rot, key_all, value_all, log_total, query_segment, key_segment, query_place = pieces
    chunk, heads_k, group_count, head_dim = query_rot.shape
    grad_grouped = grad_mixed.reshape(chunk, heads_k, group_count, head_dim)
    attn_probs = jnp.exp(
        masked_scores(query_rot, key_all, query_segment, key_segment, query_place) - log_total
    )
    grad_probs = jnp.einsum(
        "qkgd,pkd->kgqp", grad_grouped, value_all, preferred_element_type=jnp.float32
    )
    grad_value = jnp.einsum(
        "kgqp,qkgd->pkd",
        attn_probs.astype(jnp.bfloat16),
        grad_grouped,
        preferred_element_type=jnp.float32,
    )
    grad_scores = (
        attn_probs * (grad_probs - jnp.sum(attn_probs * grad_probs, axis=-1, keepdims=True))
    ).astype(jnp.bfloat16)
    grad_query = (
        jnp.einsum("kgqp,pkd->qkgd", grad_scores, key_all, preferred_element_type=jnp.float32)
        * SCORE_SCALE
    )
    grad_key = (
        jnp.einsum("kgqp,qkgd->pkd", grad_scores, query_rot, preferred_element_type=jnp.float32)
        * SCORE_SCALE
    )
    return grad_query, jnp.concatenate([grad_key, grad_value], axis=-1)


def scatter_low(partial, axis_name, axis):
    return lax.psum_scatter(
        partial.astype(jnp.bfloat16), axis_name, scatter_dimension=axis, tiled=True
    ).astype(jnp.float32)


def run_interleaved(streams):
    pending = {}
    finished = {}

    def feed(index, value):
        try:
            pending[index] = streams[index].send(value)
        except StopIteration as stop:
            finished[index] = stop.value

    for index in range(len(streams)):
        feed(index, None)
    previous = None
    while len(finished) < len(streams):
        for index in range(len(streams)):
            if index in finished:
                continue
            if previous is not None and previous[0] == index:
                feed(index, previous[1])
                previous = None
                if index in finished:
                    continue
            collective, operand = pending[index]
            if previous is not None:
                owner, result = previous
                result, operand = lax.optimization_barrier((result, operand))
                feed(owner, result)
            previous = (index, collective(operand))
    return [finished[index] for index in range(len(streams))]


def make_shards(n_dp, n_row, n_col):
    assert n_row == n_col
    transpose_pairs = [
        (a * n_col + b, b * n_col + a) for a in range(n_row) for b in range(n_col)
    ]

    def gather_half(mine, axis, axis_name):
        count = n_row if axis_name == "row" else n_col
        gathered = lax.all_gather(mine, axis_name, axis=axis)
        gathered = lax.all_gather(gathered, "dp", axis=axis)
        gathered = jnp.swapaxes(gathered, axis, axis + 1)
        shape = list(mine.shape)
        shape[axis] = mine.shape[axis] * count * n_dp
        return gathered.reshape(shape)

    def own_half(block, axis):
        half = block.shape[axis] // n_dp
        return lax.dynamic_slice_in_dim(block, lax.axis_index("dp") * half, half, axis=axis)

    def gather_features(block, axis, axis_name):
        return gather_half(own_half(block, axis), axis, axis_name)

    def reduce_half(partial, axis, axis_name):
        count = n_row if axis_name == "row" else n_col
        half = partial.shape[axis] // (count * n_dp)
        shape = list(partial.shape)
        shape[axis : axis + 1] = [count, n_dp, half]
        split = jnp.swapaxes(partial.reshape(shape), axis, axis + 1)
        split = lax.psum_scatter(split, "dp", scatter_dimension=axis)
        return lax.psum_scatter(
            split.astype(jnp.bfloat16), axis_name, scatter_dimension=axis
        ).astype(jnp.float32)

    def reduce_half_exchange(partial, axis_name):
        count = n_row if axis_name == "row" else n_col
        half = partial.shape[0] // (count * n_dp)
        split = jnp.swapaxes(partial.reshape((count, n_dp, half) + partial.shape[1:]), 0, 1)
        split = lax.psum_scatter(split, "dp", scatter_dimension=0)
        blocks = lax.all_to_all(split.astype(jnp.bfloat16), axis_name, 0, 0)
        return jnp.sum(blocks.astype(jnp.float32), axis=0)

    def reduce_features(partial, axis, axis_name):
        return lax.all_gather(reduce_half(partial, axis, axis_name), "dp", axis=axis, tiled=True)

    def transpose_grid(block):
        return lax.ppermute(block, ("row", "col"), transpose_pairs)

    def gather_tokens(rows):
        return lax.all_gather(rows, "row", axis=1, tiled=True)

    def scatter_tokens(rows):
        return lax.psum_scatter(rows, "row", scatter_dimension=1, tiled=True)

    def gather_seqs(rows):
        return lax.all_gather(rows, "col", axis=0, tiled=True)

    def scatter_seqs(rows):
        return lax.psum_scatter(rows, "col", scatter_dimension=0, tiled=True)

    def to_tokens(rows):
        batches, local, seq_len, width = rows.shape
        rows = rows.reshape(batches, local, n_row, seq_len // n_row, width)
        rows = lax.all_to_all(rows, "row", 2, 3)
        return rows.reshape(batches, local, seq_len // n_row, n_row * width)

    def to_features(rows):
        batches, local, chunk, width = rows.shape
        rows = rows.reshape(batches, local, chunk, n_row, width // n_row)
        rows = lax.all_to_all(rows, "row", 3, 2)
        return rows.reshape(batches, local, n_row * chunk, width // n_row)

    def shards(
        hidden_in,
        segment_ids,
        w_query,
        w_key,
        w_value,
        w_out,
        w_gate,
        w_up,
        w_down,
        gain_attn,
        gain_ffn,
        cotangent,
    ):
        batches, local, seq_len, width_r = hidden_in.shape
        chunk = seq_len // n_row
        row_index = lax.axis_index("row")
        col_index = lax.axis_index("col")
        query_cols = w_query.shape[1]
        key_cols = w_key.shape[1]
        key_end = query_cols + key_cols
        qkv_cols = key_end + w_value.shape[1]
        heads_q = query_cols // HD
        heads_k = key_cols // HD
        group_count = heads_q // heads_k
        ffn_cols = w_gate.shape[1]

        w_attn = gather_half(
            transpose_grid(own_half(jnp.concatenate([w_query, w_key, w_value, w_out.T], axis=1), 0)),
            0,
            "col",
        )
        w_qkv = w_attn[:, :qkv_cols]
        w_out_heads = w_attn[:, qkv_cols:].T
        w_pair = gather_features(jnp.concatenate([w_gate, w_up], axis=1), 0, "row")
        w_down_all = gather_features(w_down, 1, "row")
        gain_attn_all, gain_ffn_all = lax.all_gather(
            jnp.stack([gain_attn, gain_ffn]), "row", axis=1, tiled=True
        )

        segments = lax.all_gather(segment_ids, "row", axis=1, tiled=True)
        segments = lax.dynamic_slice_in_dim(segments, col_index * local, local, axis=1)
        places = positions(segments)
        token_place = jnp.broadcast_to(jnp.arange(seq_len), (local, seq_len))

        hidden_t = to_tokens(hidden_in)
        cotangent_t = to_tokens(cotangent)

        def micro_batch(batch_index):
            rows_f = hidden_t[batch_index].astype(jnp.float32)
            inv_attn = lax.rsqrt(jnp.mean(rows_f * rows_f, axis=-1, keepdims=True) + EPSILON)
            norm_attn = rows_f * inv_attn
            normed_attn = (norm_attn * gain_attn_all).astype(jnp.bfloat16)
            spread_attn = yield (gather_tokens, normed_attn)
            qkv = jnp.einsum(
                "std,dm->stm", spread_attn, w_qkv, preferred_element_type=jnp.float32
            )
            cosine, sine_part = rotary(places[batch_index])
            query_rot = rotate(
                qkv[..., :query_cols].reshape(local, seq_len, heads_q, HD), cosine, sine_part
            ).astype(jnp.bfloat16)
            key_all = rotate(
                qkv[..., query_cols:key_end].reshape(local, seq_len, heads_k, HD),
                cosine,
                sine_part,
            ).astype(jnp.bfloat16)
            value_all = (
                qkv[..., key_end:].reshape(local, seq_len, heads_k, HD).astype(jnp.bfloat16)
            )
            query_grouped = query_rot.reshape(local, seq_len, heads_k, group_count, HD)
            mixed, log_total = lax.map(
                attend_forward,
                (
                    query_grouped,
                    key_all,
                    value_all,
                    segments[batch_index],
                    segments[batch_index],
                    token_place,
                ),
            )
            attn_part = jnp.einsum(
                "stm,md->std", mixed, w_out_heads, preferred_element_type=jnp.float32
            )
            attn_branch = yield (scatter_tokens, attn_part.astype(jnp.bfloat16))
            attn_branch = attn_branch.astype(jnp.float32)
            resid_mid = rows_f + RESIDUAL_SCALE * attn_branch
            inv_ffn = lax.rsqrt(jnp.mean(resid_mid * resid_mid, axis=-1, keepdims=True) + EPSILON)
            norm_ffn = resid_mid * inv_ffn
            normed_ffn = (norm_ffn * gain_ffn_all).astype(jnp.bfloat16)
            spread_ffn = yield (gather_seqs, normed_ffn)
            pair = jnp.einsum(
                "std,df->stf", spread_ffn, w_pair, preferred_element_type=jnp.float32
            )
            gate_rows = pair[..., :ffn_cols]
            up_rows = pair[..., ffn_cols:]
            sigmoid_gate = jax.nn.sigmoid(gate_rows)
            act_low = (gate_rows * sigmoid_gate * up_rows).astype(jnp.bfloat16)
            ffn_part = jnp.einsum(
                "stf,fd->std", act_low, w_down_all, preferred_element_type=jnp.float32
            )
            ffn_branch = yield (scatter_seqs, ffn_part.astype(jnp.bfloat16))
            ffn_branch = ffn_branch.astype(jnp.float32)
            block_out = (resid_mid + RESIDUAL_SCALE * ffn_branch).astype(jnp.bfloat16)
            block_features = to_features(block_out[None])

            grad_rows = cotangent_t[batch_index].astype(jnp.float32)
            grad_ffn = (RESIDUAL_SCALE * grad_rows).astype(jnp.bfloat16)
            spread_grad_ffn = yield (gather_seqs, grad_ffn)
            fresh_down = jnp.einsum(
                "stf,std->fd", act_low, spread_grad_ffn, preferred_element_type=jnp.float32
            )
            grad_act = jnp.einsum(
                "std,fd->stf", spread_grad_ffn, w_down_all, preferred_element_type=jnp.float32
            )
            grad_gate_rows = (
                grad_act * up_rows * sigmoid_gate * (1.0 + gate_rows * (1.0 - sigmoid_gate))
            )
            grad_up_rows = grad_act * gate_rows * sigmoid_gate
            paired_gradient = jnp.concatenate([grad_gate_rows, grad_up_rows], axis=-1).astype(
                jnp.bfloat16
            )
            fresh_pair = jnp.einsum(
                "std,stf->df", spread_ffn, paired_gradient, preferred_element_type=jnp.float32
            )
            grad_normed_part = jnp.einsum(
                "stf,df->std", paired_gradient, w_pair, preferred_element_type=jnp.float32
            )
            grad_normed_ffn = yield (scatter_seqs, grad_normed_part.astype(jnp.bfloat16))
            grad_normed_ffn = grad_normed_ffn.astype(jnp.float32)
            scaled_ffn = grad_normed_ffn * gain_ffn_all
            gain_ffn_part = jnp.sum(grad_normed_ffn * norm_ffn, axis=(0, 1))
            inner_ffn = jnp.mean(scaled_ffn * norm_ffn, axis=-1, keepdims=True)
            grad_mid = grad_rows + inv_ffn * (scaled_ffn - norm_ffn * inner_ffn)
            grad_attn = (RESIDUAL_SCALE * grad_mid).astype(jnp.bfloat16)
            spread_grad_attn = yield (gather_tokens, grad_attn)
            fresh_out = jnp.einsum(
                "std,stm->dm", spread_grad_attn, mixed, preferred_element_type=jnp.float32
            )
            grad_mixed = jnp.einsum(
                "std,md->stm", spread_grad_attn, w_out_heads, preferred_element_type=jnp.float32
            ).astype(jnp.bfloat16)
            grad_query_rot, grad_kv = lax.map(
                attend_backward,
                (
                    grad_mixed,
                    query_grouped,
                    key_all,
                    value_all,
                    log_total,
                    segments[batch_index],
                    segments[batch_index],
                    token_place,
                ),
            )
            grad_query = rotate(
                grad_query_rot.reshape(local, seq_len, heads_q, HD), cosine, -sine_part
            )
            grad_key = rotate(grad_kv[..., :HD], cosine, -sine_part)
            grad_qkv = jnp.concatenate(
                [
                    grad_query.reshape(local, seq_len, -1),
                    grad_key.reshape(local, seq_len, -1),
                    grad_kv[..., HD:].reshape(local, seq_len, -1),
                ],
                axis=-1,
            ).astype(jnp.bfloat16)
            fresh_qkv = jnp.einsum(
                "std,stm->dm", spread_attn, grad_qkv, preferred_element_type=jnp.float32
            )
            grad_normed_attn_part = jnp.einsum(
                "stm,dm->std", grad_qkv, w_qkv, preferred_element_type=jnp.float32
            )
            grad_normed_attn = yield (
                scatter_tokens, grad_normed_attn_part.astype(jnp.bfloat16)
            )
            grad_normed_attn = grad_normed_attn.astype(jnp.float32)
            scaled_attn = grad_normed_attn * gain_attn_all
            gain_attn_part = jnp.sum(grad_normed_attn * norm_attn, axis=(0, 1))
            inner_attn = jnp.mean(scaled_attn * norm_attn, axis=-1, keepdims=True)
            input_features = to_features(
                (grad_mid + inv_attn * (scaled_attn - norm_attn * inner_attn))[None]
            )
            fresh_attn = jnp.concatenate([fresh_qkv, fresh_out], axis=1)
            return (
                block_features,
                input_features,
                fresh_attn,
                fresh_pair,
                fresh_down,
                gain_attn_part,
                gain_ffn_part,
            )

        results = run_interleaved([micro_batch(b) for b in range(batches)])
        sums = [sum(parts[1:], parts[0]) for parts in zip(*[r[2:] for r in results])]
        grad_attn_w, grad_pair_w, grad_down_w, gain_attn_total, gain_ffn_total = sums
        outs_list = [r[0] for r in results]
        inputs_grad = [r[1] for r in results]

        total_pair = reduce_features(grad_pair_w, 0, "row")
        total_down = reduce_features(grad_down_w, 1, "row")
        gain_rows = lax.psum(jnp.stack([gain_attn_total, gain_ffn_total], axis=1), "row")
        gain_cols = jnp.pad(gain_rows, ((0, 0), (0, 126)))
        total_attn = lax.all_gather(
            transpose_grid(
                reduce_half_exchange(jnp.concatenate([grad_attn_w, gain_cols], axis=1), "col")
            ),
            "dp",
            axis=0,
            tiled=True,
        )
        attn_cols = qkv_cols + w_out.shape[0]
        return (
            jnp.concatenate(outs_list),
            jnp.concatenate(inputs_grad),
            total_attn[:, :query_cols],
            total_attn[:, query_cols:key_end],
            total_attn[:, key_end:qkv_cols],
            total_attn[:, qkv_cols:attn_cols].T,
            total_pair[:, :ffn_cols],
            total_pair[:, ffn_cols:],
            total_down,
            total_attn[:, attn_cols],
            total_attn[:, attn_cols + 1],
        )

    return shards


def solution(mesh):
    activation = P(None, ("dp", "col"), None, "row")
    return jax.shard_map(
        make_shards(mesh.shape["dp"], mesh.shape["row"], mesh.shape["col"]),
        mesh=mesh,
        in_specs=(
            activation,
            P(None, ("dp", "row"), None),
            P("row", "col"),
            P("row", "col"),
            P("row", "col"),
            P("col", "row"),
            P("row", "col"),
            P("row", "col"),
            P("col", "row"),
            P("row"),
            P("row"),
            activation,
        ),
        out_specs=(
            activation,
            activation,
            P("row", "col"),
            P("row", "col"),
            P("row", "col"),
            P("col", "row"),
            P("row", "col"),
            P("row", "col"),
            P("col", "row"),
            P("row"),
            P("row"),
        ),
        check_vma=False,
    )
```

```python
import math

import jax
import jax.numpy as jnp
from jax import lax
from jax.sharding import PartitionSpec as P

HD = 64

EPSILON = 1e-05
RESIDUAL_SCALE = 0.22
SCORE_SCALE = 0.015625
ROPE_BASE = 10000000.0
MASKED_SCORE = -1e30


def positions(segment_rows):
    seq_len = segment_rows.shape[-1]
    places = jnp.arange(seq_len, dtype=jnp.int32)
    starts = jnp.concatenate(
        [
            jnp.ones(segment_rows.shape[:-1] + (1,), jnp.bool_),
            segment_rows[..., 1:] != segment_rows[..., :-1],
        ],
        axis=-1,
    )
    first_place = lax.cummax(
        jnp.where(starts, places, jnp.zeros_like(places)), axis=segment_rows.ndim - 1
    )
    return places - first_place


def rotary(place_rows):
    half_dim = HD // 2
    frequency = jnp.exp(jnp.arange(half_dim, dtype=jnp.float32) * (-2.0 * math.log(ROPE_BASE) / HD))
    angles = place_rows.astype(jnp.float32)[..., None] * frequency
    return (jnp.cos(angles)[..., None, :], jnp.sin(angles)[..., None, :])


def rotate(head_rows, cosine, sine_part):
    half_dim = head_rows.shape[-1] // 2
    first_half = head_rows[..., :half_dim]
    second_half = head_rows[..., half_dim:]
    return jnp.concatenate(
        [
            first_half * cosine - second_half * sine_part,
            second_half * cosine + first_half * sine_part,
        ],
        axis=-1,
    )


def masked_scores(query_rot, key_rot, query_segment, key_segment, query_place):
    key_place = jnp.arange(key_segment.shape[0])
    allowed = (query_segment[:, None] == key_segment[None, :]) & (
        query_place[:, None] >= key_place[None, :]
    )
    raw_scores = (
        jnp.einsum("qkgd,pkd->kgqp", query_rot, key_rot, preferred_element_type=jnp.float32)
        * SCORE_SCALE
    )
    return jnp.where(allowed, raw_scores, MASKED_SCORE)


def attend_forward(pieces):
    query_rot, key_all, value_all, query_segment, key_segment, query_place = pieces
    chunk, heads_k, group_count, head_dim = query_rot.shape
    attention_scores = masked_scores(query_rot, key_all, query_segment, key_segment, query_place)
    row_peak = jnp.max(attention_scores, axis=-1, keepdims=True)
    log_total = row_peak + jnp.log(
        jnp.sum(jnp.exp(attention_scores - row_peak), axis=-1, keepdims=True)
    )
    attn_probs = jnp.exp(attention_scores - log_total).astype(jnp.bfloat16)
    mixed = jnp.einsum("kgqp,pkd->qkgd", attn_probs, value_all, preferred_element_type=jnp.float32)
    return mixed.reshape(chunk, -1).astype(jnp.bfloat16), log_total


def attend_backward(pieces):
    grad_mixed, query_rot, key_all, value_all, log_total, query_segment, key_segment, query_place = pieces
    chunk, heads_k, group_count, head_dim = query_rot.shape
    grad_grouped = grad_mixed.reshape(chunk, heads_k, group_count, head_dim)
    attn_probs = jnp.exp(
        masked_scores(query_rot, key_all, query_segment, key_segment, query_place) - log_total
    )
    grad_probs = jnp.einsum(
        "qkgd,pkd->kgqp", grad_grouped, value_all, preferred_element_type=jnp.float32
    )
    grad_value = jnp.einsum(
        "kgqp,qkgd->pkd",
        attn_probs.astype(jnp.bfloat16),
        grad_grouped,
        preferred_element_type=jnp.float32,
    )
    grad_scores = (
        attn_probs * (grad_probs - jnp.sum(attn_probs * grad_probs, axis=-1, keepdims=True))
    ).astype(jnp.bfloat16)
    grad_query = (
        jnp.einsum("kgqp,pkd->qkgd", grad_scores, key_all, preferred_element_type=jnp.float32)
        * SCORE_SCALE
    )
    grad_key = (
        jnp.einsum("kgqp,qkgd->pkd", grad_scores, query_rot, preferred_element_type=jnp.float32)
        * SCORE_SCALE
    )
    return grad_query, jnp.concatenate([grad_key, grad_value], axis=-1)


def scatter_low(partial, axis_name, axis):
    return lax.psum_scatter(
        partial.astype(jnp.bfloat16), axis_name, scatter_dimension=axis, tiled=True
    ).astype(jnp.float32)


def run_interleaved(streams):
    pending = {}
    finished = {}

    def feed(index, value):
        try:
            pending[index] = streams[index].send(value)
        except StopIteration as stop:
            finished[index] = stop.value

    for index in range(len(streams)):
        feed(index, None)
    previous = None
    while len(finished) < len(streams):
        for index in range(len(streams)):
            if index in finished:
                continue
            if previous is not None and previous[0] == index:
                feed(index, previous[1])
                previous = None
                if index in finished:
                    continue
            collective, operand = pending[index]
            if previous is not None:
                owner, result = previous
                result, operand = lax.optimization_barrier((result, operand))
                feed(owner, result)
            previous = (index, collective(operand))
    return [finished[index] for index in range(len(streams))]


def make_shards(n_dp, n_row, n_col):
    assert n_row == n_col
    transpose_pairs = [
        (a * n_col + b, b * n_col + a) for a in range(n_row) for b in range(n_col)
    ]

    def gather_half(mine, axis, axis_name):
        count = n_row if axis_name == "row" else n_col
        gathered = lax.all_gather(mine, axis_name, axis=axis)
        gathered = lax.all_gather(gathered, "dp", axis=axis)
        gathered = jnp.swapaxes(gathered, axis, axis + 1)
        shape = list(mine.shape)
        shape[axis] = mine.shape[axis] * count * n_dp
        return gathered.reshape(shape)

    def own_half(block, axis):
        half = block.shape[axis] // n_dp
        return lax.dynamic_slice_in_dim(block, lax.axis_index("dp") * half, half, axis=axis)

    def gather_features(block, axis, axis_name):
        return gather_half(own_half(block, axis), axis, axis_name)

    def reduce_half(partial, axis, axis_name):
        count = n_row if axis_name == "row" else n_col
        half = partial.shape[axis] // (count * n_dp)
        shape = list(partial.shape)
        shape[axis : axis + 1] = [count, n_dp, half]
        split = jnp.swapaxes(partial.reshape(shape), axis, axis + 1)
        split = lax.psum_scatter(split, "dp", scatter_dimension=axis)
        return lax.psum_scatter(
            split.astype(jnp.bfloat16), axis_name, scatter_dimension=axis
        ).astype(jnp.float32)

    def reduce_half_exchange(partial, axis_name):
        count = n_row if axis_name == "row" else n_col
        half = partial.shape[0] // (count * n_dp)
        split = jnp.swapaxes(partial.reshape((count, n_dp, half) + partial.shape[1:]), 0, 1)
        split = lax.psum_scatter(split, "dp", scatter_dimension=0)
        blocks = lax.all_to_all(split.astype(jnp.bfloat16), axis_name, 0, 0)
        return jnp.sum(blocks.astype(jnp.float32), axis=0)

    def reduce_features(partial, axis, axis_name):
        return lax.all_gather(reduce_half(partial, axis, axis_name), "dp", axis=axis, tiled=True)

    def transpose_grid(block):
        return lax.ppermute(block, ("row", "col"), transpose_pairs)

    def gather_tokens(rows):
        return lax.all_gather(rows, "row", axis=1, tiled=True)

    def scatter_tokens(rows):
        return lax.psum_scatter(rows, "row", scatter_dimension=1, tiled=True)

    def gather_seqs(rows):
        return lax.all_gather(rows, "col", axis=0, tiled=True)

    def scatter_seqs(rows):
        return lax.psum_scatter(rows, "col", scatter_dimension=0, tiled=True)

    def to_tokens(rows):
        batches, local, seq_len, width = rows.shape
        rows = rows.reshape(batches, local, n_row, seq_len // n_row, width)
        rows = lax.all_to_all(rows, "row", 2, 3)
        return rows.reshape(batches, local, seq_len // n_row, n_row * width)

    def to_features(rows):
        batches, local, chunk, width = rows.shape
        rows = rows.reshape(batches, local, chunk, n_row, width // n_row)
        rows = lax.all_to_all(rows, "row", 3, 2)
        return rows.reshape(batches, local, n_row * chunk, width // n_row)

    def shards(
        hidden_in,
        segment_ids,
        w_query,
        w_key,
        w_value,
        w_out,
        w_gate,
        w_up,
        w_down,
        gain_attn,
        gain_ffn,
        cotangent,
    ):
        batches, local, seq_len, width_r = hidden_in.shape
        chunk = seq_len // n_row
        row_index = lax.axis_index("row")
        col_index = lax.axis_index("col")
        query_cols = w_query.shape[1]
        key_cols = w_key.shape[1]
        key_end = query_cols + key_cols
        qkv_cols = key_end + w_value.shape[1]
        heads_q = query_cols // HD
        heads_k = key_cols // HD
        group_count = heads_q // heads_k
        ffn_cols = w_gate.shape[1]

        w_attn = gather_half(
            transpose_grid(own_half(jnp.concatenate([w_query, w_key, w_value, w_out.T], axis=1), 0)),
            0,
            "col",
        )
        w_qkv = w_attn[:, :qkv_cols]
        w_out_heads = w_attn[:, qkv_cols:].T
        w_pair = gather_features(jnp.concatenate([w_gate, w_up], axis=1), 0, "row")
        w_down_all = gather_features(w_down, 1, "row")
        gain_attn_all, gain_ffn_all = lax.all_gather(
            jnp.stack([gain_attn, gain_ffn]), "row", axis=1, tiled=True
        )

        segments = lax.all_gather(segment_ids, "row", axis=1, tiled=True)
        segments = lax.dynamic_slice_in_dim(segments, col_index * local, local, axis=1)
        places = positions(segments)
        token_place = jnp.broadcast_to(jnp.arange(seq_len), (local, seq_len))

        hidden_t = to_tokens(hidden_in)
        cotangent_t = to_tokens(cotangent)

        def micro_batch(batch_index):
            rows_f = hidden_t[batch_index].astype(jnp.float32)
            inv_attn = lax.rsqrt(jnp.mean(rows_f * rows_f, axis=-1, keepdims=True) + EPSILON)
            norm_attn = rows_f * inv_attn
            normed_attn = (norm_attn * gain_attn_all).astype(jnp.bfloat16)
            spread_attn = yield (gather_tokens, normed_attn)
            qkv = jnp.einsum(
                "std,dm->stm", spread_attn, w_qkv, preferred_element_type=jnp.float32
            )
            cosine, sine_part = rotary(places[batch_index])
            query_rot = rotate(
                qkv[..., :query_cols].reshape(local, seq_len, heads_q, HD), cosine, sine_part
            ).astype(jnp.bfloat16)
            key_all = rotate(
                qkv[..., query_cols:key_end].reshape(local, seq_len, heads_k, HD),
                cosine,
                sine_part,
            ).astype(jnp.bfloat16)
            value_all = (
                qkv[..., key_end:].reshape(local, seq_len, heads_k, HD).astype(jnp.bfloat16)
            )
            query_grouped = query_rot.reshape(local, seq_len, heads_k, group_count, HD)
            mixed, log_total = lax.map(
                attend_forward,
                (
                    query_grouped,
                    key_all,
                    value_all,
                    segments[batch_index],
                    segments[batch_index],
                    token_place,
                ),
            )
            attn_part = jnp.einsum(
                "stm,md->std", mixed, w_out_heads, preferred_element_type=jnp.float32
            )
            attn_branch = yield (scatter_tokens, attn_part.astype(jnp.bfloat16))
            attn_branch = attn_branch.astype(jnp.float32)
            resid_mid = rows_f + RESIDUAL_SCALE * attn_branch
            inv_ffn = lax.rsqrt(jnp.mean(resid_mid * resid_mid, axis=-1, keepdims=True) + EPSILON)
            norm_ffn = resid_mid * inv_ffn
            normed_ffn = (norm_ffn * gain_ffn_all).astype(jnp.bfloat16)
            spread_ffn = yield (gather_seqs, normed_ffn)
            pair = jnp.einsum(
                "std,df->stf", spread_ffn, w_pair, preferred_element_type=jnp.float32
            )
            gate_rows = pair[..., :ffn_cols]
            up_rows = pair[..., ffn_cols:]
            sigmoid_gate = jax.nn.sigmoid(gate_rows)
            act_low = (gate_rows * sigmoid_gate * up_rows).astype(jnp.bfloat16)
            ffn_part = jnp.einsum(
                "stf,fd->std", act_low, w_down_all, preferred_element_type=jnp.float32
            )
            ffn_branch = yield (scatter_seqs, ffn_part.astype(jnp.bfloat16))
            ffn_branch = ffn_branch.astype(jnp.float32)
            block_out = (resid_mid + RESIDUAL_SCALE * ffn_branch).astype(jnp.bfloat16)
            block_features = to_features(block_out[None])

            grad_rows = cotangent_t[batch_index].astype(jnp.float32)
            grad_ffn = (RESIDUAL_SCALE * grad_rows).astype(jnp.bfloat16)
            spread_grad_ffn = yield (gather_seqs, grad_ffn)
            fresh_down = jnp.einsum(
                "stf,std->fd", act_low, spread_grad_ffn, preferred_element_type=jnp.float32
            )
            grad_act = jnp.einsum(
                "std,fd->stf", spread_grad_ffn, w_down_all, preferred_element_type=jnp.float32
            )
            grad_gate_rows = (
                grad_act * up_rows * sigmoid_gate * (1.0 + gate_rows * (1.0 - sigmoid_gate))
            )
            grad_up_rows = grad_act * gate_rows * sigmoid_gate
            paired_gradient = jnp.concatenate([grad_gate_rows, grad_up_rows], axis=-1).astype(
                jnp.bfloat16
            )
            fresh_pair = jnp.einsum(
                "std,stf->df", spread_ffn, paired_gradient, preferred_element_type=jnp.float32
            )
            grad_normed_part = jnp.einsum(
                "stf,df->std", paired_gradient, w_pair, preferred_element_type=jnp.float32
            )
            grad_normed_ffn = yield (scatter_seqs, grad_normed_part.astype(jnp.bfloat16))
            grad_normed_ffn = grad_normed_ffn.astype(jnp.float32)
            scaled_ffn = grad_normed_ffn * gain_ffn_all
            gain_ffn_part = jnp.sum(grad_normed_ffn * norm_ffn, axis=(0, 1))
            inner_ffn = jnp.mean(scaled_ffn * norm_ffn, axis=-1, keepdims=True)
            grad_mid = grad_rows + inv_ffn * (scaled_ffn - norm_ffn * inner_ffn)
            grad_attn = (RESIDUAL_SCALE * grad_mid).astype(jnp.bfloat16)
            spread_grad_attn = yield (gather_tokens, grad_attn)
            fresh_out = jnp.einsum(
                "std,stm->dm", spread_grad_attn, mixed, preferred_element_type=jnp.float32
            )
            grad_mixed = jnp.einsum(
                "std,md->stm", spread_grad_attn, w_out_heads, preferred_element_type=jnp.float32
            ).astype(jnp.bfloat16)
            grad_query_rot, grad_kv = lax.map(
                attend_backward,
                (
                    grad_mixed,
                    query_grouped,
                    key_all,
                    value_all,
                    log_total,
                    segments[batch_index],
                    segments[batch_index],
                    token_place,
                ),
            )
            grad_query = rotate(
                grad_query_rot.reshape(local, seq_len, heads_q, HD), cosine, -sine_part
            )
            grad_key = rotate(grad_kv[..., :HD], cosine, -sine_part)
            grad_qkv = jnp.concatenate(
                [
                    grad_query.reshape(local, seq_len, -1),
                    grad_key.reshape(local, seq_len, -1),
                    grad_kv[..., HD:].reshape(local, seq_len, -1),
                ],
                axis=-1,
            ).astype(jnp.bfloat16)
            fresh_qkv = jnp.einsum(
                "std,stm->dm", spread_attn, grad_qkv, preferred_element_type=jnp.float32
            )
            grad_normed_attn_part = jnp.einsum(
                "stm,dm->std", grad_qkv, w_qkv, preferred_element_type=jnp.float32
            )
            grad_normed_attn = yield (
                scatter_tokens, grad_normed_attn_part.astype(jnp.bfloat16)
            )
            grad_normed_attn = grad_normed_attn.astype(jnp.float32)
            scaled_attn = grad_normed_attn * gain_attn_all
            gain_attn_part = jnp.sum(grad_normed_attn * norm_attn, axis=(0, 1))
            inner_attn = jnp.mean(scaled_attn * norm_attn, axis=-1, keepdims=True)
            input_features = to_features(
                (grad_mid + inv_attn * (scaled_attn - norm_attn * inner_attn))[None]
            )
            fresh_attn = jnp.concatenate([fresh_qkv, fresh_out], axis=1)
            return (
                block_features,
                input_features,
                fresh_attn,
                fresh_pair,
                fresh_down,
                gain_attn_part,
                gain_ffn_part,
            )

        results = run_interleaved([micro_batch(b) for b in range(batches)])
        sums = [sum(parts[1:], parts[0]) for parts in zip(*[r[2:] for r in results])]
        grad_attn_w, grad_pair_w, grad_down_w, gain_attn_total, gain_ffn_total = sums
        outs_list = [r[0] for r in results]
        inputs_grad = [r[1] for r in results]

        total_pair = lax.all_gather(
            reduce_half_exchange(grad_pair_w, "row"), "dp", axis=0, tiled=True
        )
        total_down = reduce_features(grad_down_w, 1, "row")
        gain_rows = lax.psum(jnp.stack([gain_attn_total, gain_ffn_total], axis=1), "row")
        gain_cols = jnp.pad(gain_rows, ((0, 0), (0, 126)))
        total_attn = lax.all_gather(
            transpose_grid(
                reduce_half_exchange(jnp.concatenate([grad_attn_w, gain_cols], axis=1), "col")
            ),
            "dp",
            axis=0,
            tiled=True,
        )
        attn_cols = qkv_cols + w_out.shape[0]
        return (
            jnp.concatenate(outs_list),
            jnp.concatenate(inputs_grad),
            total_attn[:, :query_cols],
            total_attn[:, query_cols:key_end],
            total_attn[:, key_end:qkv_cols],
            total_attn[:, qkv_cols:attn_cols].T,
            total_pair[:, :ffn_cols],
            total_pair[:, ffn_cols:],
            total_down,
            total_attn[:, attn_cols],
            total_attn[:, attn_cols + 1],
        )

    return shards


def solution(mesh):
    activation = P(None, ("dp", "col"), None, "row")
    return jax.shard_map(
        make_shards(mesh.shape["dp"], mesh.shape["row"], mesh.shape["col"]),
        mesh=mesh,
        in_specs=(
            activation,
            P(None, ("dp", "row"), None),
            P("row", "col"),
            P("row", "col"),
            P("row", "col"),
            P("col", "row"),
            P("row", "col"),
            P("row", "col"),
            P("col", "row"),
            P("row"),
            P("row"),
            activation,
        ),
        out_specs=(
            activation,
            activation,
            P("row", "col"),
            P("row", "col"),
            P("row", "col"),
            P("col", "row"),
            P("row", "col"),
            P("row", "col"),
            P("col", "row"),
            P("row"),
            P("row"),
        ),
        check_vma=False,
    )
```

```python
import math

import jax
import jax.numpy as jnp
from jax import lax
from jax.sharding import PartitionSpec as P

HD = 64

EPSILON = 1e-05
RESIDUAL_SCALE = 0.22
SCORE_SCALE = 0.015625
ROPE_BASE = 10000000.0
MASKED_SCORE = -1e30


def positions(segment_rows):
    seq_len = segment_rows.shape[-1]
    places = jnp.arange(seq_len, dtype=jnp.int32)
    starts = jnp.concatenate(
        [
            jnp.ones(segment_rows.shape[:-1] + (1,), jnp.bool_),
            segment_rows[..., 1:] != segment_rows[..., :-1],
        ],
        axis=-1,
    )
    first_place = lax.cummax(
        jnp.where(starts, places, jnp.zeros_like(places)), axis=segment_rows.ndim - 1
    )
    return places - first_place


def rotary(place_rows):
    half_dim = HD // 2
    frequency = jnp.exp(jnp.arange(half_dim, dtype=jnp.float32) * (-2.0 * math.log(ROPE_BASE) / HD))
    angles = place_rows.astype(jnp.float32)[..., None] * frequency
    return (jnp.cos(angles)[..., None, :], jnp.sin(angles)[..., None, :])


def rotate(head_rows, cosine, sine_part):
    half_dim = head_rows.shape[-1] // 2
    first_half = head_rows[..., :half_dim]
    second_half = head_rows[..., half_dim:]
    return jnp.concatenate(
        [
            first_half * cosine - second_half * sine_part,
            second_half * cosine + first_half * sine_part,
        ],
        axis=-1,
    )


def masked_scores(query_rot, key_rot, query_segment, key_segment, query_place):
    key_place = jnp.arange(key_segment.shape[0])
    allowed = (query_segment[:, None] == key_segment[None, :]) & (
        query_place[:, None] >= key_place[None, :]
    )
    raw_scores = (
        jnp.einsum("qkgd,pkd->kgqp", query_rot, key_rot, preferred_element_type=jnp.float32)
        * SCORE_SCALE
    )
    return jnp.where(allowed, raw_scores, MASKED_SCORE)


def attend_forward(pieces):
    query_rot, key_all, value_all, query_segment, key_segment, query_place = pieces
    chunk, heads_k, group_count, head_dim = query_rot.shape
    attention_scores = masked_scores(query_rot, key_all, query_segment, key_segment, query_place)
    row_peak = jnp.max(attention_scores, axis=-1, keepdims=True)
    log_total = row_peak + jnp.log(
        jnp.sum(jnp.exp(attention_scores - row_peak), axis=-1, keepdims=True)
    )
    attn_probs = jnp.exp(attention_scores - log_total).astype(jnp.bfloat16)
    mixed = jnp.einsum("kgqp,pkd->qkgd", attn_probs, value_all, preferred_element_type=jnp.float32)
    return mixed.reshape(chunk, -1).astype(jnp.bfloat16), log_total


def attend_backward(pieces):
    grad_mixed, query_rot, key_all, value_all, log_total, query_segment, key_segment, query_place = pieces
    chunk, heads_k, group_count, head_dim = query_rot.shape
    grad_grouped = grad_mixed.reshape(chunk, heads_k, group_count, head_dim)
    attn_probs = jnp.exp(
        masked_scores(query_rot, key_all, query_segment, key_segment, query_place) - log_total
    )
    grad_probs = jnp.einsum(
        "qkgd,pkd->kgqp", grad_grouped, value_all, preferred_element_type=jnp.float32
    )
    grad_value = jnp.einsum(
        "kgqp,qkgd->pkd",
        attn_probs.astype(jnp.bfloat16),
        grad_grouped,
        preferred_element_type=jnp.float32,
    )
    grad_scores = (
        attn_probs * (grad_probs - jnp.sum(attn_probs * grad_probs, axis=-1, keepdims=True))
    ).astype(jnp.bfloat16)
    grad_query = (
        jnp.einsum("kgqp,pkd->qkgd", grad_scores, key_all, preferred_element_type=jnp.float32)
        * SCORE_SCALE
    )
    grad_key = (
        jnp.einsum("kgqp,qkgd->pkd", grad_scores, query_rot, preferred_element_type=jnp.float32)
        * SCORE_SCALE
    )
    return grad_query, jnp.concatenate([grad_key, grad_value], axis=-1)


def scatter_low(partial, axis_name, axis):
    return lax.psum_scatter(
        partial.astype(jnp.bfloat16), axis_name, scatter_dimension=axis, tiled=True
    ).astype(jnp.float32)


def run_interleaved(streams):
    pending = {}
    finished = {}

    def feed(index, value):
        try:
            pending[index] = streams[index].send(value)
        except StopIteration as stop:
            finished[index] = stop.value

    for index in range(len(streams)):
        feed(index, None)
    previous = None
    while len(finished) < len(streams):
        for index in range(len(streams)):
            if index in finished:
                continue
            if previous is not None and previous[0] == index:
                feed(index, previous[1])
                previous = None
                if index in finished:
                    continue
            collective, operand = pending[index]
            if previous is not None:
                owner, result = previous
                result, operand = lax.optimization_barrier((result, operand))
                feed(owner, result)
            previous = (index, collective(operand))
    return [finished[index] for index in range(len(streams))]


def make_shards(n_dp, n_row, n_col):
    assert n_row == n_col
    transpose_pairs = [
        (a * n_col + b, b * n_col + a) for a in range(n_row) for b in range(n_col)
    ]

    def gather_half(mine, axis, axis_name):
        count = n_row if axis_name == "row" else n_col
        gathered = lax.all_gather(mine, axis_name, axis=axis)
        gathered = lax.all_gather(gathered, "dp", axis=axis)
        gathered = jnp.swapaxes(gathered, axis, axis + 1)
        shape = list(mine.shape)
        shape[axis] = mine.shape[axis] * count * n_dp
        return gathered.reshape(shape)

    def own_half(block, axis):
        half = block.shape[axis] // n_dp
        return lax.dynamic_slice_in_dim(block, lax.axis_index("dp") * half, half, axis=axis)

    def gather_features(block, axis, axis_name):
        return gather_half(own_half(block, axis), axis, axis_name)

    def reduce_half(partial, axis, axis_name):
        count = n_row if axis_name == "row" else n_col
        half = partial.shape[axis] // (count * n_dp)
        shape = list(partial.shape)
        shape[axis : axis + 1] = [count, n_dp, half]
        split = jnp.swapaxes(partial.reshape(shape), axis, axis + 1)
        split = lax.psum_scatter(split, "dp", scatter_dimension=axis)
        return lax.psum_scatter(
            split.astype(jnp.bfloat16), axis_name, scatter_dimension=axis
        ).astype(jnp.float32)

    def reduce_half_exchange(partial, axis_name):
        count = n_row if axis_name == "row" else n_col
        half = partial.shape[0] // (count * n_dp)
        split = jnp.swapaxes(partial.reshape((count, n_dp, half) + partial.shape[1:]), 0, 1)
        split = lax.psum_scatter(split, "dp", scatter_dimension=0)
        blocks = lax.all_to_all(split.astype(jnp.bfloat16), axis_name, 0, 0)
        return jnp.sum(blocks.astype(jnp.float32), axis=0)

    def reduce_features(partial, axis, axis_name):
        return lax.all_gather(reduce_half(partial, axis, axis_name), "dp", axis=axis, tiled=True)

    def transpose_grid(block):
        return lax.ppermute(block, ("row", "col"), transpose_pairs)

    def gather_tokens(rows):
        return lax.all_gather(rows, "row", axis=1, tiled=True)

    def scatter_tokens(rows):
        return lax.psum_scatter(rows, "row", scatter_dimension=1, tiled=True)

    def gather_seqs(rows):
        return lax.all_gather(rows, "col", axis=0, tiled=True)

    def scatter_seqs(rows):
        return lax.psum_scatter(rows, "col", scatter_dimension=0, tiled=True)

    def to_tokens(rows):
        batches, local, seq_len, width = rows.shape
        rows = rows.reshape(batches, local, n_row, seq_len // n_row, width)
        rows = lax.all_to_all(rows, "row", 2, 3)
        return rows.reshape(batches, local, seq_len // n_row, n_row * width)

    def to_features(rows):
        batches, local, chunk, width = rows.shape
        rows = rows.reshape(batches, local, chunk, n_row, width // n_row)
        rows = lax.all_to_all(rows, "row", 3, 2)
        return rows.reshape(batches, local, n_row * chunk, width // n_row)

    def shards(
        hidden_in,
        segment_ids,
        w_query,
        w_key,
        w_value,
        w_out,
        w_gate,
        w_up,
        w_down,
        gain_attn,
        gain_ffn,
        cotangent,
    ):
        batches, local, seq_len, width_r = hidden_in.shape
        chunk = seq_len // n_row
        row_index = lax.axis_index("row")
        col_index = lax.axis_index("col")
        query_cols = w_query.shape[1]
        key_cols = w_key.shape[1]
        key_end = query_cols + key_cols
        qkv_cols = key_end + w_value.shape[1]
        heads_q = query_cols // HD
        heads_k = key_cols // HD
        group_count = heads_q // heads_k
        ffn_cols = w_gate.shape[1]

        w_attn = gather_half(
            transpose_grid(own_half(jnp.concatenate([w_query, w_key, w_value, w_out.T], axis=1), 0)),
            0,
            "col",
        )
        w_qkv = w_attn[:, :qkv_cols]
        w_out_heads = w_attn[:, qkv_cols:].T
        w_pair = gather_features(jnp.concatenate([w_gate, w_up], axis=1), 0, "row")
        w_down_all = gather_features(w_down, 1, "row")
        gain_attn_all, gain_ffn_all = lax.all_gather(
            jnp.stack([gain_attn, gain_ffn]), "row", axis=1, tiled=True
        )

        segments = lax.all_gather(segment_ids, "row", axis=1, tiled=True)
        segments = lax.dynamic_slice_in_dim(segments, col_index * local, local, axis=1)
        places = positions(segments)
        token_place = jnp.broadcast_to(jnp.arange(seq_len), (local, seq_len))

        hidden_t = to_tokens(hidden_in)
        cotangent_t = to_tokens(cotangent)

        def micro_batch(batch_index):
            rows_f = hidden_t[batch_index].astype(jnp.float32)
            inv_attn = lax.rsqrt(jnp.mean(rows_f * rows_f, axis=-1, keepdims=True) + EPSILON)
            norm_attn = rows_f * inv_attn
            normed_attn = (norm_attn * gain_attn_all).astype(jnp.bfloat16)
            spread_attn = yield (gather_tokens, normed_attn)
            qkv = jnp.einsum(
                "std,dm->stm", spread_attn, w_qkv, preferred_element_type=jnp.float32
            )
            cosine, sine_part = rotary(places[batch_index])
            query_rot = rotate(
                qkv[..., :query_cols].reshape(local, seq_len, heads_q, HD), cosine, sine_part
            ).astype(jnp.bfloat16)
            key_all = rotate(
                qkv[..., query_cols:key_end].reshape(local, seq_len, heads_k, HD),
                cosine,
                sine_part,
            ).astype(jnp.bfloat16)
            value_all = (
                qkv[..., key_end:].reshape(local, seq_len, heads_k, HD).astype(jnp.bfloat16)
            )
            query_grouped = query_rot.reshape(local, seq_len, heads_k, group_count, HD)
            mixed, log_total = lax.map(
                attend_forward,
                (
                    query_grouped,
                    key_all,
                    value_all,
                    segments[batch_index],
                    segments[batch_index],
                    token_place,
                ),
            )
            attn_part = jnp.einsum(
                "stm,md->std", mixed, w_out_heads, preferred_element_type=jnp.float32
            )
            attn_branch = yield (scatter_tokens, attn_part.astype(jnp.bfloat16))
            attn_branch = attn_branch.astype(jnp.float32)
            resid_mid = rows_f + RESIDUAL_SCALE * attn_branch
            inv_ffn = lax.rsqrt(jnp.mean(resid_mid * resid_mid, axis=-1, keepdims=True) + EPSILON)
            norm_ffn = resid_mid * inv_ffn
            normed_ffn = (norm_ffn * gain_ffn_all).astype(jnp.bfloat16)
            spread_ffn = yield (gather_seqs, normed_ffn)
            pair = jnp.einsum(
                "std,df->stf", spread_ffn, w_pair, preferred_element_type=jnp.float32
            )
            gate_rows = pair[..., :ffn_cols]
            up_rows = pair[..., ffn_cols:]
            sigmoid_gate = jax.nn.sigmoid(gate_rows)
            act_low = (gate_rows * sigmoid_gate * up_rows).astype(jnp.bfloat16)
            ffn_part = jnp.einsum(
                "stf,fd->std", act_low, w_down_all, preferred_element_type=jnp.float32
            )
            ffn_branch = yield (scatter_seqs, ffn_part.astype(jnp.bfloat16))
            ffn_branch = ffn_branch.astype(jnp.float32)
            block_out = (resid_mid + RESIDUAL_SCALE * ffn_branch).astype(jnp.bfloat16)
            block_features = to_features(block_out[None])

            grad_rows = cotangent_t[batch_index].astype(jnp.float32)
            grad_ffn = (RESIDUAL_SCALE * grad_rows).astype(jnp.bfloat16)
            spread_grad_ffn = yield (gather_seqs, grad_ffn)
            fresh_down = jnp.einsum(
                "stf,std->fd", act_low, spread_grad_ffn, preferred_element_type=jnp.float32
            )
            grad_act = jnp.einsum(
                "std,fd->stf", spread_grad_ffn, w_down_all, preferred_element_type=jnp.float32
            )
            grad_gate_rows = (
                grad_act * up_rows * sigmoid_gate * (1.0 + gate_rows * (1.0 - sigmoid_gate))
            )
            grad_up_rows = grad_act * gate_rows * sigmoid_gate
            paired_gradient = jnp.concatenate([grad_gate_rows, grad_up_rows], axis=-1).astype(
                jnp.bfloat16
            )
            fresh_pair = jnp.einsum(
                "std,stf->df", spread_ffn, paired_gradient, preferred_element_type=jnp.float32
            )
            grad_normed_part = jnp.einsum(
                "stf,df->std", paired_gradient, w_pair, preferred_element_type=jnp.float32
            )
            block_features, scatter_operand = lax.optimization_barrier(
                (block_features, grad_normed_part.astype(jnp.bfloat16))
            )
            grad_normed_ffn = yield (scatter_seqs, scatter_operand)
            grad_normed_ffn = grad_normed_ffn.astype(jnp.float32)
            scaled_ffn = grad_normed_ffn * gain_ffn_all
            gain_ffn_part = jnp.sum(grad_normed_ffn * norm_ffn, axis=(0, 1))
            inner_ffn = jnp.mean(scaled_ffn * norm_ffn, axis=-1, keepdims=True)
            grad_mid = grad_rows + inv_ffn * (scaled_ffn - norm_ffn * inner_ffn)
            grad_attn = (RESIDUAL_SCALE * grad_mid).astype(jnp.bfloat16)
            spread_grad_attn = yield (gather_tokens, grad_attn)
            fresh_out = jnp.einsum(
                "std,stm->dm", spread_grad_attn, mixed, preferred_element_type=jnp.float32
            )
            grad_mixed = jnp.einsum(
                "std,md->stm", spread_grad_attn, w_out_heads, preferred_element_type=jnp.float32
            ).astype(jnp.bfloat16)
            grad_query_rot, grad_kv = lax.map(
                attend_backward,
                (
                    grad_mixed,
                    query_grouped,
                    key_all,
                    value_all,
                    log_total,
                    segments[batch_index],
                    segments[batch_index],
                    token_place,
                ),
            )
            grad_query = rotate(
                grad_query_rot.reshape(local, seq_len, heads_q, HD), cosine, -sine_part
            )
            grad_key = rotate(grad_kv[..., :HD], cosine, -sine_part)
            grad_qkv = jnp.concatenate(
                [
                    grad_query.reshape(local, seq_len, -1),
                    grad_key.reshape(local, seq_len, -1),
                    grad_kv[..., HD:].reshape(local, seq_len, -1),
                ],
                axis=-1,
            ).astype(jnp.bfloat16)
            fresh_qkv = jnp.einsum(
                "std,stm->dm", spread_attn, grad_qkv, preferred_element_type=jnp.float32
            )
            grad_normed_attn_part = jnp.einsum(
                "stm,dm->std", grad_qkv, w_qkv, preferred_element_type=jnp.float32
            )
            grad_normed_attn = yield (
                scatter_tokens, grad_normed_attn_part.astype(jnp.bfloat16)
            )
            grad_normed_attn = grad_normed_attn.astype(jnp.float32)
            scaled_attn = grad_normed_attn * gain_attn_all
            gain_attn_part = jnp.sum(grad_normed_attn * norm_attn, axis=(0, 1))
            inner_attn = jnp.mean(scaled_attn * norm_attn, axis=-1, keepdims=True)
            input_features = to_features(
                (grad_mid + inv_attn * (scaled_attn - norm_attn * inner_attn))[None]
            )
            fresh_attn = jnp.concatenate([fresh_qkv, fresh_out], axis=1)
            return (
                block_features,
                input_features,
                fresh_attn,
                fresh_pair,
                fresh_down,
                gain_attn_part,
                gain_ffn_part,
            )

        results = run_interleaved([micro_batch(b) for b in range(batches)])
        sums = [sum(parts[1:], parts[0]) for parts in zip(*[r[2:] for r in results])]
        grad_attn_w, grad_pair_w, grad_down_w, gain_attn_total, gain_ffn_total = sums
        outs_list = [r[0] for r in results]
        inputs_grad = [r[1] for r in results]

        total_pair = reduce_features(grad_pair_w, 0, "row")
        total_down = reduce_features(grad_down_w, 1, "row")
        gain_rows = lax.psum(jnp.stack([gain_attn_total, gain_ffn_total], axis=1), "row")
        gain_cols = jnp.pad(gain_rows, ((0, 0), (0, 126)))
        attn_grads = jnp.concatenate([grad_attn_w, gain_cols], axis=1)
        early_inputs, attn_grads = lax.optimization_barrier((inputs_grad[:-1], attn_grads))
        inputs_grad = list(early_inputs) + inputs_grad[-1:]
        total_attn = lax.all_gather(
            transpose_grid(reduce_half_exchange(attn_grads, "col")),
            "dp",
            axis=0,
            tiled=True,
        )
        attn_cols = qkv_cols + w_out.shape[0]
        return (
            jnp.concatenate(outs_list),
            jnp.concatenate(inputs_grad),
            total_attn[:, :query_cols],
            total_attn[:, query_cols:key_end],
            total_attn[:, key_end:qkv_cols],
            total_attn[:, qkv_cols:attn_cols].T,
            total_pair[:, :ffn_cols],
            total_pair[:, ffn_cols:],
            total_down,
            total_attn[:, attn_cols],
            total_attn[:, attn_cols + 1],
        )

    return shards


def solution(mesh):
    activation = P(None, ("dp", "col"), None, "row")
    return jax.shard_map(
        make_shards(mesh.shape["dp"], mesh.shape["row"], mesh.shape["col"]),
        mesh=mesh,
        in_specs=(
            activation,
            P(None, ("dp", "row"), None),
            P("row", "col"),
            P("row", "col"),
            P("row", "col"),
            P("col", "row"),
            P("row", "col"),
            P("row", "col"),
            P("col", "row"),
            P("row"),
            P("row"),
            activation,
        ),
        out_specs=(
            activation,
            activation,
            P("row", "col"),
            P("row", "col"),
            P("row", "col"),
            P("col", "row"),
            P("row", "col"),
            P("row", "col"),
            P("col", "row"),
            P("row"),
            P("row"),
        ),
        check_vma=False,
    )
```

```python
import math

import jax
import jax.numpy as jnp
from jax import lax
from jax.sharding import PartitionSpec as P

HD = 64

EPSILON = 1e-05
RESIDUAL_SCALE = 0.22
SCORE_SCALE = 0.015625
ROPE_BASE = 10000000.0
MASKED_SCORE = -1e30


def positions(segment_rows):
    seq_len = segment_rows.shape[-1]
    places = jnp.arange(seq_len, dtype=jnp.int32)
    starts = jnp.concatenate(
        [
            jnp.ones(segment_rows.shape[:-1] + (1,), jnp.bool_),
            segment_rows[..., 1:] != segment_rows[..., :-1],
        ],
        axis=-1,
    )
    first_place = lax.cummax(
        jnp.where(starts, places, jnp.zeros_like(places)), axis=segment_rows.ndim - 1
    )
    return places - first_place


def rotary(place_rows):
    half_dim = HD // 2
    frequency = jnp.exp(jnp.arange(half_dim, dtype=jnp.float32) * (-2.0 * math.log(ROPE_BASE) / HD))
    angles = place_rows.astype(jnp.float32)[..., None] * frequency
    return (jnp.cos(angles)[..., None, :], jnp.sin(angles)[..., None, :])


def rotate(head_rows, cosine, sine_part):
    half_dim = head_rows.shape[-1] // 2
    first_half = head_rows[..., :half_dim]
    second_half = head_rows[..., half_dim:]
    return jnp.concatenate(
        [
            first_half * cosine - second_half * sine_part,
            second_half * cosine + first_half * sine_part,
        ],
        axis=-1,
    )


def masked_scores(query_rot, key_rot, query_segment, key_segment, query_place):
    key_place = jnp.arange(key_segment.shape[0])
    allowed = (query_segment[:, None] == key_segment[None, :]) & (
        query_place[:, None] >= key_place[None, :]
    )
    raw_scores = (
        jnp.einsum("qkgd,pkd->kgqp", query_rot, key_rot, preferred_element_type=jnp.float32)
        * SCORE_SCALE
    )
    return jnp.where(allowed, raw_scores, MASKED_SCORE)


def attend_forward(pieces):
    query_rot, key_all, value_all, query_segment, key_segment, query_place = pieces
    chunk, heads_k, group_count, head_dim = query_rot.shape
    attention_scores = masked_scores(query_rot, key_all, query_segment, key_segment, query_place)
    row_peak = jnp.max(attention_scores, axis=-1, keepdims=True)
    log_total = row_peak + jnp.log(
        jnp.sum(jnp.exp(attention_scores - row_peak), axis=-1, keepdims=True)
    )
    attn_probs = jnp.exp(attention_scores - log_total).astype(jnp.bfloat16)
    mixed = jnp.einsum("kgqp,pkd->qkgd", attn_probs, value_all, preferred_element_type=jnp.float32)
    return mixed.reshape(chunk, -1).astype(jnp.bfloat16), log_total


def attend_backward(pieces):
    grad_mixed, query_rot, key_all, value_all, log_total, query_segment, key_segment, query_place = pieces
    chunk, heads_k, group_count, head_dim = query_rot.shape
    grad_grouped = grad_mixed.reshape(chunk, heads_k, group_count, head_dim)
    attn_probs = jnp.exp(
        masked_scores(query_rot, key_all, query_segment, key_segment, query_place) - log_total
    )
    grad_probs = jnp.einsum(
        "qkgd,pkd->kgqp", grad_grouped, value_all, preferred_element_type=jnp.float32
    )
    grad_value = jnp.einsum(
        "kgqp,qkgd->pkd",
        attn_probs.astype(jnp.bfloat16),
        grad_grouped,
        preferred_element_type=jnp.float32,
    )
    grad_scores = (
        attn_probs * (grad_probs - jnp.sum(attn_probs * grad_probs, axis=-1, keepdims=True))
    ).astype(jnp.bfloat16)
    grad_query = (
        jnp.einsum("kgqp,pkd->qkgd", grad_scores, key_all, preferred_element_type=jnp.float32)
        * SCORE_SCALE
    )
    grad_key = (
        jnp.einsum("kgqp,qkgd->pkd", grad_scores, query_rot, preferred_element_type=jnp.float32)
        * SCORE_SCALE
    )
    return grad_query, jnp.concatenate([grad_key, grad_value], axis=-1)


def scatter_low(partial, axis_name, axis):
    return lax.psum_scatter(
        partial.astype(jnp.bfloat16), axis_name, scatter_dimension=axis, tiled=True
    ).astype(jnp.float32)


def run_interleaved(streams):
    pending = {}
    finished = {}

    def feed(index, value):
        try:
            pending[index] = streams[index].send(value)
        except StopIteration as stop:
            finished[index] = stop.value

    for index in range(len(streams)):
        feed(index, None)
    previous = None
    while len(finished) < len(streams):
        for index in range(len(streams)):
            if index in finished:
                continue
            if previous is not None and previous[0] == index:
                feed(index, previous[1])
                previous = None
                if index in finished:
                    continue
            collective, operand = pending[index]
            if previous is not None:
                owner, result = previous
                result, operand = lax.optimization_barrier((result, operand))
                feed(owner, result)
            previous = (index, collective(operand))
    return [finished[index] for index in range(len(streams))]


def make_shards(n_dp, n_row, n_col):
    assert n_row == n_col
    transpose_pairs = [
        (a * n_col + b, b * n_col + a) for a in range(n_row) for b in range(n_col)
    ]

    def gather_half(mine, axis, axis_name):
        count = n_row if axis_name == "row" else n_col
        gathered = lax.all_gather(mine, axis_name, axis=axis)
        gathered = lax.all_gather(gathered, "dp", axis=axis)
        gathered = jnp.swapaxes(gathered, axis, axis + 1)
        shape = list(mine.shape)
        shape[axis] = mine.shape[axis] * count * n_dp
        return gathered.reshape(shape)

    def own_half(block, axis):
        half = block.shape[axis] // n_dp
        return lax.dynamic_slice_in_dim(block, lax.axis_index("dp") * half, half, axis=axis)

    def gather_features(block, axis, axis_name):
        return gather_half(own_half(block, axis), axis, axis_name)

    def reduce_half(partial, axis, axis_name):
        count = n_row if axis_name == "row" else n_col
        half = partial.shape[axis] // (count * n_dp)
        shape = list(partial.shape)
        shape[axis : axis + 1] = [count, n_dp, half]
        split = jnp.swapaxes(partial.reshape(shape), axis, axis + 1)
        split = lax.psum_scatter(split, "dp", scatter_dimension=axis)
        return lax.psum_scatter(
            split.astype(jnp.bfloat16), axis_name, scatter_dimension=axis
        ).astype(jnp.float32)

    def reduce_half_exchange(partial, axis_name):
        count = n_row if axis_name == "row" else n_col
        half = partial.shape[0] // (count * n_dp)
        split = jnp.swapaxes(partial.reshape((count, n_dp, half) + partial.shape[1:]), 0, 1)
        split = lax.psum_scatter(split, "dp", scatter_dimension=0)
        blocks = lax.all_to_all(split.astype(jnp.bfloat16), axis_name, 0, 0)
        return jnp.sum(blocks.astype(jnp.float32), axis=0)

    def gather_dp(block, axis):
        if n_dp != 2:
            return lax.all_gather(block, "dp", axis=axis, tiled=True)
        other = lax.ppermute(block, "dp", [(0, 1), (1, 0)])
        first_core = lax.axis_index("dp") == 0
        return jnp.concatenate(
            [jnp.where(first_core, block, other), jnp.where(first_core, other, block)], axis=axis
        )

    def reduce_features(partial, axis, axis_name):
        return gather_dp(reduce_half(partial, axis, axis_name), axis)

    def transpose_grid(block):
        return lax.ppermute(block, ("row", "col"), transpose_pairs)

    def gather_tokens(rows):
        return lax.all_gather(rows, "row", axis=1, tiled=True)

    def scatter_tokens(rows):
        return lax.psum_scatter(rows, "row", scatter_dimension=1, tiled=True)

    def gather_seqs(rows):
        return lax.all_gather(rows, "col", axis=0, tiled=True)

    def scatter_seqs(rows):
        return lax.psum_scatter(rows, "col", scatter_dimension=0, tiled=True)

    def to_tokens(rows):
        batches, local, seq_len, width = rows.shape
        rows = rows.reshape(batches, local, n_row, seq_len // n_row, width)
        rows = lax.all_to_all(rows, "row", 2, 3)
        return rows.reshape(batches, local, seq_len // n_row, n_row * width)

    def to_features(rows):
        batches, local, chunk, width = rows.shape
        rows = rows.reshape(batches, local, chunk, n_row, width // n_row)
        rows = lax.all_to_all(rows, "row", 3, 2)
        return rows.reshape(batches, local, n_row * chunk, width // n_row)

    def shards(
        hidden_in,
        segment_ids,
        w_query,
        w_key,
        w_value,
        w_out,
        w_gate,
        w_up,
        w_down,
        gain_attn,
        gain_ffn,
        cotangent,
    ):
        batches, local, seq_len, width_r = hidden_in.shape
        chunk = seq_len // n_row
        row_index = lax.axis_index("row")
        col_index = lax.axis_index("col")
        query_cols = w_query.shape[1]
        key_cols = w_key.shape[1]
        key_end = query_cols + key_cols
        qkv_cols = key_end + w_value.shape[1]
        heads_q = query_cols // HD
        heads_k = key_cols // HD
        group_count = heads_q // heads_k
        ffn_cols = w_gate.shape[1]

        w_attn = gather_half(
            transpose_grid(own_half(jnp.concatenate([w_query, w_key, w_value, w_out.T], axis=1), 0)),
            0,
            "col",
        )
        w_qkv = w_attn[:, :qkv_cols]
        w_out_heads = w_attn[:, qkv_cols:].T
        w_pair = gather_features(jnp.concatenate([w_gate, w_up], axis=1), 0, "row")
        w_down_all = gather_features(w_down, 1, "row")
        gain_attn_all, gain_ffn_all = lax.all_gather(
            jnp.stack([gain_attn, gain_ffn]), "row", axis=1, tiled=True
        )

        segments = lax.all_gather(segment_ids, "row", axis=1, tiled=True)
        segments = lax.dynamic_slice_in_dim(segments, col_index * local, local, axis=1)
        places = positions(segments)
        token_place = jnp.broadcast_to(jnp.arange(seq_len), (local, seq_len))

        hidden_t = to_tokens(hidden_in)
        cotangent_t = to_tokens(cotangent)

        def micro_batch(batch_index):
            rows_f = hidden_t[batch_index].astype(jnp.float32)
            inv_attn = lax.rsqrt(jnp.mean(rows_f * rows_f, axis=-1, keepdims=True) + EPSILON)
            norm_attn = rows_f * inv_attn
            normed_attn = (norm_attn * gain_attn_all).astype(jnp.bfloat16)
            spread_attn = yield (gather_tokens, normed_attn)
            qkv = jnp.einsum(
                "std,dm->stm", spread_attn, w_qkv, preferred_element_type=jnp.float32
            )
            cosine, sine_part = rotary(places[batch_index])
            query_rot = rotate(
                qkv[..., :query_cols].reshape(local, seq_len, heads_q, HD), cosine, sine_part
            ).astype(jnp.bfloat16)
            key_all = rotate(
                qkv[..., query_cols:key_end].reshape(local, seq_len, heads_k, HD),
                cosine,
                sine_part,
            ).astype(jnp.bfloat16)
            value_all = (
                qkv[..., key_end:].reshape(local, seq_len, heads_k, HD).astype(jnp.bfloat16)
            )
            query_grouped = query_rot.reshape(local, seq_len, heads_k, group_count, HD)
            mixed, log_total = lax.map(
                attend_forward,
                (
                    query_grouped,
                    key_all,
                    value_all,
                    segments[batch_index],
                    segments[batch_index],
                    token_place,
                ),
            )
            attn_part = jnp.einsum(
                "stm,md->std", mixed, w_out_heads, preferred_element_type=jnp.float32
            )
            attn_branch = yield (scatter_tokens, attn_part.astype(jnp.bfloat16))
            attn_branch = attn_branch.astype(jnp.float32)
            resid_mid = rows_f + RESIDUAL_SCALE * attn_branch
            inv_ffn = lax.rsqrt(jnp.mean(resid_mid * resid_mid, axis=-1, keepdims=True) + EPSILON)
            norm_ffn = resid_mid * inv_ffn
            normed_ffn = (norm_ffn * gain_ffn_all).astype(jnp.bfloat16)
            spread_ffn = yield (gather_seqs, normed_ffn)
            pair = jnp.einsum(
                "std,df->stf", spread_ffn, w_pair, preferred_element_type=jnp.float32
            )
            gate_rows = pair[..., :ffn_cols]
            up_rows = pair[..., ffn_cols:]
            sigmoid_gate = jax.nn.sigmoid(gate_rows)
            act_low = (gate_rows * sigmoid_gate * up_rows).astype(jnp.bfloat16)
            ffn_part = jnp.einsum(
                "stf,fd->std", act_low, w_down_all, preferred_element_type=jnp.float32
            )
            ffn_branch = yield (scatter_seqs, ffn_part.astype(jnp.bfloat16))
            ffn_branch = ffn_branch.astype(jnp.float32)
            block_out = (resid_mid + RESIDUAL_SCALE * ffn_branch).astype(jnp.bfloat16)
            block_features = to_features(block_out[None])

            grad_rows = cotangent_t[batch_index].astype(jnp.float32)
            grad_ffn = (RESIDUAL_SCALE * grad_rows).astype(jnp.bfloat16)
            spread_grad_ffn = yield (gather_seqs, grad_ffn)
            fresh_down = jnp.einsum(
                "stf,std->fd", act_low, spread_grad_ffn, preferred_element_type=jnp.float32
            )
            grad_act = jnp.einsum(
                "std,fd->stf", spread_grad_ffn, w_down_all, preferred_element_type=jnp.float32
            )
            grad_gate_rows = (
                grad_act * up_rows * sigmoid_gate * (1.0 + gate_rows * (1.0 - sigmoid_gate))
            )
            grad_up_rows = grad_act * gate_rows * sigmoid_gate
            paired_gradient = jnp.concatenate([grad_gate_rows, grad_up_rows], axis=-1).astype(
                jnp.bfloat16
            )
            fresh_pair = jnp.einsum(
                "std,stf->df", spread_ffn, paired_gradient, preferred_element_type=jnp.float32
            )
            grad_normed_part = jnp.einsum(
                "stf,df->std", paired_gradient, w_pair, preferred_element_type=jnp.float32
            )
            block_features, scatter_operand = lax.optimization_barrier(
                (block_features, grad_normed_part.astype(jnp.bfloat16))
            )
            grad_normed_ffn = yield (scatter_seqs, scatter_operand)
            grad_normed_ffn = grad_normed_ffn.astype(jnp.float32)
            scaled_ffn = grad_normed_ffn * gain_ffn_all
            gain_ffn_part = jnp.sum(grad_normed_ffn * norm_ffn, axis=(0, 1))
            inner_ffn = jnp.mean(scaled_ffn * norm_ffn, axis=-1, keepdims=True)
            grad_mid = grad_rows + inv_ffn * (scaled_ffn - norm_ffn * inner_ffn)
            grad_attn = (RESIDUAL_SCALE * grad_mid).astype(jnp.bfloat16)
            spread_grad_attn = yield (gather_tokens, grad_attn)
            fresh_out = jnp.einsum(
                "std,stm->dm", spread_grad_attn, mixed, preferred_element_type=jnp.float32
            )
            grad_mixed = jnp.einsum(
                "std,md->stm", spread_grad_attn, w_out_heads, preferred_element_type=jnp.float32
            ).astype(jnp.bfloat16)
            grad_query_rot, grad_kv = lax.map(
                attend_backward,
                (
                    grad_mixed,
                    query_grouped,
                    key_all,
                    value_all,
                    log_total,
                    segments[batch_index],
                    segments[batch_index],
                    token_place,
                ),
            )
            grad_query = rotate(
                grad_query_rot.reshape(local, seq_len, heads_q, HD), cosine, -sine_part
            )
            grad_key = rotate(grad_kv[..., :HD], cosine, -sine_part)
            grad_qkv = jnp.concatenate(
                [
                    grad_query.reshape(local, seq_len, -1),
                    grad_key.reshape(local, seq_len, -1),
                    grad_kv[..., HD:].reshape(local, seq_len, -1),
                ],
                axis=-1,
            ).astype(jnp.bfloat16)
            fresh_qkv = jnp.einsum(
                "std,stm->dm", spread_attn, grad_qkv, preferred_element_type=jnp.float32
            )
            grad_normed_attn_part = jnp.einsum(
                "stm,dm->std", grad_qkv, w_qkv, preferred_element_type=jnp.float32
            )
            grad_normed_attn = yield (
                scatter_tokens, grad_normed_attn_part.astype(jnp.bfloat16)
            )
            grad_normed_attn = grad_normed_attn.astype(jnp.float32)
            scaled_attn = grad_normed_attn * gain_attn_all
            gain_attn_part = jnp.sum(grad_normed_attn * norm_attn, axis=(0, 1))
            inner_attn = jnp.mean(scaled_attn * norm_attn, axis=-1, keepdims=True)
            input_features = to_features(
                (grad_mid + inv_attn * (scaled_attn - norm_attn * inner_attn))[None]
            )
            fresh_attn = jnp.concatenate([fresh_qkv, fresh_out], axis=1)
            return (
                block_features,
                input_features,
                fresh_attn,
                fresh_pair,
                fresh_down,
                gain_attn_part,
                gain_ffn_part,
            )

        results = run_interleaved([micro_batch(b) for b in range(batches)])
        sums = [sum(parts[1:], parts[0]) for parts in zip(*[r[2:] for r in results])]
        grad_attn_w, grad_pair_w, grad_down_w, gain_attn_total, gain_ffn_total = sums
        outs_list = [r[0] for r in results]
        inputs_grad = [r[1] for r in results]

        total_pair = reduce_features(grad_pair_w, 0, "row")
        total_down = reduce_features(grad_down_w, 1, "row")
        gain_rows = lax.psum(jnp.stack([gain_attn_total, gain_ffn_total], axis=1), "row")
        gain_cols = jnp.pad(gain_rows, ((0, 0), (0, 126)))
        attn_grads = jnp.concatenate([grad_attn_w, gain_cols], axis=1)
        early_inputs, attn_grads = lax.optimization_barrier((inputs_grad[:-1], attn_grads))
        inputs_grad = list(early_inputs) + inputs_grad[-1:]
        total_attn = gather_dp(transpose_grid(reduce_half_exchange(attn_grads, "col")), 0)
        attn_cols = qkv_cols + w_out.shape[0]
        return (
            jnp.concatenate(outs_list),
            jnp.concatenate(inputs_grad),
            total_attn[:, :query_cols],
            total_attn[:, query_cols:key_end],
            total_attn[:, key_end:qkv_cols],
            total_attn[:, qkv_cols:attn_cols].T,
            total_pair[:, :ffn_cols],
            total_pair[:, ffn_cols:],
            total_down,
            total_attn[:, attn_cols],
            total_attn[:, attn_cols + 1],
        )

    return shards


def solution(mesh):
    activation = P(None, ("dp", "col"), None, "row")
    return jax.shard_map(
        make_shards(mesh.shape["dp"], mesh.shape["row"], mesh.shape["col"]),
        mesh=mesh,
        in_specs=(
            activation,
            P(None, ("dp", "row"), None),
            P("row", "col"),
            P("row", "col"),
            P("row", "col"),
            P("col", "row"),
            P("row", "col"),
            P("row", "col"),
            P("col", "row"),
            P("row"),
            P("row"),
            activation,
        ),
        out_specs=(
            activation,
            activation,
            P("row", "col"),
            P("row", "col"),
            P("row", "col"),
            P("col", "row"),
            P("row", "col"),
            P("row", "col"),
            P("col", "row"),
            P("row"),
            P("row"),
        ),
        check_vma=False,
    )
```

```python
import math

import jax
import jax.numpy as jnp
from jax import lax
from jax.sharding import PartitionSpec as P

HD = 64

EPSILON = 1e-05
RESIDUAL_SCALE = 0.22
SCORE_SCALE = 0.015625
ROPE_BASE = 10000000.0
MASKED_SCORE = -1e30


def positions(segment_rows):
    seq_len = segment_rows.shape[-1]
    places = jnp.arange(seq_len, dtype=jnp.int32)
    starts = jnp.concatenate(
        [
            jnp.ones(segment_rows.shape[:-1] + (1,), jnp.bool_),
            segment_rows[..., 1:] != segment_rows[..., :-1],
        ],
        axis=-1,
    )
    first_place = lax.cummax(
        jnp.where(starts, places, jnp.zeros_like(places)), axis=segment_rows.ndim - 1
    )
    return places - first_place


def rotary(place_rows):
    half_dim = HD // 2
    frequency = jnp.exp(jnp.arange(half_dim, dtype=jnp.float32) * (-2.0 * math.log(ROPE_BASE) / HD))
    angles = place_rows.astype(jnp.float32)[..., None] * frequency
    return (jnp.cos(angles)[..., None, :], jnp.sin(angles)[..., None, :])


def rotate(head_rows, cosine, sine_part):
    half_dim = head_rows.shape[-1] // 2
    first_half = head_rows[..., :half_dim]
    second_half = head_rows[..., half_dim:]
    return jnp.concatenate(
        [
            first_half * cosine - second_half * sine_part,
            second_half * cosine + first_half * sine_part,
        ],
        axis=-1,
    )


def masked_scores(query_rot, key_rot, query_segment, key_segment, query_place):
    key_place = jnp.arange(key_segment.shape[0])
    allowed = (query_segment[:, None] == key_segment[None, :]) & (
        query_place[:, None] >= key_place[None, :]
    )
    raw_scores = (
        jnp.einsum("qkgd,pkd->kgqp", query_rot, key_rot, preferred_element_type=jnp.float32)
        * SCORE_SCALE
    )
    return jnp.where(allowed, raw_scores, MASKED_SCORE)


def attend_forward(pieces):
    query_rot, key_all, value_all, query_segment, key_segment, query_place = pieces
    chunk, heads_k, group_count, head_dim = query_rot.shape
    attention_scores = masked_scores(query_rot, key_all, query_segment, key_segment, query_place)
    row_peak = jnp.max(attention_scores, axis=-1, keepdims=True)
    log_total = row_peak + jnp.log(
        jnp.sum(jnp.exp(attention_scores - row_peak), axis=-1, keepdims=True)
    )
    attn_probs = jnp.exp(attention_scores - log_total).astype(jnp.bfloat16)
    mixed = jnp.einsum("kgqp,pkd->qkgd", attn_probs, value_all, preferred_element_type=jnp.float32)
    return mixed.reshape(chunk, -1).astype(jnp.bfloat16), log_total


def attend_backward(pieces):
    grad_mixed, query_rot, key_all, value_all, log_total, query_segment, key_segment, query_place = pieces
    chunk, heads_k, group_count, head_dim = query_rot.shape
    grad_grouped = grad_mixed.reshape(chunk, heads_k, group_count, head_dim)
    attn_probs = jnp.exp(
        masked_scores(query_rot, key_all, query_segment, key_segment, query_place) - log_total
    )
    grad_probs = jnp.einsum(
        "qkgd,pkd->kgqp", grad_grouped, value_all, preferred_element_type=jnp.float32
    )
    grad_value = jnp.einsum(
        "kgqp,qkgd->pkd",
        attn_probs.astype(jnp.bfloat16),
        grad_grouped,
        preferred_element_type=jnp.float32,
    )
    grad_scores = (
        attn_probs * (grad_probs - jnp.sum(attn_probs * grad_probs, axis=-1, keepdims=True))
    ).astype(jnp.bfloat16)
    grad_query = (
        jnp.einsum("kgqp,pkd->qkgd", grad_scores, key_all, preferred_element_type=jnp.float32)
        * SCORE_SCALE
    )
    grad_key = (
        jnp.einsum("kgqp,qkgd->pkd", grad_scores, query_rot, preferred_element_type=jnp.float32)
        * SCORE_SCALE
    )
    return grad_query, jnp.concatenate([grad_key, grad_value], axis=-1)


def scatter_low(partial, axis_name, axis):
    return lax.psum_scatter(
        partial.astype(jnp.bfloat16), axis_name, scatter_dimension=axis, tiled=True
    ).astype(jnp.float32)


def run_interleaved(streams):
    pending = {}
    finished = {}

    def feed(index, value):
        try:
            pending[index] = streams[index].send(value)
        except StopIteration as stop:
            finished[index] = stop.value

    for index in range(len(streams)):
        feed(index, None)
    previous = None
    while len(finished) < len(streams):
        for index in range(len(streams)):
            if index in finished:
                continue
            if previous is not None and previous[0] == index:
                feed(index, previous[1])
                previous = None
                if index in finished:
                    continue
            collective, operand = pending[index]
            if previous is not None:
                owner, result = previous
                result, operand = lax.optimization_barrier((result, operand))
                feed(owner, result)
            previous = (index, collective(operand))
    return [finished[index] for index in range(len(streams))]


def make_shards(n_dp, n_row, n_col):
    assert n_row == n_col
    transpose_pairs = [
        (a * n_col + b, b * n_col + a) for a in range(n_row) for b in range(n_col)
    ]

    def gather_half(mine, axis, axis_name):
        count = n_row if axis_name == "row" else n_col
        gathered = lax.all_gather(mine, axis_name, axis=axis)
        gathered = lax.all_gather(gathered, "dp", axis=axis)
        gathered = jnp.swapaxes(gathered, axis, axis + 1)
        shape = list(mine.shape)
        shape[axis] = mine.shape[axis] * count * n_dp
        return gathered.reshape(shape)

    def own_half(block, axis):
        half = block.shape[axis] // n_dp
        return lax.dynamic_slice_in_dim(block, lax.axis_index("dp") * half, half, axis=axis)

    def gather_features(block, axis, axis_name):
        return gather_half(own_half(block, axis), axis, axis_name)

    def reduce_half(partial, axis, axis_name):
        count = n_row if axis_name == "row" else n_col
        half = partial.shape[axis] // (count * n_dp)
        shape = list(partial.shape)
        shape[axis : axis + 1] = [count, n_dp, half]
        split = jnp.swapaxes(partial.reshape(shape), axis, axis + 1)
        split = lax.psum_scatter(split, "dp", scatter_dimension=axis)
        return lax.psum_scatter(
            split.astype(jnp.bfloat16), axis_name, scatter_dimension=axis
        ).astype(jnp.float32)

    def reduce_half_exchange(partial, axis_name):
        count = n_row if axis_name == "row" else n_col
        half = partial.shape[0] // (count * n_dp)
        split = jnp.swapaxes(partial.reshape((count, n_dp, half) + partial.shape[1:]), 0, 1)
        split = lax.psum_scatter(split, "dp", scatter_dimension=0)
        blocks = lax.all_to_all(split.astype(jnp.bfloat16), axis_name, 0, 0)
        return jnp.sum(blocks.astype(jnp.float32), axis=0)

    def reduce_features(partial, axis, axis_name):
        return lax.all_gather(reduce_half(partial, axis, axis_name), "dp", axis=axis, tiled=True)

    def transpose_grid(block):
        return lax.ppermute(block, ("row", "col"), transpose_pairs)

    def gather_tokens(rows):
        return lax.all_gather(rows, "row", axis=1, tiled=True)

    def scatter_tokens(rows):
        return lax.psum_scatter(rows, "row", scatter_dimension=1, tiled=True)

    def gather_seqs(rows):
        return lax.all_gather(rows, "col", axis=0, tiled=True)

    def scatter_seqs(rows):
        return lax.psum_scatter(rows, "col", scatter_dimension=0, tiled=True)

    def to_tokens(rows):
        batches, local, seq_len, width = rows.shape
        rows = rows.reshape(batches, local, n_row, seq_len // n_row, width)
        rows = lax.all_to_all(rows, "row", 2, 3)
        return rows.reshape(batches, local, seq_len // n_row, n_row * width)

    def to_features(rows):
        batches, local, chunk, width = rows.shape
        rows = rows.reshape(batches, local, chunk, n_row, width // n_row)
        rows = lax.all_to_all(rows, "row", 3, 2)
        return rows.reshape(batches, local, n_row * chunk, width // n_row)

    def shards(
        hidden_in,
        segment_ids,
        w_query,
        w_key,
        w_value,
        w_out,
        w_gate,
        w_up,
        w_down,
        gain_attn,
        gain_ffn,
        cotangent,
    ):
        batches, local, seq_len, width_r = hidden_in.shape
        chunk = seq_len // n_row
        row_index = lax.axis_index("row")
        col_index = lax.axis_index("col")
        query_cols = w_query.shape[1]
        key_cols = w_key.shape[1]
        key_end = query_cols + key_cols
        qkv_cols = key_end + w_value.shape[1]
        heads_q = query_cols // HD
        heads_k = key_cols // HD
        group_count = heads_q // heads_k
        ffn_cols = w_gate.shape[1]

        w_attn = gather_half(
            transpose_grid(own_half(jnp.concatenate([w_query, w_key, w_value, w_out.T], axis=1), 0)),
            0,
            "col",
        )
        w_qkv = w_attn[:, :qkv_cols]
        w_out_heads = w_attn[:, qkv_cols:].T
        w_pair = gather_features(jnp.concatenate([w_gate, w_up], axis=1), 0, "row")
        w_down_all = gather_features(w_down, 1, "row")
        gain_attn_all, gain_ffn_all = lax.all_gather(
            jnp.stack([gain_attn, gain_ffn]), "row", axis=1, tiled=True
        )

        segments = lax.all_gather(segment_ids, "row", axis=1, tiled=True)
        segments = lax.dynamic_slice_in_dim(segments, col_index * local, local, axis=1)
        places = positions(segments)
        token_place = jnp.broadcast_to(jnp.arange(seq_len), (local, seq_len))

        hidden_t, cotangent_t = to_tokens(jnp.concatenate([hidden_in, cotangent], axis=1)).reshape(
            (batches, 2, local, chunk, width_r * n_row)
        ).transpose(1, 0, 2, 3, 4)

        def micro_batch(batch_index):
            rows_f = hidden_t[batch_index].astype(jnp.float32)
            inv_attn = lax.rsqrt(jnp.mean(rows_f * rows_f, axis=-1, keepdims=True) + EPSILON)
            norm_attn = rows_f * inv_attn
            normed_attn = (norm_attn * gain_attn_all).astype(jnp.bfloat16)
            spread_attn = yield (gather_tokens, normed_attn)
            qkv = jnp.einsum(
                "std,dm->stm", spread_attn, w_qkv, preferred_element_type=jnp.float32
            )
            cosine, sine_part = rotary(places[batch_index])
            query_rot = rotate(
                qkv[..., :query_cols].reshape(local, seq_len, heads_q, HD), cosine, sine_part
            ).astype(jnp.bfloat16)
            key_all = rotate(
                qkv[..., query_cols:key_end].reshape(local, seq_len, heads_k, HD),
                cosine,
                sine_part,
            ).astype(jnp.bfloat16)
            value_all = (
                qkv[..., key_end:].reshape(local, seq_len, heads_k, HD).astype(jnp.bfloat16)
            )
            query_grouped = query_rot.reshape(local, seq_len, heads_k, group_count, HD)
            mixed, log_total = lax.map(
                attend_forward,
                (
                    query_grouped,
                    key_all,
                    value_all,
                    segments[batch_index],
                    segments[batch_index],
                    token_place,
                ),
            )
            attn_part = jnp.einsum(
                "stm,md->std", mixed, w_out_heads, preferred_element_type=jnp.float32
            )
            attn_branch = yield (scatter_tokens, attn_part.astype(jnp.bfloat16))
            attn_branch = attn_branch.astype(jnp.float32)
            resid_mid = rows_f + RESIDUAL_SCALE * attn_branch
            inv_ffn = lax.rsqrt(jnp.mean(resid_mid * resid_mid, axis=-1, keepdims=True) + EPSILON)
            norm_ffn = resid_mid * inv_ffn
            normed_ffn = (norm_ffn * gain_ffn_all).astype(jnp.bfloat16)
            spread_ffn = yield (gather_seqs, normed_ffn)
            pair = jnp.einsum(
                "std,df->stf", spread_ffn, w_pair, preferred_element_type=jnp.float32
            )
            gate_rows = pair[..., :ffn_cols]
            up_rows = pair[..., ffn_cols:]
            sigmoid_gate = jax.nn.sigmoid(gate_rows)
            act_low = (gate_rows * sigmoid_gate * up_rows).astype(jnp.bfloat16)
            ffn_part = jnp.einsum(
                "stf,fd->std", act_low, w_down_all, preferred_element_type=jnp.float32
            )
            ffn_branch = yield (scatter_seqs, ffn_part.astype(jnp.bfloat16))
            ffn_branch = ffn_branch.astype(jnp.float32)
            block_out = (resid_mid + RESIDUAL_SCALE * ffn_branch).astype(jnp.bfloat16)
            block_features = to_features(block_out[None])

            grad_rows = cotangent_t[batch_index].astype(jnp.float32)
            grad_ffn = (RESIDUAL_SCALE * grad_rows).astype(jnp.bfloat16)
            spread_grad_ffn = yield (gather_seqs, grad_ffn)
            fresh_down = jnp.einsum(
                "stf,std->fd", act_low, spread_grad_ffn, preferred_element_type=jnp.float32
            )
            grad_act = jnp.einsum(
                "std,fd->stf", spread_grad_ffn, w_down_all, preferred_element_type=jnp.float32
            )
            grad_gate_rows = (
                grad_act * up_rows * sigmoid_gate * (1.0 + gate_rows * (1.0 - sigmoid_gate))
            )
            grad_up_rows = grad_act * gate_rows * sigmoid_gate
            paired_gradient = jnp.concatenate([grad_gate_rows, grad_up_rows], axis=-1).astype(
                jnp.bfloat16
            )
            fresh_pair = jnp.einsum(
                "std,stf->df", spread_ffn, paired_gradient, preferred_element_type=jnp.float32
            )
            grad_normed_part = jnp.einsum(
                "stf,df->std", paired_gradient, w_pair, preferred_element_type=jnp.float32
            )
            block_features, scatter_operand = lax.optimization_barrier(
                (block_features, grad_normed_part.astype(jnp.bfloat16))
            )
            grad_normed_ffn = yield (scatter_seqs, scatter_operand)
            grad_normed_ffn = grad_normed_ffn.astype(jnp.float32)
            scaled_ffn = grad_normed_ffn * gain_ffn_all
            gain_ffn_part = jnp.sum(grad_normed_ffn * norm_ffn, axis=(0, 1))
            inner_ffn = jnp.mean(scaled_ffn * norm_ffn, axis=-1, keepdims=True)
            grad_mid = grad_rows + inv_ffn * (scaled_ffn - norm_ffn * inner_ffn)
            grad_attn = (RESIDUAL_SCALE * grad_mid).astype(jnp.bfloat16)
            spread_grad_attn = yield (gather_tokens, grad_attn)
            fresh_out = jnp.einsum(
                "std,stm->dm", spread_grad_attn, mixed, preferred_element_type=jnp.float32
            )
            grad_mixed = jnp.einsum(
                "std,md->stm", spread_grad_attn, w_out_heads, preferred_element_type=jnp.float32
            ).astype(jnp.bfloat16)
            grad_query_rot, grad_kv = lax.map(
                attend_backward,
                (
                    grad_mixed,
                    query_grouped,
                    key_all,
                    value_all,
                    log_total,
                    segments[batch_index],
                    segments[batch_index],
                    token_place,
                ),
            )
            grad_query = rotate(
                grad_query_rot.reshape(local, seq_len, heads_q, HD), cosine, -sine_part
            )
            grad_key = rotate(grad_kv[..., :HD], cosine, -sine_part)
            grad_qkv = jnp.concatenate(
                [
                    grad_query.reshape(local, seq_len, -1),
                    grad_key.reshape(local, seq_len, -1),
                    grad_kv[..., HD:].reshape(local, seq_len, -1),
                ],
                axis=-1,
            ).astype(jnp.bfloat16)
            fresh_qkv = jnp.einsum(
                "std,stm->dm", spread_attn, grad_qkv, preferred_element_type=jnp.float32
            )
            grad_normed_attn_part = jnp.einsum(
                "stm,dm->std", grad_qkv, w_qkv, preferred_element_type=jnp.float32
            )
            grad_normed_attn = yield (
                scatter_tokens, grad_normed_attn_part.astype(jnp.bfloat16)
            )
            grad_normed_attn = grad_normed_attn.astype(jnp.float32)
            scaled_attn = grad_normed_attn * gain_attn_all
            gain_attn_part = jnp.sum(grad_normed_attn * norm_attn, axis=(0, 1))
            inner_attn = jnp.mean(scaled_attn * norm_attn, axis=-1, keepdims=True)
            input_features = to_features(
                (grad_mid + inv_attn * (scaled_attn - norm_attn * inner_attn))[None]
            )
            fresh_attn = jnp.concatenate([fresh_qkv, fresh_out], axis=1)
            return (
                block_features,
                input_features,
                fresh_attn,
                fresh_pair,
                fresh_down,
                gain_attn_part,
                gain_ffn_part,
            )

        results = run_interleaved([micro_batch(b) for b in range(batches)])
        sums = [sum(parts[1:], parts[0]) for parts in zip(*[r[2:] for r in results])]
        grad_attn_w, grad_pair_w, grad_down_w, gain_attn_total, gain_ffn_total = sums
        outs_list = [r[0] for r in results]
        inputs_grad = [r[1] for r in results]

        total_pair = reduce_features(grad_pair_w, 0, "row")
        total_down = reduce_features(grad_down_w, 1, "row")
        gain_rows = lax.psum(jnp.stack([gain_attn_total, gain_ffn_total], axis=1), "row")
        gain_cols = jnp.pad(gain_rows, ((0, 0), (0, 126)))
        attn_grads = jnp.concatenate([grad_attn_w, gain_cols], axis=1)
        early_inputs, attn_grads = lax.optimization_barrier((inputs_grad[:-1], attn_grads))
        inputs_grad = list(early_inputs) + inputs_grad[-1:]
        total_attn = lax.all_gather(
            transpose_grid(reduce_half_exchange(attn_grads, "col")),
            "dp",
            axis=0,
            tiled=True,
        )
        attn_cols = qkv_cols + w_out.shape[0]
        return (
            jnp.concatenate(outs_list),
            jnp.concatenate(inputs_grad),
            total_attn[:, :query_cols],
            total_attn[:, query_cols:key_end],
            total_attn[:, key_end:qkv_cols],
            total_attn[:, qkv_cols:attn_cols].T,
            total_pair[:, :ffn_cols],
            total_pair[:, ffn_cols:],
            total_down,
            total_attn[:, attn_cols],
            total_attn[:, attn_cols + 1],
        )

    return shards


def solution(mesh):
    activation = P(None, ("dp", "col"), None, "row")
    return jax.shard_map(
        make_shards(mesh.shape["dp"], mesh.shape["row"], mesh.shape["col"]),
        mesh=mesh,
        in_specs=(
            activation,
            P(None, ("dp", "row"), None),
            P("row", "col"),
            P("row", "col"),
            P("row", "col"),
            P("col", "row"),
            P("row", "col"),
            P("row", "col"),
            P("col", "row"),
            P("row"),
            P("row"),
            activation,
        ),
        out_specs=(
            activation,
            activation,
            P("row", "col"),
            P("row", "col"),
            P("row", "col"),
            P("col", "row"),
            P("row", "col"),
            P("row", "col"),
            P("col", "row"),
            P("row"),
            P("row"),
        ),
        check_vma=False,
    )
```

```python
import math

import jax
import jax.numpy as jnp
from jax import lax
from jax.sharding import PartitionSpec as P

HD = 64

EPSILON = 1e-05
RESIDUAL_SCALE = 0.22
SCORE_SCALE = 0.015625
ROPE_BASE = 10000000.0
MASKED_SCORE = -1e30


def positions(segment_rows):
    seq_len = segment_rows.shape[-1]
    places = jnp.arange(seq_len, dtype=jnp.int32)
    starts = jnp.concatenate(
        [
            jnp.ones(segment_rows.shape[:-1] + (1,), jnp.bool_),
            segment_rows[..., 1:] != segment_rows[..., :-1],
        ],
        axis=-1,
    )
    first_place = lax.cummax(
        jnp.where(starts, places, jnp.zeros_like(places)), axis=segment_rows.ndim - 1
    )
    return places - first_place


def rotary(place_rows):
    half_dim = HD // 2
    frequency = jnp.exp(jnp.arange(half_dim, dtype=jnp.float32) * (-2.0 * math.log(ROPE_BASE) / HD))
    angles = place_rows.astype(jnp.float32)[..., None] * frequency
    return (jnp.cos(angles)[..., None, :], jnp.sin(angles)[..., None, :])


def rotate(head_rows, cosine, sine_part):
    half_dim = head_rows.shape[-1] // 2
    first_half = head_rows[..., :half_dim]
    second_half = head_rows[..., half_dim:]
    return jnp.concatenate(
        [
            first_half * cosine - second_half * sine_part,
            second_half * cosine + first_half * sine_part,
        ],
        axis=-1,
    )


def masked_scores(query_rot, key_rot, query_segment, key_segment, query_place):
    key_place = jnp.arange(key_segment.shape[0])
    allowed = (query_segment[:, None] == key_segment[None, :]) & (
        query_place[:, None] >= key_place[None, :]
    )
    raw_scores = (
        jnp.einsum("qkgd,pkd->kgqp", query_rot, key_rot, preferred_element_type=jnp.float32)
        * SCORE_SCALE
    )
    return jnp.where(allowed, raw_scores, MASKED_SCORE)


def attend_forward(pieces):
    query_rot, key_all, value_all, query_segment, key_segment, query_place = pieces
    chunk, heads_k, group_count, head_dim = query_rot.shape
    attention_scores = masked_scores(query_rot, key_all, query_segment, key_segment, query_place)
    row_peak = jnp.max(attention_scores, axis=-1, keepdims=True)
    log_total = row_peak + jnp.log(
        jnp.sum(jnp.exp(attention_scores - row_peak), axis=-1, keepdims=True)
    )
    attn_probs = jnp.exp(attention_scores - log_total).astype(jnp.bfloat16)
    mixed = jnp.einsum("kgqp,pkd->qkgd", attn_probs, value_all, preferred_element_type=jnp.float32)
    return mixed.reshape(chunk, -1).astype(jnp.bfloat16), log_total


def attend_backward(pieces):
    grad_mixed, query_rot, key_all, value_all, log_total, query_segment, key_segment, query_place = pieces
    chunk, heads_k, group_count, head_dim = query_rot.shape
    grad_grouped = grad_mixed.reshape(chunk, heads_k, group_count, head_dim)
    attn_probs = jnp.exp(
        masked_scores(query_rot, key_all, query_segment, key_segment, query_place) - log_total
    )
    grad_probs = jnp.einsum(
        "qkgd,pkd->kgqp", grad_grouped, value_all, preferred_element_type=jnp.float32
    )
    grad_value = jnp.einsum(
        "kgqp,qkgd->pkd",
        attn_probs.astype(jnp.bfloat16),
        grad_grouped,
        preferred_element_type=jnp.float32,
    )
    grad_scores = (
        attn_probs * (grad_probs - jnp.sum(attn_probs * grad_probs, axis=-1, keepdims=True))
    ).astype(jnp.bfloat16)
    grad_query = (
        jnp.einsum("kgqp,pkd->qkgd", grad_scores, key_all, preferred_element_type=jnp.float32)
        * SCORE_SCALE
    )
    grad_key = (
        jnp.einsum("kgqp,qkgd->pkd", grad_scores, query_rot, preferred_element_type=jnp.float32)
        * SCORE_SCALE
    )
    return grad_query, jnp.concatenate([grad_key, grad_value], axis=-1)


def scatter_low(partial, axis_name, axis):
    return lax.psum_scatter(
        partial.astype(jnp.bfloat16), axis_name, scatter_dimension=axis, tiled=True
    ).astype(jnp.float32)


def run_interleaved(streams):
    pending = {}
    finished = {}

    def feed(index, value):
        try:
            pending[index] = streams[index].send(value)
        except StopIteration as stop:
            finished[index] = stop.value

    for index in range(len(streams)):
        feed(index, None)
    previous = None
    while len(finished) < len(streams):
        for index in range(len(streams)):
            if index in finished:
                continue
            if previous is not None and previous[0] == index:
                feed(index, previous[1])
                previous = None
                if index in finished:
                    continue
            collective, operand = pending[index]
            if previous is not None:
                owner, result = previous
                result, operand = lax.optimization_barrier((result, operand))
                feed(owner, result)
            previous = (index, collective(operand))
    return [finished[index] for index in range(len(streams))]


def make_shards(n_dp, n_row, n_col):
    assert n_row == n_col
    transpose_pairs = [
        (a * n_col + b, b * n_col + a) for a in range(n_row) for b in range(n_col)
    ]

    def gather_half(mine, axis, axis_name):
        count = n_row if axis_name == "row" else n_col
        gathered = lax.all_gather(mine, axis_name, axis=axis)
        gathered = lax.all_gather(gathered, "dp", axis=axis)
        gathered = jnp.swapaxes(gathered, axis, axis + 1)
        shape = list(mine.shape)
        shape[axis] = mine.shape[axis] * count * n_dp
        return gathered.reshape(shape)

    def own_half(block, axis):
        half = block.shape[axis] // n_dp
        return lax.dynamic_slice_in_dim(block, lax.axis_index("dp") * half, half, axis=axis)

    def gather_features(block, axis, axis_name):
        return gather_half(own_half(block, axis), axis, axis_name)

    def reduce_half(partial, axis, axis_name):
        count = n_row if axis_name == "row" else n_col
        half = partial.shape[axis] // (count * n_dp)
        shape = list(partial.shape)
        shape[axis : axis + 1] = [count, n_dp, half]
        split = jnp.swapaxes(partial.reshape(shape), axis, axis + 1)
        split = lax.psum_scatter(split, "dp", scatter_dimension=axis)
        return lax.psum_scatter(
            split.astype(jnp.bfloat16), axis_name, scatter_dimension=axis
        ).astype(jnp.float32)

    def reduce_half_exchange(partial, axis_name):
        count = n_row if axis_name == "row" else n_col
        half = partial.shape[0] // (count * n_dp)
        split = jnp.swapaxes(partial.reshape((count, n_dp, half) + partial.shape[1:]), 0, 1)
        split = lax.psum_scatter(split, "dp", scatter_dimension=0)
        blocks = lax.all_to_all(split.astype(jnp.bfloat16), axis_name, 0, 0)
        return jnp.sum(blocks.astype(jnp.float32), axis=0)

    def reduce_features(partial, axis, axis_name):
        return lax.all_gather(reduce_half(partial, axis, axis_name), "dp", axis=axis, tiled=True)

    def transpose_grid(block):
        return lax.ppermute(block, ("row", "col"), transpose_pairs)

    def gather_tokens(rows):
        return lax.all_gather(rows, "row", axis=1, tiled=True)

    def scatter_tokens(rows):
        return lax.psum_scatter(rows, "row", scatter_dimension=1, tiled=True)

    def gather_seqs(rows):
        return lax.all_gather(rows, "col", axis=0, tiled=True)

    def scatter_seqs(rows):
        return lax.psum_scatter(rows, "col", scatter_dimension=0, tiled=True)

    def to_tokens(rows):
        batches, local, seq_len, width = rows.shape
        rows = rows.reshape(batches, local, n_row, seq_len // n_row, width)
        rows = lax.all_to_all(rows, "row", 2, 3)
        return rows.reshape(batches, local, seq_len // n_row, n_row * width)

    def to_features(rows):
        batches, local, chunk, width = rows.shape
        rows = rows.reshape(batches, local, chunk, n_row, width // n_row)
        rows = lax.all_to_all(rows, "row", 3, 2)
        return rows.reshape(batches, local, n_row * chunk, width // n_row)

    def shards(
        hidden_in,
        segment_ids,
        w_query,
        w_key,
        w_value,
        w_out,
        w_gate,
        w_up,
        w_down,
        gain_attn,
        gain_ffn,
        cotangent,
    ):
        batches, local, seq_len, width_r = hidden_in.shape
        chunk = seq_len // n_row
        row_index = lax.axis_index("row")
        col_index = lax.axis_index("col")
        query_cols = w_query.shape[1]
        key_cols = w_key.shape[1]
        key_end = query_cols + key_cols
        qkv_cols = key_end + w_value.shape[1]
        heads_q = query_cols // HD
        heads_k = key_cols // HD
        group_count = heads_q // heads_k
        ffn_cols = w_gate.shape[1]

        w_attn = gather_half(
            transpose_grid(own_half(jnp.concatenate([w_query, w_key, w_value, w_out.T], axis=1), 0)),
            0,
            "col",
        )
        w_qkv = w_attn[:, :qkv_cols]
        w_out_heads = w_attn[:, qkv_cols:].T
        w_pair = gather_features(jnp.concatenate([w_gate, w_up], axis=1), 0, "row")
        w_down_all = gather_features(w_down, 1, "row")
        gain_attn_all, gain_ffn_all = lax.all_gather(
            jnp.stack([gain_attn, gain_ffn]), "row", axis=1, tiled=True
        )

        segments = lax.all_gather(segment_ids, "row", axis=1, tiled=True)
        segments = lax.dynamic_slice_in_dim(segments, col_index * local, local, axis=1)
        places = positions(segments)
        token_place = jnp.broadcast_to(jnp.arange(seq_len), (local, seq_len))

        hidden_t, cotangent_t = to_tokens(jnp.concatenate([hidden_in, cotangent], axis=1)).reshape(
            (batches, 2, local, chunk, width_r * n_row)
        ).transpose(1, 0, 2, 3, 4)

        def micro_batch(batch_index):
            rows_f = hidden_t[batch_index].astype(jnp.float32)
            inv_attn = lax.rsqrt(jnp.mean(rows_f * rows_f, axis=-1, keepdims=True) + EPSILON)
            norm_attn = rows_f * inv_attn
            normed_attn = (norm_attn * gain_attn_all).astype(jnp.bfloat16)
            spread_attn = yield (gather_tokens, normed_attn)
            qkv = jnp.einsum(
                "std,dm->stm", spread_attn, w_qkv, preferred_element_type=jnp.float32
            )
            cosine, sine_part = rotary(places[batch_index])
            query_rot = rotate(
                qkv[..., :query_cols].reshape(local, seq_len, heads_q, HD), cosine, sine_part
            ).astype(jnp.bfloat16)
            key_all = rotate(
                qkv[..., query_cols:key_end].reshape(local, seq_len, heads_k, HD),
                cosine,
                sine_part,
            ).astype(jnp.bfloat16)
            value_all = (
                qkv[..., key_end:].reshape(local, seq_len, heads_k, HD).astype(jnp.bfloat16)
            )
            query_grouped = query_rot.reshape(local, seq_len, heads_k, group_count, HD)
            mixed, log_total = lax.map(
                attend_forward,
                (
                    query_grouped,
                    key_all,
                    value_all,
                    segments[batch_index],
                    segments[batch_index],
                    token_place,
                ),
            )
            attn_part = jnp.einsum(
                "stm,md->std", mixed, w_out_heads, preferred_element_type=jnp.float32
            )
            attn_branch = yield (scatter_tokens, attn_part.astype(jnp.bfloat16))
            attn_branch = attn_branch.astype(jnp.float32)
            resid_mid = rows_f + RESIDUAL_SCALE * attn_branch
            inv_ffn = lax.rsqrt(jnp.mean(resid_mid * resid_mid, axis=-1, keepdims=True) + EPSILON)
            norm_ffn = resid_mid * inv_ffn
            normed_ffn = (norm_ffn * gain_ffn_all).astype(jnp.bfloat16)
            spread_ffn = yield (gather_seqs, normed_ffn)
            pair = jnp.einsum(
                "std,df->stf", spread_ffn, w_pair, preferred_element_type=jnp.float32
            )
            gate_rows = pair[..., :ffn_cols]
            up_rows = pair[..., ffn_cols:]
            sigmoid_gate = jax.nn.sigmoid(gate_rows)
            act_low = (gate_rows * sigmoid_gate * up_rows).astype(jnp.bfloat16)
            ffn_part = jnp.einsum(
                "stf,fd->std", act_low, w_down_all, preferred_element_type=jnp.float32
            )
            ffn_branch = yield (scatter_seqs, ffn_part.astype(jnp.bfloat16))
            ffn_branch = ffn_branch.astype(jnp.float32)
            block_out = (resid_mid + RESIDUAL_SCALE * ffn_branch).astype(jnp.bfloat16)
            block_features = to_features(block_out[None])

            grad_rows = cotangent_t[batch_index].astype(jnp.float32)
            grad_ffn = (RESIDUAL_SCALE * grad_rows).astype(jnp.bfloat16)
            spread_grad_ffn = yield (gather_seqs, grad_ffn)
            fresh_down = jnp.einsum(
                "stf,std->fd", act_low, spread_grad_ffn, preferred_element_type=jnp.float32
            )
            grad_act = jnp.einsum(
                "std,fd->stf", spread_grad_ffn, w_down_all, preferred_element_type=jnp.float32
            )
            grad_gate_rows = (
                grad_act * up_rows * sigmoid_gate * (1.0 + gate_rows * (1.0 - sigmoid_gate))
            )
            grad_up_rows = grad_act * gate_rows * sigmoid_gate
            paired_gradient = jnp.concatenate([grad_gate_rows, grad_up_rows], axis=-1).astype(
                jnp.bfloat16
            )
            fresh_pair = jnp.einsum(
                "std,stf->df", spread_ffn, paired_gradient, preferred_element_type=jnp.float32
            )
            grad_normed_part = jnp.einsum(
                "stf,df->std", paired_gradient, w_pair, preferred_element_type=jnp.float32
            )
            block_features, scatter_operand = lax.optimization_barrier(
                (block_features, grad_normed_part.astype(jnp.bfloat16))
            )
            grad_normed_ffn = yield (scatter_seqs, scatter_operand)
            grad_normed_ffn = grad_normed_ffn.astype(jnp.float32)
            scaled_ffn = grad_normed_ffn * gain_ffn_all
            gain_ffn_part = jnp.sum(grad_normed_ffn * norm_ffn, axis=(0, 1))
            inner_ffn = jnp.mean(scaled_ffn * norm_ffn, axis=-1, keepdims=True)
            grad_mid = grad_rows + inv_ffn * (scaled_ffn - norm_ffn * inner_ffn)
            grad_attn = (RESIDUAL_SCALE * grad_mid).astype(jnp.bfloat16)
            spread_grad_attn = yield (gather_tokens, grad_attn)
            fresh_out = jnp.einsum(
                "std,stm->dm", spread_grad_attn, mixed, preferred_element_type=jnp.float32
            )
            grad_mixed = jnp.einsum(
                "std,md->stm", spread_grad_attn, w_out_heads, preferred_element_type=jnp.float32
            ).astype(jnp.bfloat16)
            grad_query_rot, grad_kv = lax.map(
                attend_backward,
                (
                    grad_mixed,
                    query_grouped,
                    key_all,
                    value_all,
                    log_total,
                    segments[batch_index],
                    segments[batch_index],
                    token_place,
                ),
            )
            grad_query = rotate(
                grad_query_rot.reshape(local, seq_len, heads_q, HD), cosine, -sine_part
            )
            grad_key = rotate(grad_kv[..., :HD], cosine, -sine_part)
            grad_qkv = jnp.concatenate(
                [
                    grad_query.reshape(local, seq_len, -1),
                    grad_key.reshape(local, seq_len, -1),
                    grad_kv[..., HD:].reshape(local, seq_len, -1),
                ],
                axis=-1,
            ).astype(jnp.bfloat16)
            fresh_qkv = jnp.einsum(
                "std,stm->dm", spread_attn, grad_qkv, preferred_element_type=jnp.float32
            )
            grad_normed_attn_part = jnp.einsum(
                "stm,dm->std", grad_qkv, w_qkv, preferred_element_type=jnp.float32
            )
            grad_normed_attn = yield (
                scatter_tokens, grad_normed_attn_part.astype(jnp.bfloat16)
            )
            grad_normed_attn = grad_normed_attn.astype(jnp.float32)
            scaled_attn = grad_normed_attn * gain_attn_all
            gain_attn_part = jnp.sum(grad_normed_attn * norm_attn, axis=(0, 1))
            inner_attn = jnp.mean(scaled_attn * norm_attn, axis=-1, keepdims=True)
            input_features = to_features(
                (grad_mid + inv_attn * (scaled_attn - norm_attn * inner_attn))[None]
            )
            fresh_attn = jnp.concatenate([fresh_qkv, fresh_out], axis=1)
            return (
                block_features,
                input_features,
                fresh_attn,
                fresh_pair,
                fresh_down,
                gain_attn_part,
                gain_ffn_part,
            )

        results = run_interleaved([micro_batch(b) for b in range(batches)])
        sums = [sum(parts[1:], parts[0]) for parts in zip(*[r[2:] for r in results])]
        grad_attn_w, grad_pair_w, grad_down_w, gain_attn_total, gain_ffn_total = sums
        outs_list = [r[0] for r in results]
        inputs_grad = [r[1] for r in results]

        total_pair = reduce_features(grad_pair_w, 0, "row")
        total_down = lax.all_gather(
            reduce_half_exchange(grad_down_w.T, "row"), "dp", axis=0, tiled=True
        ).T
        gain_rows = lax.psum(jnp.stack([gain_attn_total, gain_ffn_total], axis=1), "row")
        gain_cols = jnp.pad(gain_rows, ((0, 0), (0, 126)))
        attn_grads = jnp.concatenate([grad_attn_w, gain_cols], axis=1)
        early_inputs, attn_grads = lax.optimization_barrier((inputs_grad[:-1], attn_grads))
        inputs_grad = list(early_inputs) + inputs_grad[-1:]
        total_attn = lax.all_gather(
            transpose_grid(reduce_half_exchange(attn_grads, "col")),
            "dp",
            axis=0,
            tiled=True,
        )
        attn_cols = qkv_cols + w_out.shape[0]
        return (
            jnp.concatenate(outs_list),
            jnp.concatenate(inputs_grad),
            total_attn[:, :query_cols],
            total_attn[:, query_cols:key_end],
            total_attn[:, key_end:qkv_cols],
            total_attn[:, qkv_cols:attn_cols].T,
            total_pair[:, :ffn_cols],
            total_pair[:, ffn_cols:],
            total_down,
            total_attn[:, attn_cols],
            total_attn[:, attn_cols + 1],
        )

    return shards


def solution(mesh):
    activation = P(None, ("dp", "col"), None, "row")
    return jax.shard_map(
        make_shards(mesh.shape["dp"], mesh.shape["row"], mesh.shape["col"]),
        mesh=mesh,
        in_specs=(
            activation,
            P(None, ("dp", "row"), None),
            P("row", "col"),
            P("row", "col"),
            P("row", "col"),
            P("col", "row"),
            P("row", "col"),
            P("row", "col"),
            P("col", "row"),
            P("row"),
            P("row"),
            activation,
        ),
        out_specs=(
            activation,
            activation,
            P("row", "col"),
            P("row", "col"),
            P("row", "col"),
            P("col", "row"),
            P("row", "col"),
            P("row", "col"),
            P("col", "row"),
            P("row"),
            P("row"),
        ),
        check_vma=False,
    )
```
